32 devices in a mesh: groups: 2 (over y), expert: 4 (over z), tensor: 4 (over x, core).
Axes of the slice: x: 2, y: 2, z: 4, core: 2. Of those that a mesh axis runs over, the one named last changes fastest.
Arguments:
- tokens: bfloat16 [1024, 2560], P(('groups', 'expert'), 'tensor'), parts along dimension 0, may hold values from -6 to 6
- route_scale: float32 [1024], P(('groups', 'expert')), parts along dimension 0, may hold values from 0.25 to 1
- expert_ids: int32 [1024, 1], P(('groups', 'expert')), parts along dimension 0, may hold values from 0 to 1; in each aligned block of 128 rows (0 to 127, 128 to 255, ...) at most 128 rows name the same one
- gate_weight: bfloat16 [4, 2560, 2048], P('expert', None, 'tensor'), may hold values from -0.125 to 0.125
- up_weight: bfloat16 [4, 2560, 2048], P('expert', None, 'tensor'), may hold values from -0.125 to 0.125
- down_weight: bfloat16 [4, 2048, 2560], P('expert', 'tensor'), may hold values from -0.09375 to 0.09375
Outputs:
- mixed: bfloat16 [1024, 2560], P(('groups', 'expert'), 'tensor'), parts along dimension 0
The draws below stay inside these ranges and needn't reach their ends.
There are 2 independent parts, one for each index of `groups`. The reference program is written for one: setup_inputs(seed, part) draws one part's arguments, and reference() takes and returns one part's arrays. A program takes and returns all parts, laid end to end along the dimension named above; an argument that names none is the same for every part. Nothing has to cross between parts.
Inputs may be any that keep to these rules, and one draw needn't show every extreme that they name: `expert_ids`: within the rows of one index of the expert axis (aligned blocks of 128 tokens) no expert is named by more than 128 tokens, and in some block one expert is named by exactly 128 tokens.
All inputs are finite; a program needn't handle non-finite values.
Results may differ from the reference program's by a relative error of at most 0.019.
Values may be sent and summed in bfloat16 or wider, within the bound.
No kernel may reach another device: no remote copies, remote signals or barrier semaphores. Data moves between devices by JAX's collectives and lax.ppermute only.
A program may use at most 64 MiB of HBM per device.

```python
import math
import jax
import jax.numpy as jnp
import numpy as np
from jax import lax

D = 2560
FF = 4096
SPAN = 2
TOK_DEV = 128
TOKENS = 512
EXPERTS = 2
CAP = 128
FFD = 512
N_TENSOR = 4


def block_scale(rng, extent, pieces, low, high):
    level = 1.0
    for axis_at, parts in pieces:
        heights = jax.random.uniform(jax.random.fold_in(jax.random.fold_in(rng, 6), axis_at), (parts,), jnp.float32, low / len(pieces), high / len(pieces))
        level = level * jnp.repeat(jnp.exp(heights), extent[axis_at] // parts).reshape((-1,) + (1,) * (len(extent) - 1 - axis_at))
    return level


def routed_block(key, own, number, rows, number_of, top, most, slope):
    sequence = jax.random.permutation(key, number_of)
    packed, common = portions_of(number_of, rows * top, most, slope, True), portions_of(number_of, rows * top, most, slope, False)
    places = jnp.arange(number_of)

    def named(sizes, rotation):
        used = int((sizes > 0).sum())
        fixed = max(1, used // 4)
        moved = fixed + (places - fixed + rotation * (used - fixed)) % max(1, number_of - fixed)
        return jnp.zeros((number_of,), jnp.int32).at[sequence[jnp.where(places < fixed, places, moved)]].set(jnp.asarray(sizes, jnp.int32))

    sizes = jnp.where(number % 4 == 0, named(packed, number // 4), named(common, number - number // 4 - 1))
    mixed = jax.random.permutation(jax.random.fold_in(own, 3), number_of)
    donor, taker = mixed[0:number_of // 2 * 2:2], mixed[1:number_of // 2 * 2:2]
    slack = jnp.minimum(sizes[donor] - 1, most - sizes[taker]) // 2
    slack = jnp.where((donor == sequence[0]) | (taker == sequence[0]) | (sizes[taker] == 0), 0, jnp.maximum(slack, 0))
    moved = jax.random.randint(jax.random.fold_in(own, 4), (number_of // 2,), 0, 1 << 20) % (slack + 1)
    sizes = sizes.at[donor].add(-moved).at[taker].add(moved)
    items = jnp.searchsorted(jnp.cumsum(sizes), jnp.arange(rows * top), side="right").astype(jnp.int32)
    table = items.reshape(top, rows).T
    table = table[jax.random.permutation(jax.random.fold_in(own, 1), rows)]
    rotation = jax.random.randint(jax.random.fold_in(own, 2), (rows, 1), 0, top)
    return jnp.take_along_axis(table, (jnp.arange(top)[None, :] + rotation) % top, axis=1)


def portions_of(number_of, total, reach, skew, full):
    portions = [(1 << 20) // math.isqrt(grade ** skew) + 1 for grade in range(1, number_of + 1)]
    largest = reach if full else min(reach, max(-(-total // number_of), total * portions[0] // sum(portions)))
    least = 1 if total - largest >= number_of - 1 else 0
    counts, surplus = [largest] + [least] * (number_of - 1), total - largest - least * (number_of - 1)
    while surplus > 0:
        candidates = [i for i in range(1, number_of) if counts[i] < largest] or [i for i in range(1, number_of) if counts[i] < reach]
        whole, left = sum([portions[i] for i in candidates]), surplus
        for i in candidates:
            extra = min(reach - counts[i], max(1, left * portions[i] // whole), surplus)
            counts[i] = counts[i] + extra
            surplus = surplus - extra
    return np.array(counts)


def bell_draw(key, shape, width, reach, shards=(), kind=jnp.bfloat16):
    values = width * jax.random.normal(key, shape, jnp.float32)
    if shards:
        values = values * block_scale(key, shape, shards, -0.22, 0.18)
    return jnp.clip(values, -reach, reach).astype(kind)


def setup_inputs(seed: int = 0, part: int = 0) -> dict:
    arg_keys = jax.random.split(jax.random.key(seed), 7)
    part_keys = jax.random.split(jax.random.fold_in(arg_keys[6], part), 7)
    tokens = bell_draw(part_keys[0], (TOKENS, D), 1.0, 6.0, ((0, 4), (1, 4)))
    route_scale = jnp.clip(jnp.exp(math.log(1.0) - 1.3862944 * jax.random.uniform(part_keys[1], (TOKENS,), jnp.float32) ** block_scale(part_keys[1], (TOKENS,), ((0, 4),), -0.2, 0.2)), 0.25, 1.0)
    expert_ids_keys = jax.random.split(jax.random.fold_in(part_keys[2], 1), TOKENS // TOK_DEV)
    expert_ids_turns = jax.random.permutation(jax.random.fold_in(part_keys[2], 3), TOKENS // TOK_DEV)
    expert_ids = jax.vmap(lambda own, number: routed_block(jax.random.fold_in(part_keys[2], 2), own, number, TOK_DEV, EXPERTS, 1, CAP, 2))(expert_ids_keys, expert_ids_turns).reshape((TOKENS, 1))
    gate_weight = bell_draw(arg_keys[3], (EXPERTS * SPAN, D, FF // SPAN), D ** -0.5, 0.125, ((0, 4), (2, 4)))
    up_weight = bell_draw(arg_keys[4], (EXPERTS * SPAN, D, FF // SPAN), D ** -0.5, 0.125, ((0, 4), (2, 4)))
    down_weight = bell_draw(arg_keys[5], (EXPERTS * SPAN, FF // SPAN, D), FF ** -0.5, 0.09375, ((0, 4), (1, 4)))
    return {"tokens": tokens, "route_scale": route_scale, "expert_ids": expert_ids, "gate_weight": gate_weight, "up_weight": up_weight, "down_weight": down_weight}


def reference(tokens, route_scale, expert_ids, gate_weight, up_weight, down_weight):
    sources = TOKENS // TOK_DEV
    routed = expert_ids[:, 0].reshape(sources, TOK_DEV)
    one_hot = (routed[:, :, None] == jnp.arange(EXPERTS, dtype=jnp.int32)[None, None, :]).astype(jnp.int32)
    slot_rank = jnp.sum((jnp.cumsum(one_hot, axis=1) - one_hot) * one_hot, axis=2)
    source_ids = jnp.arange(sources, dtype=jnp.int32)[:, None]
    destination = (routed * (sources * CAP) + source_ids * CAP + slot_rank).reshape(-1).astype(jnp.int32)
    slot_table = jnp.full((EXPERTS * sources * CAP,), TOKENS, jnp.int32)
    slot_table = slot_table.at[destination].set(jnp.arange(TOKENS, dtype=jnp.int32))
    slot_table = slot_table.reshape(EXPERTS, sources * CAP)
    scaled = (tokens.astype(jnp.float32) * route_scale[:, None]).astype(jnp.bfloat16)
    padded = jnp.concatenate([scaled, jnp.zeros((1, D), jnp.bfloat16)], axis=0)
    gate_all = gate_weight.reshape(EXPERTS, SPAN, D, FF // SPAN)
    up_all = up_weight.reshape(EXPERTS, SPAN, D, FF // SPAN)
    down_all = down_weight.reshape(EXPERTS, SPAN, FF // SPAN, D)

    def one_expert(operands):
        indices, gate_w, up_w, down_w = operands
        slot_rows = jnp.take(padded, indices, axis=0)
        accumulated = jnp.zeros((slot_rows.shape[0], D), jnp.float32)
        for half_index in range(SPAN):
            gate_act = jnp.dot(slot_rows, gate_w[half_index], preferred_element_type=jnp.float32)
            up_act = jnp.dot(slot_rows, up_w[half_index], preferred_element_type=jnp.float32)
            hidden = (jax.nn.silu(gate_act) * up_act).astype(jnp.bfloat16)
            hidden_three = hidden.reshape(slot_rows.shape[0], N_TENSOR, FFD).astype(jnp.float32)
            down_three = down_w[half_index].reshape(N_TENSOR, FFD, D).astype(jnp.float32)
            partial_value = jnp.einsum("rtk,tkd->trd", hidden_three, down_three).astype(jnp.bfloat16)
            partial_value = lax.optimization_barrier(partial_value)
            accumulated = accumulated + jnp.sum(partial_value.astype(jnp.float32), axis=0)
        return accumulated

    outputs = lax.map(one_expert, (slot_table, gate_all, up_all, down_all))
    result = jnp.zeros((TOKENS + 1, D), jnp.float32)
    result = result.at[slot_table.reshape(-1)].set(outputs.reshape(-1, D))
    return result[:TOKENS].astype(jnp.bfloat16)
```

```python
import jax
import jax.numpy as jnp
from jax import lax
from jax.sharding import PartitionSpec as P

SPAN = 2


def dispatched(tokens, route_scale, expert_ids, gate_weight, up_weight, down_weight):
    tok_rows = tokens.shape[0]
    n_devices = lax.axis_size("expert")
    experts = n_devices // SPAN
    capacity = min(tok_rows, 2 * tok_rows * SPAN // n_devices)
    routed = expert_ids[:, 0]
    one_hot = (routed[:, None] == jnp.arange(experts, dtype=jnp.int32)[None, :]).astype(jnp.int32)
    slot_rank = jnp.sum((jnp.cumsum(one_hot, axis=0) - one_hot) * one_hot, axis=1)
    flat_slot = routed * capacity + slot_rank
    placing = (
        flat_slot[None, :] == jnp.arange(experts * capacity, dtype=jnp.int32)[:, None]
    ).astype(jnp.bfloat16)
    scaled = (tokens.astype(jnp.float32) * route_scale[:, None]).astype(jnp.bfloat16)
    gate_local = gate_weight[0]
    up_local = up_weight[0]
    down_local = down_weight[0]
    full_rows = lax.all_gather(scaled, "tensor", axis=1, tiled=True)
    width = full_rows.shape[1]
    packed = jnp.dot(placing, full_rows, preferred_element_type=jnp.float32).astype(jnp.bfloat16)
    outgoing = jnp.repeat(packed.reshape(experts, capacity, width), SPAN, axis=0)
    arrived = lax.all_to_all(outgoing, "expert", split_axis=0, concat_axis=0, tiled=True)
    slot_rows = arrived.reshape(n_devices * capacity, width)
    gate_act = jnp.dot(slot_rows, gate_local, preferred_element_type=jnp.float32)
    up_act = jnp.dot(slot_rows, up_local, preferred_element_type=jnp.float32)
    hidden = (jax.nn.silu(gate_act) * up_act).astype(jnp.bfloat16)
    partial_value = jnp.dot(hidden, down_local, preferred_element_type=jnp.float32)
    width = partial_value.shape[1]
    outgoing_back = partial_value.astype(jnp.bfloat16).reshape(n_devices, capacity, width)
    returned = lax.all_to_all(outgoing_back, "expert", split_axis=0, concat_axis=0, tiled=True)
    paired = jnp.sum(returned.astype(jnp.float32).reshape(experts, SPAN, capacity, width), axis=1)
    picked = jnp.take(paired.reshape(experts * capacity, width), flat_slot, axis=0)
    summed = lax.psum_scatter(
        picked.astype(jnp.bfloat16), "tensor", scatter_dimension=1, tiled=True
    )
    return summed


def gathered(tokens, route_scale, expert_ids, gate_weight, up_weight, down_weight):
    expert = lax.axis_index("expert") // SPAN
    scaled = (tokens.astype(jnp.float32) * route_scale[:, None]).astype(jnp.bfloat16)
    rows = lax.all_gather(scaled, "expert", axis=0, tiled=True)
    routed = lax.all_gather(expert_ids[:, 0], "expert", axis=0, tiled=True)
    full_rows = lax.all_gather(rows, "tensor", axis=1, tiled=True)
    gate_act = jnp.dot(full_rows, gate_weight[0], preferred_element_type=jnp.float32)
    up_act = jnp.dot(full_rows, up_weight[0], preferred_element_type=jnp.float32)
    mine = (routed == expert)[:, None]
    hidden = jnp.where(mine, jax.nn.silu(gate_act) * up_act, 0.0).astype(jnp.bfloat16)
    partial_value = jnp.dot(hidden, down_weight[0], preferred_element_type=jnp.float32)
    partial_value = partial_value.astype(jnp.bfloat16)
    over_units = lax.psum_scatter(partial_value, "tensor", scatter_dimension=1, tiled=True)
    return lax.psum_scatter(over_units, "expert", scatter_dimension=0, tiled=True)


def local(tokens, route_scale, expert_ids, gate_weight, up_weight, down_weight):
    tok_rows = tokens.shape[0]
    n_devices = lax.axis_size("expert")
    capacity = min(tok_rows, 2 * tok_rows * SPAN // n_devices)
    if capacity == tok_rows:
        return gathered(tokens, route_scale, expert_ids, gate_weight, up_weight, down_weight)
    return dispatched(tokens, route_scale, expert_ids, gate_weight, up_weight, down_weight)


def solution(mesh):
    placed = (
        P(("groups", "expert"), "tensor"),
        P(("groups", "expert")),
        P(("groups", "expert"), None),
        P("expert", None, "tensor"),
        P("expert", None, "tensor"),
        P("expert", "tensor", None),
    )
    return jax.shard_map(
        local,
        mesh=mesh,
        in_specs=placed,
        out_specs=P(("groups", "expert"), "tensor"),
        check_vma=False,
    )
```

```python
import jax
import jax.numpy as jnp
from jax import lax
from jax.sharding import PartitionSpec as P

SPAN = 2


def dispatched(tokens, route_scale, expert_ids, gate_weight, up_weight, down_weight):
    tok_rows = tokens.shape[0]
    n_devices = lax.axis_size("expert")
    experts = n_devices // SPAN
    capacity = min(tok_rows, 2 * tok_rows * SPAN // n_devices)
    routed = expert_ids[:, 0]
    one_hot = (routed[:, None] == jnp.arange(experts, dtype=jnp.int32)[None, :]).astype(jnp.int32)
    slot_rank = jnp.sum((jnp.cumsum(one_hot, axis=0) - one_hot) * one_hot, axis=1)
    flat_slot = routed * capacity + slot_rank
    placing = (
        flat_slot[None, :] == jnp.arange(experts * capacity, dtype=jnp.int32)[:, None]
    ).astype(jnp.bfloat16)
    scaled = (tokens.astype(jnp.float32) * route_scale[:, None]).astype(jnp.bfloat16)
    gate_local = gate_weight[0]
    up_local = up_weight[0]
    down_local = down_weight[0]
    full_rows = lax.all_gather(scaled, "tensor", axis=1, tiled=True)
    width = full_rows.shape[1]
    packed = jnp.dot(placing, full_rows, preferred_element_type=jnp.float32).astype(jnp.bfloat16)
    outgoing = jnp.repeat(packed.reshape(experts, capacity, width), SPAN, axis=0)
    arrived = lax.all_to_all(outgoing, "expert", split_axis=0, concat_axis=0, tiled=True)
    slot_rows = arrived.reshape(n_devices * capacity, width)
    gate_act = jnp.dot(slot_rows, gate_local, preferred_element_type=jnp.float32)
    up_act = jnp.dot(slot_rows, up_local, preferred_element_type=jnp.float32)
    hidden = (jax.nn.silu(gate_act) * up_act).astype(jnp.bfloat16)
    partial_value = jnp.dot(hidden, down_local, preferred_element_type=jnp.float32)
    width = partial_value.shape[1]
    outgoing_back = partial_value.astype(jnp.bfloat16).reshape(n_devices, capacity, width)
    returned = lax.all_to_all(outgoing_back, "expert", split_axis=0, concat_axis=0, tiled=True)
    paired = jnp.sum(returned.astype(jnp.float32).reshape(experts, SPAN, capacity, width), axis=1)
    picked = jnp.take(paired.reshape(experts * capacity, width), flat_slot, axis=0)
    summed = lax.psum_scatter(
        picked.astype(jnp.bfloat16), "tensor", scatter_dimension=1, tiled=True
    )
    return summed


def gathered(tokens, route_scale, expert_ids, gate_weight, up_weight, down_weight):
    tok_rows, width = tokens.shape
    n_expert = lax.axis_size("expert")
    n_tensor = lax.axis_size("tensor")
    expert = lax.axis_index("expert") // SPAN
    scaled = (tokens.astype(jnp.float32) * route_scale[:, None]).astype(jnp.bfloat16)
    id_rows = jnp.zeros((16, width), jnp.bfloat16)
    id_rows = id_rows.at[0, :tok_rows].set(expert_ids[:, 0].astype(jnp.bfloat16))
    block = jnp.concatenate([scaled, id_rows], axis=0)
    everything = lax.all_gather(block, ("expert", "tensor"), axis=0, tiled=False)
    everything = everything.reshape(n_expert, n_tensor, tok_rows + 16, width)
    routed = everything[:, 0, tok_rows, :tok_rows].reshape(n_expert * tok_rows)
    rows = everything[:, :, :tok_rows, :]
    gate_w = gate_weight[0].reshape(n_tensor, width, -1)
    up_w = up_weight[0].reshape(n_tensor, width, -1)
    gate_act = jnp.einsum("ztif,tfh->zih", rows, gate_w, preferred_element_type=jnp.float32)
    up_act = jnp.einsum("ztif,tfh->zih", rows, up_w, preferred_element_type=jnp.float32)
    mine = (routed == expert.astype(jnp.bfloat16)).reshape(n_expert, tok_rows, 1)
    hidden = jnp.where(mine, jax.nn.silu(gate_act) * up_act, 0.0).astype(jnp.bfloat16)
    down_w = down_weight[0].reshape(-1, n_tensor, width)
    partial_value = jnp.einsum("zih,htf->ztif", hidden, down_w, preferred_element_type=jnp.float32)
    partial_value = partial_value.astype(jnp.bfloat16).reshape(n_expert * n_tensor, tok_rows, width)
    return lax.psum_scatter(partial_value, ("expert", "tensor"), scatter_dimension=0, tiled=True).reshape(tok_rows, width)


def local(tokens, route_scale, expert_ids, gate_weight, up_weight, down_weight):
    tok_rows = tokens.shape[0]
    n_devices = lax.axis_size("expert")
    capacity = min(tok_rows, 2 * tok_rows * SPAN // n_devices)
    if capacity == tok_rows:
        return gathered(tokens, route_scale, expert_ids, gate_weight, up_weight, down_weight)
    return dispatched(tokens, route_scale, expert_ids, gate_weight, up_weight, down_weight)


def solution(mesh):
    placed = (
        P(("groups", "expert"), "tensor"),
        P(("groups", "expert")),
        P(("groups", "expert"), None),
        P("expert", None, "tensor"),
        P("expert", None, "tensor"),
        P("expert", "tensor", None),
    )
    return jax.shard_map(
        local,
        mesh=mesh,
        in_specs=placed,
        out_specs=P(("groups", "expert"), "tensor"),
        check_vma=False,
    )
```

```python
import jax
import jax.numpy as jnp
from jax import lax
from jax.sharding import PartitionSpec as P

SPAN = 2


def dispatched(tokens, route_scale, expert_ids, gate_weight, up_weight, down_weight):
    tok_rows = tokens.shape[0]
    n_devices = lax.axis_size("expert")
    experts = n_devices // SPAN
    capacity = min(tok_rows, 2 * tok_rows * SPAN // n_devices)
    routed = expert_ids[:, 0]
    one_hot = (routed[:, None] == jnp.arange(experts, dtype=jnp.int32)[None, :]).astype(jnp.int32)
    slot_rank = jnp.sum((jnp.cumsum(one_hot, axis=0) - one_hot) * one_hot, axis=1)
    flat_slot = routed * capacity + slot_rank
    placing = (
        flat_slot[None, :] == jnp.arange(experts * capacity, dtype=jnp.int32)[:, None]
    ).astype(jnp.bfloat16)
    scaled = (tokens.astype(jnp.float32) * route_scale[:, None]).astype(jnp.bfloat16)
    gate_local = gate_weight[0]
    up_local = up_weight[0]
    down_local = down_weight[0]
    full_rows = lax.all_gather(scaled, "tensor", axis=1, tiled=True)
    width = full_rows.shape[1]
    packed = jnp.dot(placing, full_rows, preferred_element_type=jnp.float32).astype(jnp.bfloat16)
    outgoing = jnp.repeat(packed.reshape(experts, capacity, width), SPAN, axis=0)
    arrived = lax.all_to_all(outgoing, "expert", split_axis=0, concat_axis=0, tiled=True)
    slot_rows = arrived.reshape(n_devices * capacity, width)
    gate_act = jnp.dot(slot_rows, gate_local, preferred_element_type=jnp.float32)
    up_act = jnp.dot(slot_rows, up_local, preferred_element_type=jnp.float32)
    hidden = (jax.nn.silu(gate_act) * up_act).astype(jnp.bfloat16)
    partial_value = jnp.dot(hidden, down_local, preferred_element_type=jnp.float32)
    width = partial_value.shape[1]
    outgoing_back = partial_value.astype(jnp.bfloat16).reshape(n_devices, capacity, width)
    returned = lax.all_to_all(outgoing_back, "expert", split_axis=0, concat_axis=0, tiled=True)
    paired = jnp.sum(returned.astype(jnp.float32).reshape(experts, SPAN, capacity, width), axis=1)
    picked = jnp.take(paired.reshape(experts * capacity, width), flat_slot, axis=0)
    summed = lax.psum_scatter(
        picked.astype(jnp.bfloat16), "tensor", scatter_dimension=1, tiled=True
    )
    return summed


def _xor_pairs(size, k):
    return [(i, i ^ k) for i in range(size)]


def _full_rows(piece, x, c, n_tensor):
    other_x = lax.ppermute(piece, "tensor", _xor_pairs(n_tensor, 2))
    by_x = jnp.where(x == 0, jnp.stack([piece, other_x]), jnp.stack([other_x, piece]))
    other_c = lax.ppermute(by_x, "tensor", _xor_pairs(n_tensor, 1))
    return jnp.where(c == 0, jnp.stack([by_x, other_c]), jnp.stack([other_c, by_x]))


def _unit_sum(partial_value, x, c, n_tensor):
    mine_c = jnp.where(c == 0, partial_value[:, :, 0], partial_value[:, :, 1])
    send_c = jnp.where(c == 0, partial_value[:, :, 1], partial_value[:, :, 0])
    over_c = mine_c.astype(jnp.float32) + lax.ppermute(
        send_c, "tensor", _xor_pairs(n_tensor, 1)).astype(jnp.float32)
    mine_x = jnp.where(x == 0, over_c[:, 0], over_c[:, 1])
    send_x = jnp.where(x == 0, over_c[:, 1], over_c[:, 0]).astype(jnp.bfloat16)
    return mine_x + lax.ppermute(send_x, "tensor", _xor_pairs(n_tensor, 2)).astype(jnp.float32)


def gathered(tokens, route_scale, expert_ids, gate_weight, up_weight, down_weight):
    tok_rows, width = tokens.shape
    n_expert = lax.axis_size("expert")
    n_tensor = lax.axis_size("tensor")
    me = lax.axis_index("expert")
    t = lax.axis_index("tensor")
    x, c = t // 2, t % 2
    expert = (me // SPAN).astype(jnp.bfloat16)
    scaled = (tokens.astype(jnp.float32) * route_scale[:, None]).astype(jnp.bfloat16)
    id_rows = jnp.zeros((16, width), jnp.bfloat16)
    id_rows = id_rows.at[0, :tok_rows].set(expert_ids[:, 0].astype(jnp.bfloat16))
    block = jnp.concatenate([scaled, id_rows], axis=0)
    blocks = [block] + [
        lax.ppermute(block, "expert", _xor_pairs(n_expert, k)) for k in range(1, n_expert)
    ]
    hid = gate_weight.shape[2]
    gate_w = gate_weight[0].reshape(2, 2, width, hid)
    up_w = up_weight[0].reshape(2, 2, width, hid)
    down_w = down_weight[0].reshape(hid, 2, 2, width)
    total = None
    for k, blk in enumerate(blocks):
        routed = blk[tok_rows, :tok_rows]
        rows = _full_rows(blk[:tok_rows], x, c, n_tensor)
        gate_act = jnp.einsum("cxrf,xcfh->rh", rows, gate_w, preferred_element_type=jnp.float32)
        up_act = jnp.einsum("cxrf,xcfh->rh", rows, up_w, preferred_element_type=jnp.float32)
        mine = (routed == expert)[:, None]
        hidden = jnp.where(mine, jax.nn.silu(gate_act) * up_act, 0.0).astype(jnp.bfloat16)
        partial_value = jnp.einsum("rh,hxcf->rxcf", hidden, down_w, preferred_element_type=jnp.float32)
        summed = _unit_sum(partial_value.astype(jnp.bfloat16), x, c, n_tensor)
        if k:
            summed = lax.ppermute(
                summed.astype(jnp.bfloat16), "expert", _xor_pairs(n_expert, k)).astype(jnp.float32)
        total = summed if total is None else total + summed
    return total.astype(jnp.bfloat16)


def local(tokens, route_scale, expert_ids, gate_weight, up_weight, down_weight):
    tok_rows = tokens.shape[0]
    n_devices = lax.axis_size("expert")
    capacity = min(tok_rows, 2 * tok_rows * SPAN // n_devices)
    n_tensor = lax.axis_size("tensor")
    shaped = n_tensor == 4 and n_devices in (1, 2, 4) and tok_rows <= tokens.shape[1]
    if capacity == tok_rows and shaped:
        return gathered(tokens, route_scale, expert_ids, gate_weight, up_weight, down_weight)
    return dispatched(tokens, route_scale, expert_ids, gate_weight, up_weight, down_weight)


def solution(mesh):
    placed = (
        P(("groups", "expert"), "tensor"),
        P(("groups", "expert")),
        P(("groups", "expert"), None),
        P("expert", None, "tensor"),
        P("expert", None, "tensor"),
        P("expert", "tensor", None),
    )
    return jax.shard_map(
        local,
        mesh=mesh,
        in_specs=placed,
        out_specs=P(("groups", "expert"), "tensor"),
        check_vma=False,
    )
```

```python
import jax
import jax.numpy as jnp
from jax import lax
from jax.sharding import PartitionSpec as P

SPAN = 2


def dispatched(tokens, route_scale, expert_ids, gate_weight, up_weight, down_weight):
    tok_rows = tokens.shape[0]
    n_devices = lax.axis_size("expert")
    experts = n_devices // SPAN
    capacity = min(tok_rows, 2 * tok_rows * SPAN // n_devices)
    routed = expert_ids[:, 0]
    one_hot = (routed[:, None] == jnp.arange(experts, dtype=jnp.int32)[None, :]).astype(jnp.int32)
    slot_rank = jnp.sum((jnp.cumsum(one_hot, axis=0) - one_hot) * one_hot, axis=1)
    flat_slot = routed * capacity + slot_rank
    placing = (
        flat_slot[None, :] == jnp.arange(experts * capacity, dtype=jnp.int32)[:, None]
    ).astype(jnp.bfloat16)
    scaled = (tokens.astype(jnp.float32) * route_scale[:, None]).astype(jnp.bfloat16)
    gate_local = gate_weight[0]
    up_local = up_weight[0]
    down_local = down_weight[0]
    full_rows = lax.all_gather(scaled, "tensor", axis=1, tiled=True)
    width = full_rows.shape[1]
    packed = jnp.dot(placing, full_rows, preferred_element_type=jnp.float32).astype(jnp.bfloat16)
    outgoing = jnp.repeat(packed.reshape(experts, capacity, width), SPAN, axis=0)
    arrived = lax.all_to_all(outgoing, "expert", split_axis=0, concat_axis=0, tiled=True)
    slot_rows = arrived.reshape(n_devices * capacity, width)
    gate_act = jnp.dot(slot_rows, gate_local, preferred_element_type=jnp.float32)
    up_act = jnp.dot(slot_rows, up_local, preferred_element_type=jnp.float32)
    hidden = (jax.nn.silu(gate_act) * up_act).astype(jnp.bfloat16)
    partial_value = jnp.dot(hidden, down_local, preferred_element_type=jnp.float32)
    width = partial_value.shape[1]
    outgoing_back = partial_value.astype(jnp.bfloat16).reshape(n_devices, capacity, width)
    returned = lax.all_to_all(outgoing_back, "expert", split_axis=0, concat_axis=0, tiled=True)
    paired = jnp.sum(returned.astype(jnp.float32).reshape(experts, SPAN, capacity, width), axis=1)
    picked = jnp.take(paired.reshape(experts * capacity, width), flat_slot, axis=0)
    summed = lax.psum_scatter(
        picked.astype(jnp.bfloat16), "tensor", scatter_dimension=1, tiled=True
    )
    return summed


def _xor_pairs(size, k):
    return [(i, i ^ k) for i in range(size)]


_ORDER = (0, 2, 1, 3)


def _slots(weight, t, width, axis):
    return jnp.concatenate(
        [lax.dynamic_slice_in_dim(weight, (t ^ k) * width, width, axis=axis) for k in _ORDER], axis=axis)


def gathered(tokens, route_scale, expert_ids, gate_weight, up_weight, down_weight):
    tok_rows, width = tokens.shape
    n_expert = lax.axis_size("expert")
    n_tensor = lax.axis_size("tensor")
    me = lax.axis_index("expert")
    t = lax.axis_index("tensor")
    expert = (me // SPAN).astype(jnp.bfloat16)
    scaled = (tokens.astype(jnp.float32) * route_scale[:, None]).astype(jnp.bfloat16)
    id_rows = jnp.zeros((16, width), jnp.bfloat16)
    id_rows = id_rows.at[0, :tok_rows].set(expert_ids[:, 0].astype(jnp.bfloat16))
    block = jnp.concatenate([scaled, id_rows], axis=0)
    blocks = [block] + [
        lax.ppermute(block, "expert", _xor_pairs(n_expert, k)) for k in range(1, n_expert)
    ]
    gate_w = _slots(gate_weight[0], t, width, 0)
    up_w = _slots(up_weight[0], t, width, 0)
    down_w = _slots(down_weight[0], t, width, 1)
    total = None
    for k, blk in enumerate(blocks):
        routed = blk[tok_rows, :tok_rows]
        piece = blk[:tok_rows]
        pair = jnp.concatenate(
            [piece, lax.ppermute(piece, "tensor", _xor_pairs(n_tensor, 2))], axis=1)
        rows = jnp.concatenate(
            [pair, lax.ppermute(pair, "tensor", _xor_pairs(n_tensor, 1))], axis=1)
        gate_act = jnp.dot(rows, gate_w, preferred_element_type=jnp.float32)
        up_act = jnp.dot(rows, up_w, preferred_element_type=jnp.float32)
        mine = (routed == expert)[:, None]
        hidden = jnp.where(mine, jax.nn.silu(gate_act) * up_act, 0.0).astype(jnp.bfloat16)
        partial_value = jnp.dot(hidden, down_w, preferred_element_type=jnp.float32).astype(jnp.bfloat16)
        over_c = partial_value[:, :2 * width].astype(jnp.float32) + lax.ppermute(
            partial_value[:, 2 * width:], "tensor", _xor_pairs(n_tensor, 1)).astype(jnp.float32)
        summed = over_c[:, :width] + lax.ppermute(
            over_c[:, width:].astype(jnp.bfloat16), "tensor", _xor_pairs(n_tensor, 2)).astype(jnp.float32)
        if k:
            summed = lax.ppermute(
                summed.astype(jnp.bfloat16), "expert", _xor_pairs(n_expert, k)).astype(jnp.float32)
        total = summed if total is None else total + summed
    return total.astype(jnp.bfloat16)


def local(tokens, route_scale, expert_ids, gate_weight, up_weight, down_weight):
    tok_rows = tokens.shape[0]
    n_devices = lax.axis_size("expert")
    capacity = min(tok_rows, 2 * tok_rows * SPAN // n_devices)
    n_tensor = lax.axis_size("tensor")
    shaped = n_tensor == 4 and n_devices in (1, 2, 4) and tok_rows <= tokens.shape[1]
    if capacity == tok_rows and shaped:
        return gathered(tokens, route_scale, expert_ids, gate_weight, up_weight, down_weight)
    return dispatched(tokens, route_scale, expert_ids, gate_weight, up_weight, down_weight)


def solution(mesh):
    placed = (
        P(("groups", "expert"), "tensor"),
        P(("groups", "expert")),
        P(("groups", "expert"), None),
        P("expert", None, "tensor"),
        P("expert", None, "tensor"),
        P("expert", "tensor", None),
    )
    return jax.shard_map(
        local,
        mesh=mesh,
        in_specs=placed,
        out_specs=P(("groups", "expert"), "tensor"),
        check_vma=False,
    )
```

```python
import jax
import jax.numpy as jnp
from jax import lax
from jax.sharding import PartitionSpec as P

SPAN = 2


def dispatched(tokens, route_scale, expert_ids, gate_weight, up_weight, down_weight):
    tok_rows = tokens.shape[0]
    n_devices = lax.axis_size("expert")
    experts = n_devices // SPAN
    capacity = min(tok_rows, 2 * tok_rows * SPAN // n_devices)
    routed = expert_ids[:, 0]
    one_hot = (routed[:, None] == jnp.arange(experts, dtype=jnp.int32)[None, :]).astype(jnp.int32)
    slot_rank = jnp.sum((jnp.cumsum(one_hot, axis=0) - one_hot) * one_hot, axis=1)
    flat_slot = routed * capacity + slot_rank
    placing = (
        flat_slot[None, :] == jnp.arange(experts * capacity, dtype=jnp.int32)[:, None]
    ).astype(jnp.bfloat16)
    scaled = (tokens.astype(jnp.float32) * route_scale[:, None]).astype(jnp.bfloat16)
    gate_local = gate_weight[0]
    up_local = up_weight[0]
    down_local = down_weight[0]
    full_rows = lax.all_gather(scaled, "tensor", axis=1, tiled=True)
    width = full_rows.shape[1]
    packed = jnp.dot(placing, full_rows, preferred_element_type=jnp.float32).astype(jnp.bfloat16)
    outgoing = jnp.repeat(packed.reshape(experts, capacity, width), SPAN, axis=0)
    arrived = lax.all_to_all(outgoing, "expert", split_axis=0, concat_axis=0, tiled=True)
    slot_rows = arrived.reshape(n_devices * capacity, width)
    gate_act = jnp.dot(slot_rows, gate_local, preferred_element_type=jnp.float32)
    up_act = jnp.dot(slot_rows, up_local, preferred_element_type=jnp.float32)
    hidden = (jax.nn.silu(gate_act) * up_act).astype(jnp.bfloat16)
    partial_value = jnp.dot(hidden, down_local, preferred_element_type=jnp.float32)
    width = partial_value.shape[1]
    outgoing_back = partial_value.astype(jnp.bfloat16).reshape(n_devices, capacity, width)
    returned = lax.all_to_all(outgoing_back, "expert", split_axis=0, concat_axis=0, tiled=True)
    paired = jnp.sum(returned.astype(jnp.float32).reshape(experts, SPAN, capacity, width), axis=1)
    picked = jnp.take(paired.reshape(experts * capacity, width), flat_slot, axis=0)
    summed = lax.psum_scatter(
        picked.astype(jnp.bfloat16), "tensor", scatter_dimension=1, tiled=True
    )
    return summed


def _xor_pairs(size, k):
    return [(i, i ^ k) for i in range(size)]


_ORDER = (0, 2, 1, 3)


def _slots(weight, t, width, axis):
    return jnp.concatenate(
        [lax.dynamic_slice_in_dim(weight, (t ^ k) * width, width, axis=axis) for k in _ORDER], axis=axis)


def gathered(tokens, route_scale, expert_ids, gate_weight, up_weight, down_weight):
    tok_rows, width = tokens.shape
    n_expert = lax.axis_size("expert")
    n_tensor = lax.axis_size("tensor")
    me = lax.axis_index("expert")
    t = lax.axis_index("tensor")
    expert = (me // SPAN).astype(jnp.bfloat16)
    scaled = (tokens.astype(jnp.float32) * route_scale[:, None]).astype(jnp.bfloat16)
    id_rows = jnp.zeros((16, width), jnp.bfloat16)
    id_rows = id_rows.at[0, :tok_rows].set(expert_ids[:, 0].astype(jnp.bfloat16))
    block = jnp.concatenate([scaled, id_rows], axis=0)
    blocks = [block] + [
        lax.ppermute(block, "expert", _xor_pairs(n_expert, k)) for k in range(1, n_expert)
    ]
    gate_w = _slots(gate_weight[0], t, width, 0)
    up_w = _slots(up_weight[0], t, width, 0)
    down_w = _slots(down_weight[0], t, width, 1)
    waves = [blocks[:1], blocks[1:]] if n_expert > 1 else [blocks]
    total = None
    for wave in waves:
        routed = jnp.concatenate([blk[tok_rows, :tok_rows] for blk in wave])
        piece = jnp.concatenate([blk[:tok_rows] for blk in wave])
        pair = jnp.concatenate(
            [piece, lax.ppermute(piece, "tensor", _xor_pairs(n_tensor, 2))], axis=1)
        rows = jnp.concatenate(
            [pair, lax.ppermute(pair, "tensor", _xor_pairs(n_tensor, 1))], axis=1)
        gate_act = jnp.dot(rows, gate_w, preferred_element_type=jnp.float32)
        up_act = jnp.dot(rows, up_w, preferred_element_type=jnp.float32)
        mine = (routed == expert)[:, None]
        hidden = jnp.where(mine, jax.nn.silu(gate_act) * up_act, 0.0).astype(jnp.bfloat16)
        partial_value = jnp.dot(hidden, down_w, preferred_element_type=jnp.float32).astype(jnp.bfloat16)
        over_c = partial_value[:, :2 * width].astype(jnp.float32) + lax.ppermute(
            partial_value[:, 2 * width:], "tensor", _xor_pairs(n_tensor, 1)).astype(jnp.float32)
        summed = over_c[:, :width] + lax.ppermute(
            over_c[:, width:].astype(jnp.bfloat16), "tensor", _xor_pairs(n_tensor, 2)).astype(jnp.float32)
        if total is None:
            total = summed
            continue
        for k in range(1, n_expert):
            part = summed[(k - 1) * tok_rows:k * tok_rows].astype(jnp.bfloat16)
            total = total + lax.ppermute(part, "expert", _xor_pairs(n_expert, k)).astype(jnp.float32)
    return total.astype(jnp.bfloat16)


def local(tokens, route_scale, expert_ids, gate_weight, up_weight, down_weight):
    tok_rows = tokens.shape[0]
    n_devices = lax.axis_size("expert")
    capacity = min(tok_rows, 2 * tok_rows * SPAN // n_devices)
    n_tensor = lax.axis_size("tensor")
    shaped = n_tensor == 4 and n_devices in (1, 2, 4) and tok_rows <= tokens.shape[1]
    if capacity == tok_rows and shaped:
        return gathered(tokens, route_scale, expert_ids, gate_weight, up_weight, down_weight)
    return dispatched(tokens, route_scale, expert_ids, gate_weight, up_weight, down_weight)


def solution(mesh):
    placed = (
        P(("groups", "expert"), "tensor"),
        P(("groups", "expert")),
        P(("groups", "expert"), None),
        P("expert", None, "tensor"),
        P("expert", None, "tensor"),
        P("expert", "tensor", None),
    )
    return jax.shard_map(
        local,
        mesh=mesh,
        in_specs=placed,
        out_specs=P(("groups", "expert"), "tensor"),
        check_vma=False,
    )
```

```python
import jax
import jax.numpy as jnp
from jax import lax
from jax.sharding import PartitionSpec as P

SPAN = 2


def dispatched(tokens, route_scale, expert_ids, gate_weight, up_weight, down_weight):
    tok_rows = tokens.shape[0]
    n_devices = lax.axis_size("expert")
    experts = n_devices // SPAN
    capacity = min(tok_rows, 2 * tok_rows * SPAN // n_devices)
    routed = expert_ids[:, 0]
    one_hot = (routed[:, None] == jnp.arange(experts, dtype=jnp.int32)[None, :]).astype(jnp.int32)
    slot_rank = jnp.sum((jnp.cumsum(one_hot, axis=0) - one_hot) * one_hot, axis=1)
    flat_slot = routed * capacity + slot_rank
    placing = (
        flat_slot[None, :] == jnp.arange(experts * capacity, dtype=jnp.int32)[:, None]
    ).astype(jnp.bfloat16)
    scaled = (tokens.astype(jnp.float32) * route_scale[:, None]).astype(jnp.bfloat16)
    gate_local = gate_weight[0]
    up_local = up_weight[0]
    down_local = down_weight[0]
    full_rows = lax.all_gather(scaled, "tensor", axis=1, tiled=True)
    width = full_rows.shape[1]
    packed = jnp.dot(placing, full_rows, preferred_element_type=jnp.float32).astype(jnp.bfloat16)
    outgoing = jnp.repeat(packed.reshape(experts, capacity, width), SPAN, axis=0)
    arrived = lax.all_to_all(outgoing, "expert", split_axis=0, concat_axis=0, tiled=True)
    slot_rows = arrived.reshape(n_devices * capacity, width)
    gate_act = jnp.dot(slot_rows, gate_local, preferred_element_type=jnp.float32)
    up_act = jnp.dot(slot_rows, up_local, preferred_element_type=jnp.float32)
    hidden = (jax.nn.silu(gate_act) * up_act).astype(jnp.bfloat16)
    partial_value = jnp.dot(hidden, down_local, preferred_element_type=jnp.float32)
    width = partial_value.shape[1]
    outgoing_back = partial_value.astype(jnp.bfloat16).reshape(n_devices, capacity, width)
    returned = lax.all_to_all(outgoing_back, "expert", split_axis=0, concat_axis=0, tiled=True)
    paired = jnp.sum(returned.astype(jnp.float32).reshape(experts, SPAN, capacity, width), axis=1)
    picked = jnp.take(paired.reshape(experts * capacity, width), flat_slot, axis=0)
    summed = lax.psum_scatter(
        picked.astype(jnp.bfloat16), "tensor", scatter_dimension=1, tiled=True
    )
    return summed


def _xor_pairs(size, k):
    return [(i, i ^ k) for i in range(size)]


_ORDER = (0, 2, 1, 3)


def _slots(weight, t, width, axis, order=_ORDER):
    return jnp.concatenate(
        [lax.dynamic_slice_in_dim(weight, (t ^ k) * width, width, axis=axis) for k in order], axis=axis)


def gathered(tokens, route_scale, expert_ids, gate_weight, up_weight, down_weight):
    tok_rows, width = tokens.shape
    n_expert = lax.axis_size("expert")
    n_tensor = lax.axis_size("tensor")
    me = lax.axis_index("expert")
    t = lax.axis_index("tensor")
    expert = (me // SPAN).astype(jnp.bfloat16)
    scaled = (tokens.astype(jnp.float32) * route_scale[:, None]).astype(jnp.bfloat16)
    id_rows = jnp.zeros((16, width), jnp.bfloat16)
    id_rows = id_rows.at[0, :tok_rows].set(expert_ids[:, 0].astype(jnp.bfloat16))
    block = jnp.concatenate([scaled, id_rows], axis=0)
    blocks = [block] + [
        lax.ppermute(block, "expert", _xor_pairs(n_expert, k)) for k in range(1, n_expert)
    ]
    gate_w = _slots(gate_weight[0], t, width, 0)
    up_w = _slots(up_weight[0], t, width, 0)
    down_keep = _slots(down_weight[0], t, width, 1, _ORDER[:2])
    down_send = _slots(down_weight[0], t, width, 1, _ORDER[2:])
    waves = [[0], [1], list(range(2, n_expert))][:max(1, min(3, n_expert))]
    total = None
    previous = None
    for wave in waves:
        routed = jnp.concatenate([blocks[k][tok_rows, :tok_rows] for k in wave])
        piece = jnp.concatenate([blocks[k][:tok_rows] for k in wave])
        pair = jnp.concatenate(
            [piece, lax.ppermute(piece, "tensor", _xor_pairs(n_tensor, 2))], axis=1)
        rows = jnp.concatenate(
            [pair, lax.ppermute(pair, "tensor", _xor_pairs(n_tensor, 1))], axis=1)
        if previous is not None:
            rows, routed, _ = lax.optimization_barrier((rows, routed, previous))
        gate_act = jnp.dot(rows, gate_w, preferred_element_type=jnp.float32)
        up_act = jnp.dot(rows, up_w, preferred_element_type=jnp.float32)
        mine = (routed == expert)[:, None]
        hidden = jnp.where(mine, jax.nn.silu(gate_act) * up_act, 0.0).astype(jnp.bfloat16)
        keep = jnp.dot(hidden, down_keep, preferred_element_type=jnp.float32).astype(jnp.bfloat16)
        send = jnp.dot(hidden, down_send, preferred_element_type=jnp.float32).astype(jnp.bfloat16)
        previous = keep
        over_c = keep.astype(jnp.float32) + lax.ppermute(
            send, "tensor", _xor_pairs(n_tensor, 1)).astype(jnp.float32)
        summed = over_c[:, :width] + lax.ppermute(
            over_c[:, width:].astype(jnp.bfloat16), "tensor", _xor_pairs(n_tensor, 2)).astype(jnp.float32)
        for i, k in enumerate(wave):
            part = summed[i * tok_rows:(i + 1) * tok_rows]
            if k:
                part = lax.ppermute(
                    part.astype(jnp.bfloat16), "expert", _xor_pairs(n_expert, k)).astype(jnp.float32)
            total = part if total is None else total + part
    return total.astype(jnp.bfloat16)


def local(tokens, route_scale, expert_ids, gate_weight, up_weight, down_weight):
    tok_rows = tokens.shape[0]
    n_devices = lax.axis_size("expert")
    capacity = min(tok_rows, 2 * tok_rows * SPAN // n_devices)
    n_tensor = lax.axis_size("tensor")
    shaped = n_tensor == 4 and n_devices in (1, 2, 4) and tok_rows <= tokens.shape[1]
    if capacity == tok_rows and shaped:
        return gathered(tokens, route_scale, expert_ids, gate_weight, up_weight, down_weight)
    return dispatched(tokens, route_scale, expert_ids, gate_weight, up_weight, down_weight)


def solution(mesh):
    placed = (
        P(("groups", "expert"), "tensor"),
        P(("groups", "expert")),
        P(("groups", "expert"), None),
        P("expert", None, "tensor"),
        P("expert", None, "tensor"),
        P("expert", "tensor", None),
    )
    return jax.shard_map(
        local,
        mesh=mesh,
        in_specs=placed,
        out_specs=P(("groups", "expert"), "tensor"),
        check_vma=False,
    )
```

```python
import jax
import jax.numpy as jnp
from jax import lax
from jax.sharding import PartitionSpec as P

SPAN = 2


def dispatched(tokens, route_scale, expert_ids, gate_weight, up_weight, down_weight):
    tok_rows = tokens.shape[0]
    n_devices = lax.axis_size("expert")
    experts = n_devices // SPAN
    capacity = min(tok_rows, 2 * tok_rows * SPAN // n_devices)
    routed = expert_ids[:, 0]
    one_hot = (routed[:, None] == jnp.arange(experts, dtype=jnp.int32)[None, :]).astype(jnp.int32)
    slot_rank = jnp.sum((jnp.cumsum(one_hot, axis=0) - one_hot) * one_hot, axis=1)
    flat_slot = routed * capacity + slot_rank
    placing = (
        flat_slot[None, :] == jnp.arange(experts * capacity, dtype=jnp.int32)[:, None]
    ).astype(jnp.bfloat16)
    scaled = (tokens.astype(jnp.float32) * route_scale[:, None]).astype(jnp.bfloat16)
    gate_local = gate_weight[0]
    up_local = up_weight[0]
    down_local = down_weight[0]
    full_rows = lax.all_gather(scaled, "tensor", axis=1, tiled=True)
    width = full_rows.shape[1]
    packed = jnp.dot(placing, full_rows, preferred_element_type=jnp.float32).astype(jnp.bfloat16)
    outgoing = jnp.repeat(packed.reshape(experts, capacity, width), SPAN, axis=0)
    arrived = lax.all_to_all(outgoing, "expert", split_axis=0, concat_axis=0, tiled=True)
    slot_rows = arrived.reshape(n_devices * capacity, width)
    gate_act = jnp.dot(slot_rows, gate_local, preferred_element_type=jnp.float32)
    up_act = jnp.dot(slot_rows, up_local, preferred_element_type=jnp.float32)
    hidden = (jax.nn.silu(gate_act) * up_act).astype(jnp.bfloat16)
    partial_value = jnp.dot(hidden, down_local, preferred_element_type=jnp.float32)
    width = partial_value.shape[1]
    outgoing_back = partial_value.astype(jnp.bfloat16).reshape(n_devices, capacity, width)
    returned = lax.all_to_all(outgoing_back, "expert", split_axis=0, concat_axis=0, tiled=True)
    paired = jnp.sum(returned.astype(jnp.float32).reshape(experts, SPAN, capacity, width), axis=1)
    picked = jnp.take(paired.reshape(experts * capacity, width), flat_slot, axis=0)
    summed = lax.psum_scatter(
        picked.astype(jnp.bfloat16), "tensor", scatter_dimension=1, tiled=True
    )
    return summed


def _xor_pairs(size, k):
    return [(i, i ^ k) for i in range(size)]


_ORDER = (0, 2, 1, 3)


def _slots(weight, t, width, axis, order=_ORDER):
    return jnp.concatenate(
        [lax.dynamic_slice_in_dim(weight, (t ^ k) * width, width, axis=axis) for k in order], axis=axis)


def gathered(tokens, route_scale, expert_ids, gate_weight, up_weight, down_weight):
    tok_rows, width = tokens.shape
    n_expert = lax.axis_size("expert")
    n_tensor = lax.axis_size("tensor")
    me = lax.axis_index("expert")
    t = lax.axis_index("tensor")
    expert = (me // SPAN).astype(jnp.bfloat16)
    scaled = (tokens.astype(jnp.float32) * route_scale[:, None]).astype(jnp.bfloat16)
    id_rows = jnp.zeros((16, width), jnp.bfloat16)
    id_rows = id_rows.at[0, :tok_rows].set(expert_ids[:, 0].astype(jnp.bfloat16))
    block = jnp.concatenate([scaled, id_rows], axis=0)
    blocks = [block] + [
        lax.ppermute(block, "expert", _xor_pairs(n_expert, k)) for k in range(1, n_expert)
    ]
    gate_w = _slots(gate_weight[0], t, width, 0)
    up_w = _slots(up_weight[0], t, width, 0)
    down_keep = _slots(down_weight[0], t, width, 1, _ORDER[:2])
    down_send = _slots(down_weight[0], t, width, 1, _ORDER[2:])
    waves = [[k] for k in range(n_expert)]
    total = None
    previous = None
    for wave in waves:
        routed = jnp.concatenate([blocks[k][tok_rows, :tok_rows] for k in wave])
        piece = jnp.concatenate([blocks[k][:tok_rows] for k in wave])
        pair = jnp.concatenate(
            [piece, lax.ppermute(piece, "tensor", _xor_pairs(n_tensor, 2))], axis=1)
        rows = jnp.concatenate(
            [pair, lax.ppermute(pair, "tensor", _xor_pairs(n_tensor, 1))], axis=1)
        if previous is not None:
            rows, routed, _ = lax.optimization_barrier((rows, routed, previous))
        gate_act = jnp.dot(rows, gate_w, preferred_element_type=jnp.float32)
        up_act = jnp.dot(rows, up_w, preferred_element_type=jnp.float32)
        mine = (routed == expert)[:, None]
        hidden = jnp.where(mine, jax.nn.silu(gate_act) * up_act, 0.0).astype(jnp.bfloat16)
        keep = jnp.dot(hidden, down_keep, preferred_element_type=jnp.float32).astype(jnp.bfloat16)
        send = jnp.dot(hidden, down_send, preferred_element_type=jnp.float32).astype(jnp.bfloat16)
        previous = keep
        over_c = keep.astype(jnp.float32) + lax.ppermute(
            send, "tensor", _xor_pairs(n_tensor, 1)).astype(jnp.float32)
        summed = over_c[:, :width] + lax.ppermute(
            over_c[:, width:].astype(jnp.bfloat16), "tensor", _xor_pairs(n_tensor, 2)).astype(jnp.float32)
        for i, k in enumerate(wave):
            part = summed[i * tok_rows:(i + 1) * tok_rows]
            if k:
                part = lax.ppermute(
                    part.astype(jnp.bfloat16), "expert", _xor_pairs(n_expert, k)).astype(jnp.float32)
            total = part if total is None else total + part
    return total.astype(jnp.bfloat16)


def local(tokens, route_scale, expert_ids, gate_weight, up_weight, down_weight):
    tok_rows = tokens.shape[0]
    n_devices = lax.axis_size("expert")
    capacity = min(tok_rows, 2 * tok_rows * SPAN // n_devices)
    n_tensor = lax.axis_size("tensor")
    shaped = n_tensor == 4 and n_devices in (1, 2, 4) and tok_rows <= tokens.shape[1]
    if capacity == tok_rows and shaped:
        return gathered(tokens, route_scale, expert_ids, gate_weight, up_weight, down_weight)
    return dispatched(tokens, route_scale, expert_ids, gate_weight, up_weight, down_weight)


def solution(mesh):
    placed = (
        P(("groups", "expert"), "tensor"),
        P(("groups", "expert")),
        P(("groups", "expert"), None),
        P("expert", None, "tensor"),
        P("expert", None, "tensor"),
        P("expert", "tensor", None),
    )
    return jax.shard_map(
        local,
        mesh=mesh,
        in_specs=placed,
        out_specs=P(("groups", "expert"), "tensor"),
        check_vma=False,
    )
```

```python
import jax
import jax.numpy as jnp
from jax import lax
from jax.sharding import PartitionSpec as P

SPAN = 2


def dispatched(tokens, route_scale, expert_ids, gate_weight, up_weight, down_weight):
    tok_rows = tokens.shape[0]
    n_devices = lax.axis_size("expert")
    experts = n_devices // SPAN
    capacity = min(tok_rows, 2 * tok_rows * SPAN // n_devices)
    routed = expert_ids[:, 0]
    one_hot = (routed[:, None] == jnp.arange(experts, dtype=jnp.int32)[None, :]).astype(jnp.int32)
    slot_rank = jnp.sum((jnp.cumsum(one_hot, axis=0) - one_hot) * one_hot, axis=1)
    flat_slot = routed * capacity + slot_rank
    placing = (
        flat_slot[None, :] == jnp.arange(experts * capacity, dtype=jnp.int32)[:, None]
    ).astype(jnp.bfloat16)
    scaled = (tokens.astype(jnp.float32) * route_scale[:, None]).astype(jnp.bfloat16)
    gate_local = gate_weight[0]
    up_local = up_weight[0]
    down_local = down_weight[0]
    full_rows = lax.all_gather(scaled, "tensor", axis=1, tiled=True)
    width = full_rows.shape[1]
    packed = jnp.dot(placing, full_rows, preferred_element_type=jnp.float32).astype(jnp.bfloat16)
    outgoing = jnp.repeat(packed.reshape(experts, capacity, width), SPAN, axis=0)
    arrived = lax.all_to_all(outgoing, "expert", split_axis=0, concat_axis=0, tiled=True)
    slot_rows = arrived.reshape(n_devices * capacity, width)
    gate_act = jnp.dot(slot_rows, gate_local, preferred_element_type=jnp.float32)
    up_act = jnp.dot(slot_rows, up_local, preferred_element_type=jnp.float32)
    hidden = (jax.nn.silu(gate_act) * up_act).astype(jnp.bfloat16)
    partial_value = jnp.dot(hidden, down_local, preferred_element_type=jnp.float32)
    width = partial_value.shape[1]
    outgoing_back = partial_value.astype(jnp.bfloat16).reshape(n_devices, capacity, width)
    returned = lax.all_to_all(outgoing_back, "expert", split_axis=0, concat_axis=0, tiled=True)
    paired = jnp.sum(returned.astype(jnp.float32).reshape(experts, SPAN, capacity, width), axis=1)
    picked = jnp.take(paired.reshape(experts * capacity, width), flat_slot, axis=0)
    summed = lax.psum_scatter(
        picked.astype(jnp.bfloat16), "tensor", scatter_dimension=1, tiled=True
    )
    return summed


def _xor_pairs(size, k):
    return [(i, i ^ k) for i in range(size)]


_ORDER = (0, 2, 1, 3)


def _slots(weight, t, width, axis, order=_ORDER):
    return jnp.concatenate(
        [lax.dynamic_slice_in_dim(weight, (t ^ k) * width, width, axis=axis) for k in order], axis=axis)


def gathered(tokens, route_scale, expert_ids, gate_weight, up_weight, down_weight):
    tok_rows, width = tokens.shape
    n_expert = lax.axis_size("expert")
    n_tensor = lax.axis_size("tensor")
    me = lax.axis_index("expert")
    t = lax.axis_index("tensor")
    scaled = (tokens.astype(jnp.float32) * route_scale[:, None]).astype(jnp.bfloat16)
    blocks = [scaled] + [
        lax.ppermute(scaled, "expert", _xor_pairs(n_expert, k)) for k in range(1, n_expert)
    ]
    routed = expert_ids[:, 0][:, None]
    gate_w = _slots(gate_weight[0], t, width, 0)
    up_w = _slots(up_weight[0], t, width, 0)
    down_keep = _slots(down_weight[0], t, width, 1, _ORDER[:2])
    down_send = _slots(down_weight[0], t, width, 1, _ORDER[2:])
    waves = [[k] for k in range(n_expert)]
    total = None
    previous = None
    for wave in waves:
        piece = jnp.concatenate([blocks[k] for k in wave])
        pair = jnp.concatenate(
            [piece, lax.ppermute(piece, "tensor", _xor_pairs(n_tensor, 2))], axis=1)
        rows = jnp.concatenate(
            [pair, lax.ppermute(pair, "tensor", _xor_pairs(n_tensor, 1))], axis=1)
        if previous is not None:
            rows, _ = lax.optimization_barrier((rows, previous))
        gate_act = jnp.dot(rows, gate_w, preferred_element_type=jnp.float32)
        up_act = jnp.dot(rows, up_w, preferred_element_type=jnp.float32)
        hidden = (jax.nn.silu(gate_act) * up_act).astype(jnp.bfloat16)
        keep = jnp.dot(hidden, down_keep, preferred_element_type=jnp.float32).astype(jnp.bfloat16)
        send = jnp.dot(hidden, down_send, preferred_element_type=jnp.float32).astype(jnp.bfloat16)
        previous = keep
        over_c = keep.astype(jnp.float32) + lax.ppermute(
            send, "tensor", _xor_pairs(n_tensor, 1)).astype(jnp.float32)
        summed = over_c[:, :width] + lax.ppermute(
            over_c[:, width:].astype(jnp.bfloat16), "tensor", _xor_pairs(n_tensor, 2)).astype(jnp.float32)
        for i, k in enumerate(wave):
            part = summed[i * tok_rows:(i + 1) * tok_rows]
            if k:
                part = lax.ppermute(
                    part.astype(jnp.bfloat16), "expert", _xor_pairs(n_expert, k)).astype(jnp.float32)
            part = jnp.where(routed == (me ^ k) // SPAN, part, 0.0)
            total = part if total is None else total + part
    return total.astype(jnp.bfloat16)


def local(tokens, route_scale, expert_ids, gate_weight, up_weight, down_weight):
    tok_rows = tokens.shape[0]
    n_devices = lax.axis_size("expert")
    capacity = min(tok_rows, 2 * tok_rows * SPAN // n_devices)
    n_tensor = lax.axis_size("tensor")
    shaped = n_tensor == 4 and n_devices in (1, 2, 4) and tok_rows <= tokens.shape[1]
    if capacity == tok_rows and shaped:
        return gathered(tokens, route_scale, expert_ids, gate_weight, up_weight, down_weight)
    return dispatched(tokens, route_scale, expert_ids, gate_weight, up_weight, down_weight)


def solution(mesh):
    placed = (
        P(("groups", "expert"), "tensor"),
        P(("groups", "expert")),
        P(("groups", "expert"), None),
        P("expert", None, "tensor"),
        P("expert", None, "tensor"),
        P("expert", "tensor", None),
    )
    return jax.shard_map(
        local,
        mesh=mesh,
        in_specs=placed,
        out_specs=P(("groups", "expert"), "tensor"),
        check_vma=False,
    )
```

```python
import jax
import jax.numpy as jnp
from jax import lax
from jax.sharding import PartitionSpec as P

SPAN = 2


def dispatched(tokens, route_scale, expert_ids, gate_weight, up_weight, down_weight):
    tok_rows = tokens.shape[0]
    n_devices = lax.axis_size("expert")
    experts = n_devices // SPAN
    capacity = min(tok_rows, 2 * tok_rows * SPAN // n_devices)
    routed = expert_ids[:, 0]
    one_hot = (routed[:, None] == jnp.arange(experts, dtype=jnp.int32)[None, :]).astype(jnp.int32)
    slot_rank = jnp.sum((jnp.cumsum(one_hot, axis=0) - one_hot) * one_hot, axis=1)
    flat_slot = routed * capacity + slot_rank
    placing = (
        flat_slot[None, :] == jnp.arange(experts * capacity, dtype=jnp.int32)[:, None]
    ).astype(jnp.bfloat16)
    scaled = (tokens.astype(jnp.float32) * route_scale[:, None]).astype(jnp.bfloat16)
    gate_local = gate_weight[0]
    up_local = up_weight[0]
    down_local = down_weight[0]
    full_rows = lax.all_gather(scaled, "tensor", axis=1, tiled=True)
    width = full_rows.shape[1]
    packed = jnp.dot(placing, full_rows, preferred_element_type=jnp.float32).astype(jnp.bfloat16)
    outgoing = jnp.repeat(packed.reshape(experts, capacity, width), SPAN, axis=0)
    arrived = lax.all_to_all(outgoing, "expert", split_axis=0, concat_axis=0, tiled=True)
    slot_rows = arrived.reshape(n_devices * capacity, width)
    gate_act = jnp.dot(slot_rows, gate_local, preferred_element_type=jnp.float32)
    up_act = jnp.dot(slot_rows, up_local, preferred_element_type=jnp.float32)
    hidden = (jax.nn.silu(gate_act) * up_act).astype(jnp.bfloat16)
    partial_value = jnp.dot(hidden, down_local, preferred_element_type=jnp.float32)
    width = partial_value.shape[1]
    outgoing_back = partial_value.astype(jnp.bfloat16).reshape(n_devices, capacity, width)
    returned = lax.all_to_all(outgoing_back, "expert", split_axis=0, concat_axis=0, tiled=True)
    paired = jnp.sum(returned.astype(jnp.float32).reshape(experts, SPAN, capacity, width), axis=1)
    picked = jnp.take(paired.reshape(experts * capacity, width), flat_slot, axis=0)
    summed = lax.psum_scatter(
        picked.astype(jnp.bfloat16), "tensor", scatter_dimension=1, tiled=True
    )
    return summed


def _xor_pairs(size, k):
    return [(i, i ^ k) for i in range(size)]


_ORDER = (0, 2, 1, 3)


def _slots(weight, t, width, axis, order=_ORDER):
    return jnp.concatenate(
        [lax.dynamic_slice_in_dim(weight, (t ^ k) * width, width, axis=axis) for k in order], axis=axis)


def gathered(tokens, route_scale, expert_ids, gate_weight, up_weight, down_weight):
    tok_rows, width = tokens.shape
    n_expert = lax.axis_size("expert")
    n_tensor = lax.axis_size("tensor")
    me = lax.axis_index("expert")
    t = lax.axis_index("tensor")
    scaled = (tokens.astype(jnp.float32) * route_scale[:, None]).astype(jnp.bfloat16)
    blocks = [scaled] + [
        lax.ppermute(scaled, "expert", _xor_pairs(n_expert, k)) for k in range(1, n_expert)
    ]
    routed = expert_ids[:, 0][:, None]
    gate_w = _slots(gate_weight[0], t, width, 0)
    up_w = _slots(up_weight[0], t, width, 0)
    down_keep = _slots(down_weight[0], t, width, 1, _ORDER[:2])
    down_send = _slots(down_weight[0], t, width, 1, _ORDER[2:])
    waves = [[k] for k in range(n_expert)]
    total = None
    previous = None
    for wave in waves:
        piece = jnp.concatenate([blocks[k] for k in wave])
        pair = jnp.concatenate(
            [piece, lax.ppermute(piece, "tensor", _xor_pairs(n_tensor, 2))], axis=1)
        rows = jnp.concatenate(
            [pair, lax.ppermute(pair, "tensor", _xor_pairs(n_tensor, 1))], axis=1)
        if previous is not None:
            rows, _ = lax.optimization_barrier((rows, previous))
        gate_act = jnp.dot(rows, gate_w, preferred_element_type=jnp.float32)
        up_act = jnp.dot(rows, up_w, preferred_element_type=jnp.float32)
        hidden = (jax.nn.silu(gate_act) * up_act).astype(jnp.bfloat16)
        keep = jnp.dot(hidden, down_keep, preferred_element_type=jnp.float32).astype(jnp.bfloat16)
        send = jnp.dot(hidden, down_send, preferred_element_type=jnp.float32).astype(jnp.bfloat16)
        over_c = keep.astype(jnp.float32) + lax.ppermute(
            send, "tensor", _xor_pairs(n_tensor, 1)).astype(jnp.float32)
        summed = over_c[:, :width] + lax.ppermute(
            over_c[:, width:].astype(jnp.bfloat16), "tensor", _xor_pairs(n_tensor, 2)).astype(jnp.float32)
        previous = summed
        for i, k in enumerate(wave):
            part = summed[i * tok_rows:(i + 1) * tok_rows]
            if k:
                part = lax.ppermute(
                    part.astype(jnp.bfloat16), "expert", _xor_pairs(n_expert, k)).astype(jnp.float32)
            part = jnp.where(routed == (me ^ k) // SPAN, part, 0.0)
            total = part if total is None else total + part
    return total.astype(jnp.bfloat16)


def local(tokens, route_scale, expert_ids, gate_weight, up_weight, down_weight):
    tok_rows = tokens.shape[0]
    n_devices = lax.axis_size("expert")
    capacity = min(tok_rows, 2 * tok_rows * SPAN // n_devices)
    n_tensor = lax.axis_size("tensor")
    shaped = n_tensor == 4 and n_devices in (1, 2, 4) and tok_rows <= tokens.shape[1]
    if capacity == tok_rows and shaped:
        return gathered(tokens, route_scale, expert_ids, gate_weight, up_weight, down_weight)
    return dispatched(tokens, route_scale, expert_ids, gate_weight, up_weight, down_weight)


def solution(mesh):
    placed = (
        P(("groups", "expert"), "tensor"),
        P(("groups", "expert")),
        P(("groups", "expert"), None),
        P("expert", None, "tensor"),
        P("expert", None, "tensor"),
        P("expert", "tensor", None),
    )
    return jax.shard_map(
        local,
        mesh=mesh,
        in_specs=placed,
        out_specs=P(("groups", "expert"), "tensor"),
        check_vma=False,
    )
```

```python
import jax
import jax.numpy as jnp
from jax import lax
from jax.sharding import PartitionSpec as P

SPAN = 2


def dispatched(tokens, route_scale, expert_ids, gate_weight, up_weight, down_weight):
    tok_rows = tokens.shape[0]
    n_devices = lax.axis_size("expert")
    experts = n_devices // SPAN
    capacity = min(tok_rows, 2 * tok_rows * SPAN // n_devices)
    routed = expert_ids[:, 0]
    one_hot = (routed[:, None] == jnp.arange(experts, dtype=jnp.int32)[None, :]).astype(jnp.int32)
    slot_rank = jnp.sum((jnp.cumsum(one_hot, axis=0) - one_hot) * one_hot, axis=1)
    flat_slot = routed * capacity + slot_rank
    placing = (
        flat_slot[None, :] == jnp.arange(experts * capacity, dtype=jnp.int32)[:, None]
    ).astype(jnp.bfloat16)
    scaled = (tokens.astype(jnp.float32) * route_scale[:, None]).astype(jnp.bfloat16)
    gate_local = gate_weight[0]
    up_local = up_weight[0]
    down_local = down_weight[0]
    full_rows = lax.all_gather(scaled, "tensor", axis=1, tiled=True)
    width = full_rows.shape[1]
    packed = jnp.dot(placing, full_rows, preferred_element_type=jnp.float32).astype(jnp.bfloat16)
    outgoing = jnp.repeat(packed.reshape(experts, capacity, width), SPAN, axis=0)
    arrived = lax.all_to_all(outgoing, "expert", split_axis=0, concat_axis=0, tiled=True)
    slot_rows = arrived.reshape(n_devices * capacity, width)
    gate_act = jnp.dot(slot_rows, gate_local, preferred_element_type=jnp.float32)
    up_act = jnp.dot(slot_rows, up_local, preferred_element_type=jnp.float32)
    hidden = (jax.nn.silu(gate_act) * up_act).astype(jnp.bfloat16)
    partial_value = jnp.dot(hidden, down_local, preferred_element_type=jnp.float32)
    width = partial_value.shape[1]
    outgoing_back = partial_value.astype(jnp.bfloat16).reshape(n_devices, capacity, width)
    returned = lax.all_to_all(outgoing_back, "expert", split_axis=0, concat_axis=0, tiled=True)
    paired = jnp.sum(returned.astype(jnp.float32).reshape(experts, SPAN, capacity, width), axis=1)
    picked = jnp.take(paired.reshape(experts * capacity, width), flat_slot, axis=0)
    summed = lax.psum_scatter(
        picked.astype(jnp.bfloat16), "tensor", scatter_dimension=1, tiled=True
    )
    return summed


def _xor_pairs(size, k):
    return [(i, i ^ k) for i in range(size)]


_ORDER = (0, 2, 1, 3)


def _slots(weight, t, width, axis, order=_ORDER):
    return jnp.concatenate(
        [lax.dynamic_slice_in_dim(weight, (t ^ k) * width, width, axis=axis) for k in order], axis=axis)


def gathered(tokens, route_scale, expert_ids, gate_weight, up_weight, down_weight):
    tok_rows, width = tokens.shape
    n_expert = lax.axis_size("expert")
    n_tensor = lax.axis_size("tensor")
    me = lax.axis_index("expert")
    t = lax.axis_index("tensor")
    scaled = (tokens.astype(jnp.float32) * route_scale[:, None]).astype(jnp.bfloat16)
    blocks = [scaled] + [
        lax.ppermute(scaled, "expert", _xor_pairs(n_expert, k)) for k in range(1, n_expert)
    ]
    routed = expert_ids[:, 0][:, None]
    gate_w = _slots(gate_weight[0], t, width, 0)
    up_w = _slots(up_weight[0], t, width, 0)
    down_keep = _slots(down_weight[0], t, width, 1, _ORDER[:2])
    down_send = _slots(down_weight[0], t, width, 1, _ORDER[2:])
    waves = [[k] for k in [0] + list(range(2, n_expert)) + [1][:n_expert - 1]]
    total = None
    previous = None
    for wave in waves:
        piece = jnp.concatenate([blocks[k] for k in wave])
        pair = jnp.concatenate(
            [piece, lax.ppermute(piece, "tensor", _xor_pairs(n_tensor, 2))], axis=1)
        rows = jnp.concatenate(
            [pair, lax.ppermute(pair, "tensor", _xor_pairs(n_tensor, 1))], axis=1)
        if previous is not None:
            rows, _ = lax.optimization_barrier((rows, previous))
        gate_act = jnp.dot(rows, gate_w, preferred_element_type=jnp.float32)
        up_act = jnp.dot(rows, up_w, preferred_element_type=jnp.float32)
        hidden = (jax.nn.silu(gate_act) * up_act).astype(jnp.bfloat16)
        keep = jnp.dot(hidden, down_keep, preferred_element_type=jnp.float32).astype(jnp.bfloat16)
        send = jnp.dot(hidden, down_send, preferred_element_type=jnp.float32).astype(jnp.bfloat16)
        previous = keep
        over_c = keep.astype(jnp.float32) + lax.ppermute(
            send, "tensor", _xor_pairs(n_tensor, 1)).astype(jnp.float32)
        summed = over_c[:, :width] + lax.ppermute(
            over_c[:, width:].astype(jnp.bfloat16), "tensor", _xor_pairs(n_tensor, 2)).astype(jnp.float32)
        for i, k in enumerate(wave):
            part = summed[i * tok_rows:(i + 1) * tok_rows]
            if k:
                part = lax.ppermute(
                    part.astype(jnp.bfloat16), "expert", _xor_pairs(n_expert, k)).astype(jnp.float32)
            part = jnp.where(routed == (me ^ k) // SPAN, part, 0.0)
            total = part if total is None else total + part
    return total.astype(jnp.bfloat16)


def local(tokens, route_scale, expert_ids, gate_weight, up_weight, down_weight):
    tok_rows = tokens.shape[0]
    n_devices = lax.axis_size("expert")
    capacity = min(tok_rows, 2 * tok_rows * SPAN // n_devices)
    n_tensor = lax.axis_size("tensor")
    shaped = n_tensor == 4 and n_devices in (1, 2, 4) and tok_rows <= tokens.shape[1]
    if capacity == tok_rows and shaped:
        return gathered(tokens, route_scale, expert_ids, gate_weight, up_weight, down_weight)
    return dispatched(tokens, route_scale, expert_ids, gate_weight, up_weight, down_weight)


def solution(mesh):
    placed = (
        P(("groups", "expert"), "tensor"),
        P(("groups", "expert")),
        P(("groups", "expert"), None),
        P("expert", None, "tensor"),
        P("expert", None, "tensor"),
        P("expert", "tensor", None),
    )
    return jax.shard_map(
        local,
        mesh=mesh,
        in_specs=placed,
        out_specs=P(("groups", "expert"), "tensor"),
        check_vma=False,
    )
```

```python
import jax
import jax.numpy as jnp
from jax import lax
from jax.sharding import PartitionSpec as P

SPAN = 2


def dispatched(tokens, route_scale, expert_ids, gate_weight, up_weight, down_weight):
    tok_rows = tokens.shape[0]
    n_devices = lax.axis_size("expert")
    experts = n_devices // SPAN
    capacity = min(tok_rows, 2 * tok_rows * SPAN // n_devices)
    routed = expert_ids[:, 0]
    one_hot = (routed[:, None] == jnp.arange(experts, dtype=jnp.int32)[None, :]).astype(jnp.int32)
    slot_rank = jnp.sum((jnp.cumsum(one_hot, axis=0) - one_hot) * one_hot, axis=1)
    flat_slot = routed * capacity + slot_rank
    placing = (
        flat_slot[None, :] == jnp.arange(experts * capacity, dtype=jnp.int32)[:, None]
    ).astype(jnp.bfloat16)
    scaled = (tokens.astype(jnp.float32) * route_scale[:, None]).astype(jnp.bfloat16)
    gate_local = gate_weight[0]
    up_local = up_weight[0]
    down_local = down_weight[0]
    full_rows = lax.all_gather(scaled, "tensor", axis=1, tiled=True)
    width = full_rows.shape[1]
    packed = jnp.dot(placing, full_rows, preferred_element_type=jnp.float32).astype(jnp.bfloat16)
    outgoing = jnp.repeat(packed.reshape(experts, capacity, width), SPAN, axis=0)
    arrived = lax.all_to_all(outgoing, "expert", split_axis=0, concat_axis=0, tiled=True)
    slot_rows = arrived.reshape(n_devices * capacity, width)
    gate_act = jnp.dot(slot_rows, gate_local, preferred_element_type=jnp.float32)
    up_act = jnp.dot(slot_rows, up_local, preferred_element_type=jnp.float32)
    hidden = (jax.nn.silu(gate_act) * up_act).astype(jnp.bfloat16)
    partial_value = jnp.dot(hidden, down_local, preferred_element_type=jnp.float32)
    width = partial_value.shape[1]
    outgoing_back = partial_value.astype(jnp.bfloat16).reshape(n_devices, capacity, width)
    returned = lax.all_to_all(outgoing_back, "expert", split_axis=0, concat_axis=0, tiled=True)
    paired = jnp.sum(returned.astype(jnp.float32).reshape(experts, SPAN, capacity, width), axis=1)
    picked = jnp.take(paired.reshape(experts * capacity, width), flat_slot, axis=0)
    summed = lax.psum_scatter(
        picked.astype(jnp.bfloat16), "tensor", scatter_dimension=1, tiled=True
    )
    return summed


def _xor_pairs(size, k):
    return [(i, i ^ k) for i in range(size)]


_ORDER = (0, 2, 1, 3)


def _slots(weight, t, width, axis, order=_ORDER):
    return jnp.concatenate(
        [lax.dynamic_slice_in_dim(weight, (t ^ k) * width, width, axis=axis) for k in order], axis=axis)


def gathered(tokens, route_scale, expert_ids, gate_weight, up_weight, down_weight):
    tok_rows, width = tokens.shape
    n_expert = lax.axis_size("expert")
    n_tensor = lax.axis_size("tensor")
    me = lax.axis_index("expert")
    t = lax.axis_index("tensor")
    scaled = (tokens.astype(jnp.float32) * route_scale[:, None]).astype(jnp.bfloat16)
    routed = expert_ids[:, 0][:, None]
    gate_w = _slots(gate_weight[0], t, width, 0)
    up_w = _slots(up_weight[0], t, width, 0)
    down_keep = _slots(down_weight[0], t, width, 1, _ORDER[:2])
    down_send = _slots(down_weight[0], t, width, 1, _ORDER[2:])
    waves = [[k] for k in [0] + list(range(2, n_expert)) + [1][:n_expert - 1]]
    blocks = {0: scaled}
    source = scaled
    for wave in waves[1:]:
        k = wave[0]
        blocks[k] = lax.ppermute(source, "expert", _xor_pairs(n_expert, k))
        source, _ = lax.optimization_barrier((scaled, blocks[k]))
    total = None
    previous = None
    for wave in waves:
        piece = jnp.concatenate([blocks[k] for k in wave])
        pair = jnp.concatenate(
            [piece, lax.ppermute(piece, "tensor", _xor_pairs(n_tensor, 2))], axis=1)
        rows = jnp.concatenate(
            [pair, lax.ppermute(pair, "tensor", _xor_pairs(n_tensor, 1))], axis=1)
        if previous is not None:
            rows, _ = lax.optimization_barrier((rows, previous))
        gate_act = jnp.dot(rows, gate_w, preferred_element_type=jnp.float32)
        up_act = jnp.dot(rows, up_w, preferred_element_type=jnp.float32)
        hidden = (jax.nn.silu(gate_act) * up_act).astype(jnp.bfloat16)
        keep = jnp.dot(hidden, down_keep, preferred_element_type=jnp.float32).astype(jnp.bfloat16)
        send = jnp.dot(hidden, down_send, preferred_element_type=jnp.float32).astype(jnp.bfloat16)
        previous = keep
        over_c = keep.astype(jnp.float32) + lax.ppermute(
            send, "tensor", _xor_pairs(n_tensor, 1)).astype(jnp.float32)
        summed = over_c[:, :width] + lax.ppermute(
            over_c[:, width:].astype(jnp.bfloat16), "tensor", _xor_pairs(n_tensor, 2)).astype(jnp.float32)
        for i, k in enumerate(wave):
            part = summed[i * tok_rows:(i + 1) * tok_rows]
            if k:
                part = lax.ppermute(
                    part.astype(jnp.bfloat16), "expert", _xor_pairs(n_expert, k)).astype(jnp.float32)
            part = jnp.where(routed == (me ^ k) // SPAN, part, 0.0)
            total = part if total is None else total + part
    return total.astype(jnp.bfloat16)


def local(tokens, route_scale, expert_ids, gate_weight, up_weight, down_weight):
    tok_rows = tokens.shape[0]
    n_devices = lax.axis_size("expert")
    capacity = min(tok_rows, 2 * tok_rows * SPAN // n_devices)
    n_tensor = lax.axis_size("tensor")
    shaped = n_tensor == 4 and n_devices in (1, 2, 4) and tok_rows <= tokens.shape[1]
    if capacity == tok_rows and shaped:
        return gathered(tokens, route_scale, expert_ids, gate_weight, up_weight, down_weight)
    return dispatched(tokens, route_scale, expert_ids, gate_weight, up_weight, down_weight)


def solution(mesh):
    placed = (
        P(("groups", "expert"), "tensor"),
        P(("groups", "expert")),
        P(("groups", "expert"), None),
        P("expert", None, "tensor"),
        P("expert", None, "tensor"),
        P("expert", "tensor", None),
    )
    return jax.shard_map(
        local,
        mesh=mesh,
        in_specs=placed,
        out_specs=P(("groups", "expert"), "tensor"),
        check_vma=False,
    )
```

```python
import jax
import jax.numpy as jnp
from jax import lax
from jax.sharding import PartitionSpec as P

SPAN = 2


def dispatched(tokens, route_scale, expert_ids, gate_weight, up_weight, down_weight):
    tok_rows = tokens.shape[0]
    n_devices = lax.axis_size("expert")
    experts = n_devices // SPAN
    capacity = min(tok_rows, 2 * tok_rows * SPAN // n_devices)
    routed = expert_ids[:, 0]
    one_hot = (routed[:, None] == jnp.arange(experts, dtype=jnp.int32)[None, :]).astype(jnp.int32)
    slot_rank = jnp.sum((jnp.cumsum(one_hot, axis=0) - one_hot) * one_hot, axis=1)
    flat_slot = routed * capacity + slot_rank
    placing = (
        flat_slot[None, :] == jnp.arange(experts * capacity, dtype=jnp.int32)[:, None]
    ).astype(jnp.bfloat16)
    scaled = (tokens.astype(jnp.float32) * route_scale[:, None]).astype(jnp.bfloat16)
    gate_local = gate_weight[0]
    up_local = up_weight[0]
    down_local = down_weight[0]
    full_rows = lax.all_gather(scaled, "tensor", axis=1, tiled=True)
    width = full_rows.shape[1]
    packed = jnp.dot(placing, full_rows, preferred_element_type=jnp.float32).astype(jnp.bfloat16)
    outgoing = jnp.repeat(packed.reshape(experts, capacity, width), SPAN, axis=0)
    arrived = lax.all_to_all(outgoing, "expert", split_axis=0, concat_axis=0, tiled=True)
    slot_rows = arrived.reshape(n_devices * capacity, width)
    gate_act = jnp.dot(slot_rows, gate_local, preferred_element_type=jnp.float32)
    up_act = jnp.dot(slot_rows, up_local, preferred_element_type=jnp.float32)
    hidden = (jax.nn.silu(gate_act) * up_act).astype(jnp.bfloat16)
    partial_value = jnp.dot(hidden, down_local, preferred_element_type=jnp.float32)
    width = partial_value.shape[1]
    outgoing_back = partial_value.astype(jnp.bfloat16).reshape(n_devices, capacity, width)
    returned = lax.all_to_all(outgoing_back, "expert", split_axis=0, concat_axis=0, tiled=True)
    paired = jnp.sum(returned.astype(jnp.float32).reshape(experts, SPAN, capacity, width), axis=1)
    picked = jnp.take(paired.reshape(experts * capacity, width), flat_slot, axis=0)
    summed = lax.psum_scatter(
        picked.astype(jnp.bfloat16), "tensor", scatter_dimension=1, tiled=True
    )
    return summed


def _xor_pairs(size, k):
    return [(i, i ^ k) for i in range(size)]


_ORDER = (0, 2, 1, 3)


def _slots(weight, t, width, axis, order=_ORDER):
    return jnp.concatenate(
        [lax.dynamic_slice_in_dim(weight, (t ^ k) * width, width, axis=axis) for k in order], axis=axis)


def gathered(tokens, route_scale, expert_ids, gate_weight, up_weight, down_weight):
    tok_rows, width = tokens.shape
    n_expert = lax.axis_size("expert")
    n_tensor = lax.axis_size("tensor")
    me = lax.axis_index("expert")
    t = lax.axis_index("tensor")
    scaled = (tokens.astype(jnp.float32) * route_scale[:, None]).astype(jnp.bfloat16)
    blocks = [scaled] + [
        lax.ppermute(scaled, "expert", _xor_pairs(n_expert, k)) for k in range(1, n_expert)
    ]
    routed = expert_ids[:, 0][:, None]
    gate_w = _slots(gate_weight[0], t, width, 0)
    up_w = _slots(up_weight[0], t, width, 0)
    down_keep = _slots(down_weight[0], t, width, 1, _ORDER[:2])
    down_send = _slots(down_weight[0], t, width, 1, _ORDER[2:])
    waves = [[k] for k in [0] + list(range(2, n_expert)) + [1][:n_expert - 1]]
    total = None
    previous = None
    for wave in waves:
        piece = jnp.concatenate([blocks[k] for k in wave])
        pair = jnp.concatenate(
            [piece, lax.ppermute(piece, "tensor", _xor_pairs(n_tensor, 2))], axis=1)
        rows = jnp.concatenate(
            [pair, lax.ppermute(pair, "tensor", _xor_pairs(n_tensor, 1))], axis=1)
        if previous is not None:
            rows, _ = lax.optimization_barrier((rows, previous))
        gate_act = jnp.dot(rows, gate_w, preferred_element_type=jnp.float32)
        up_act = jnp.dot(rows, up_w, preferred_element_type=jnp.float32)
        hidden = (jax.nn.silu(gate_act) * up_act).astype(jnp.bfloat16)
        keep = jnp.dot(hidden, down_keep, preferred_element_type=jnp.float32).astype(jnp.bfloat16)
        send = jnp.dot(hidden, down_send, preferred_element_type=jnp.float32).astype(jnp.bfloat16)
        previous = keep
        over_c = keep.astype(jnp.float32) + lax.ppermute(
            send, "tensor", _xor_pairs(n_tensor, 1)).astype(jnp.float32)
        k = wave[-1]
        if k and wave is waves[-1] and len(wave) == 1:
            diagonal = [(z * n_tensor + u, (z ^ k) * n_tensor + (u ^ 2))
                        for z in range(n_expert) for u in range(n_tensor)]
            part = lax.ppermute(
                over_c[:, :width].astype(jnp.bfloat16), "expert", _xor_pairs(n_expert, k)).astype(jnp.float32)
            part = part + lax.ppermute(
                over_c[:, width:].astype(jnp.bfloat16), ("expert", "tensor"), diagonal).astype(jnp.float32)
            part = jnp.where(routed == (me ^ k) // SPAN, part, 0.0)
            total = part if total is None else total + part
            continue
        summed = over_c[:, :width] + lax.ppermute(
            over_c[:, width:].astype(jnp.bfloat16), "tensor", _xor_pairs(n_tensor, 2)).astype(jnp.float32)
        for i, k in enumerate(wave):
            part = summed[i * tok_rows:(i + 1) * tok_rows]
            if k:
                part = lax.ppermute(
                    part.astype(jnp.bfloat16), "expert", _xor_pairs(n_expert, k)).astype(jnp.float32)
            part = jnp.where(routed == (me ^ k) // SPAN, part, 0.0)
            total = part if total is None else total + part
    return total.astype(jnp.bfloat16)


def local(tokens, route_scale, expert_ids, gate_weight, up_weight, down_weight):
    tok_rows = tokens.shape[0]
    n_devices = lax.axis_size("expert")
    capacity = min(tok_rows, 2 * tok_rows * SPAN // n_devices)
    n_tensor = lax.axis_size("tensor")
    shaped = n_tensor == 4 and n_devices in (1, 2, 4) and tok_rows <= tokens.shape[1]
    if capacity == tok_rows and shaped:
        return gathered(tokens, route_scale, expert_ids, gate_weight, up_weight, down_weight)
    return dispatched(tokens, route_scale, expert_ids, gate_weight, up_weight, down_weight)


def solution(mesh):
    placed = (
        P(("groups", "expert"), "tensor"),
        P(("groups", "expert")),
        P(("groups", "expert"), None),
        P("expert", None, "tensor"),
        P("expert", None, "tensor"),
        P("expert", "tensor", None),
    )
    return jax.shard_map(
        local,
        mesh=mesh,
        in_specs=placed,
        out_specs=P(("groups", "expert"), "tensor"),
        check_vma=False,
    )
```

```python
import jax
import jax.numpy as jnp
from jax import lax
from jax.sharding import PartitionSpec as P

SPAN = 2


def dispatched(tokens, route_scale, expert_ids, gate_weight, up_weight, down_weight):
    tok_rows = tokens.shape[0]
    n_devices = lax.axis_size("expert")
    experts = n_devices // SPAN
    capacity = min(tok_rows, 2 * tok_rows * SPAN // n_devices)
    routed = expert_ids[:, 0]
    one_hot = (routed[:, None] == jnp.arange(experts, dtype=jnp.int32)[None, :]).astype(jnp.int32)
    slot_rank = jnp.sum((jnp.cumsum(one_hot, axis=0) - one_hot) * one_hot, axis=1)
    flat_slot = routed * capacity + slot_rank
    placing = (
        flat_slot[None, :] == jnp.arange(experts * capacity, dtype=jnp.int32)[:, None]
    ).astype(jnp.bfloat16)
    scaled = (tokens.astype(jnp.float32) * route_scale[:, None]).astype(jnp.bfloat16)
    gate_local = gate_weight[0]
    up_local = up_weight[0]
    down_local = down_weight[0]
    full_rows = lax.all_gather(scaled, "tensor", axis=1, tiled=True)
    width = full_rows.shape[1]
    packed = jnp.dot(placing, full_rows, preferred_element_type=jnp.float32).astype(jnp.bfloat16)
    outgoing = jnp.repeat(packed.reshape(experts, capacity, width), SPAN, axis=0)
    arrived = lax.all_to_all(outgoing, "expert", split_axis=0, concat_axis=0, tiled=True)
    slot_rows = arrived.reshape(n_devices * capacity, width)
    gate_act = jnp.dot(slot_rows, gate_local, preferred_element_type=jnp.float32)
    up_act = jnp.dot(slot_rows, up_local, preferred_element_type=jnp.float32)
    hidden = (jax.nn.silu(gate_act) * up_act).astype(jnp.bfloat16)
    partial_value = jnp.dot(hidden, down_local, preferred_element_type=jnp.float32)
    width = partial_value.shape[1]
    outgoing_back = partial_value.astype(jnp.bfloat16).reshape(n_devices, capacity, width)
    returned = lax.all_to_all(outgoing_back, "expert", split_axis=0, concat_axis=0, tiled=True)
    paired = jnp.sum(returned.astype(jnp.float32).reshape(experts, SPAN, capacity, width), axis=1)
    picked = jnp.take(paired.reshape(experts * capacity, width), flat_slot, axis=0)
    summed = lax.psum_scatter(
        picked.astype(jnp.bfloat16), "tensor", scatter_dimension=1, tiled=True
    )
    return summed


def _xor_pairs(size, k):
    return [(i, i ^ k) for i in range(size)]


_ORDER = (0, 2, 1, 3)


def _slots(weight, t, width, axis, order=_ORDER):
    return jnp.concatenate(
        [lax.dynamic_slice_in_dim(weight, (t ^ k) * width, width, axis=axis) for k in order], axis=axis)


def gathered(tokens, route_scale, expert_ids, gate_weight, up_weight, down_weight):
    tok_rows, width = tokens.shape
    n_expert = lax.axis_size("expert")
    n_tensor = lax.axis_size("tensor")
    me = lax.axis_index("expert")
    t = lax.axis_index("tensor")
    scaled = (tokens.astype(jnp.float32) * route_scale[:, None]).astype(jnp.bfloat16)
    blocks = [scaled] + [
        lax.ppermute(scaled, "expert", _xor_pairs(n_expert, k)) for k in range(1, n_expert)
    ]
    routed = expert_ids[:, 0][:, None]
    gate_w = _slots(gate_weight[0], t, width, 0)
    up_w = _slots(up_weight[0], t, width, 0)
    down_keep = _slots(down_weight[0], t, width, 1, _ORDER[:2])
    down_send = _slots(down_weight[0], t, width, 1, _ORDER[2:])
    waves = [[k] for k in [0] + list(range(2, n_expert)) + [1][:n_expert - 1]]
    total = None
    previous = None
    for wave in waves:
        piece = jnp.concatenate([blocks[k] for k in wave])
        pair = jnp.concatenate(
            [piece, lax.ppermute(piece, "tensor", _xor_pairs(n_tensor, 2))], axis=1)
        rows = jnp.concatenate(
            [pair, lax.ppermute(pair, "tensor", _xor_pairs(n_tensor, 1))], axis=1)
        if previous is not None:
            rows, _ = lax.optimization_barrier((rows, previous))
        gate_act = jnp.dot(rows, gate_w, preferred_element_type=jnp.float32)
        up_act = jnp.dot(rows, up_w, preferred_element_type=jnp.float32)
        hidden = (jax.nn.silu(gate_act) * up_act).astype(jnp.bfloat16)
        keep = jnp.dot(hidden, down_keep, preferred_element_type=jnp.float32).astype(jnp.bfloat16)
        send = jnp.dot(hidden, down_send, preferred_element_type=jnp.float32).astype(jnp.bfloat16)
        previous = keep
        if wave is waves[0] and len(waves) > 1:
            others, _ = lax.optimization_barrier(([blocks[k] for k in range(1, n_expert)], keep))
            blocks = [blocks[0]] + others
        over_c = keep.astype(jnp.float32) + lax.ppermute(
            send, "tensor", _xor_pairs(n_tensor, 1)).astype(jnp.float32)
        summed = over_c[:, :width] + lax.ppermute(
            over_c[:, width:].astype(jnp.bfloat16), "tensor", _xor_pairs(n_tensor, 2)).astype(jnp.float32)
        for i, k in enumerate(wave):
            part = summed[i * tok_rows:(i + 1) * tok_rows]
            if k:
                part = lax.ppermute(
                    part.astype(jnp.bfloat16), "expert", _xor_pairs(n_expert, k)).astype(jnp.float32)
            part = jnp.where(routed == (me ^ k) // SPAN, part, 0.0)
            total = part if total is None else total + part
    return total.astype(jnp.bfloat16)


def local(tokens, route_scale, expert_ids, gate_weight, up_weight, down_weight):
    tok_rows = tokens.shape[0]
    n_devices = lax.axis_size("expert")
    capacity = min(tok_rows, 2 * tok_rows * SPAN // n_devices)
    n_tensor = lax.axis_size("tensor")
    shaped = n_tensor == 4 and n_devices in (1, 2, 4) and tok_rows <= tokens.shape[1]
    if capacity == tok_rows and shaped:
        return gathered(tokens, route_scale, expert_ids, gate_weight, up_weight, down_weight)
    return dispatched(tokens, route_scale, expert_ids, gate_weight, up_weight, down_weight)


def solution(mesh):
    placed = (
        P(("groups", "expert"), "tensor"),
        P(("groups", "expert")),
        P(("groups", "expert"), None),
        P("expert", None, "tensor"),
        P("expert", None, "tensor"),
        P("expert", "tensor", None),
    )
    return jax.shard_map(
        local,
        mesh=mesh,
        in_specs=placed,
        out_specs=P(("groups", "expert"), "tensor"),
        check_vma=False,
    )
```

```python
import jax
import jax.numpy as jnp
from jax import lax
from jax.sharding import PartitionSpec as P

SPAN = 2


def dispatched(tokens, route_scale, expert_ids, gate_weight, up_weight, down_weight):
    tok_rows = tokens.shape[0]
    n_devices = lax.axis_size("expert")
    experts = n_devices // SPAN
    capacity = min(tok_rows, 2 * tok_rows * SPAN // n_devices)
    routed = expert_ids[:, 0]
    one_hot = (routed[:, None] == jnp.arange(experts, dtype=jnp.int32)[None, :]).astype(jnp.int32)
    slot_rank = jnp.sum((jnp.cumsum(one_hot, axis=0) - one_hot) * one_hot, axis=1)
    flat_slot = routed * capacity + slot_rank
    placing = (
        flat_slot[None, :] == jnp.arange(experts * capacity, dtype=jnp.int32)[:, None]
    ).astype(jnp.bfloat16)
    scaled = (tokens.astype(jnp.float32) * route_scale[:, None]).astype(jnp.bfloat16)
    gate_local = gate_weight[0]
    up_local = up_weight[0]
    down_local = down_weight[0]
    full_rows = lax.all_gather(scaled, "tensor", axis=1, tiled=True)
    width = full_rows.shape[1]
    packed = jnp.dot(placing, full_rows, preferred_element_type=jnp.float32).astype(jnp.bfloat16)
    outgoing = jnp.repeat(packed.reshape(experts, capacity, width), SPAN, axis=0)
    arrived = lax.all_to_all(outgoing, "expert", split_axis=0, concat_axis=0, tiled=True)
    slot_rows = arrived.reshape(n_devices * capacity, width)
    gate_act = jnp.dot(slot_rows, gate_local, preferred_element_type=jnp.float32)
    up_act = jnp.dot(slot_rows, up_local, preferred_element_type=jnp.float32)
    hidden = (jax.nn.silu(gate_act) * up_act).astype(jnp.bfloat16)
    partial_value = jnp.dot(hidden, down_local, preferred_element_type=jnp.float32)
    width = partial_value.shape[1]
    outgoing_back = partial_value.astype(jnp.bfloat16).reshape(n_devices, capacity, width)
    returned = lax.all_to_all(outgoing_back, "expert", split_axis=0, concat_axis=0, tiled=True)
    paired = jnp.sum(returned.astype(jnp.float32).reshape(experts, SPAN, capacity, width), axis=1)
    picked = jnp.take(paired.reshape(experts * capacity, width), flat_slot, axis=0)
    summed = lax.psum_scatter(
        picked.astype(jnp.bfloat16), "tensor", scatter_dimension=1, tiled=True
    )
    return summed


def _xor_pairs(size, k):
    return [(i, i ^ k) for i in range(size)]


_ORDER = (0, 2, 1, 3)


def _slots(weight, t, width, axis, order=_ORDER):
    return jnp.concatenate(
        [lax.dynamic_slice_in_dim(weight, (t ^ k) * width, width, axis=axis) for k in order], axis=axis)


def gathered(tokens, route_scale, expert_ids, gate_weight, up_weight, down_weight):
    tok_rows, width = tokens.shape
    n_expert = lax.axis_size("expert")
    n_tensor = lax.axis_size("tensor")
    me = lax.axis_index("expert")
    t = lax.axis_index("tensor")
    scaled = (tokens.astype(jnp.float32) * route_scale[:, None]).astype(jnp.bfloat16)
    blocks = [scaled] + [
        lax.ppermute(scaled, "expert", _xor_pairs(n_expert, k)) for k in range(1, n_expert)
    ]
    routed = expert_ids[:, 0][:, None]
    gate_w = _slots(gate_weight[0], t, width, 0)
    up_w = _slots(up_weight[0], t, width, 0)
    down_keep = _slots(down_weight[0], t, width, 1, _ORDER[:2])
    down_send = _slots(down_weight[0], t, width, 1, _ORDER[2:])
    waves = [[0], list(range(2, n_expert)), [1][:n_expert - 1]]
    waves = [wave for wave in waves if wave]
    total = None
    previous = None
    for wave in waves:
        piece = jnp.concatenate([blocks[k] for k in wave])
        pair = jnp.concatenate(
            [piece, lax.ppermute(piece, "tensor", _xor_pairs(n_tensor, 2))], axis=1)
        rows = jnp.concatenate(
            [pair, lax.ppermute(pair, "tensor", _xor_pairs(n_tensor, 1))], axis=1)
        if previous is not None:
            rows, _ = lax.optimization_barrier((rows, previous))
        gate_act = jnp.dot(rows, gate_w, preferred_element_type=jnp.float32)
        up_act = jnp.dot(rows, up_w, preferred_element_type=jnp.float32)
        hidden = (jax.nn.silu(gate_act) * up_act).astype(jnp.bfloat16)
        keep = jnp.dot(hidden, down_keep, preferred_element_type=jnp.float32).astype(jnp.bfloat16)
        send = jnp.dot(hidden, down_send, preferred_element_type=jnp.float32).astype(jnp.bfloat16)
        previous = keep
        over_c = keep.astype(jnp.float32) + lax.ppermute(
            send, "tensor", _xor_pairs(n_tensor, 1)).astype(jnp.float32)
        summed = over_c[:, :width] + lax.ppermute(
            over_c[:, width:].astype(jnp.bfloat16), "tensor", _xor_pairs(n_tensor, 2)).astype(jnp.float32)
        for i, k in enumerate(wave):
            part = summed[i * tok_rows:(i + 1) * tok_rows]
            if k:
                part = lax.ppermute(
                    part.astype(jnp.bfloat16), "expert", _xor_pairs(n_expert, k)).astype(jnp.float32)
            part = jnp.where(routed == (me ^ k) // SPAN, part, 0.0)
            total = part if total is None else total + part
    return total.astype(jnp.bfloat16)


def local(tokens, route_scale, expert_ids, gate_weight, up_weight, down_weight):
    tok_rows = tokens.shape[0]
    n_devices = lax.axis_size("expert")
    capacity = min(tok_rows, 2 * tok_rows * SPAN // n_devices)
    n_tensor = lax.axis_size("tensor")
    shaped = n_tensor == 4 and n_devices in (1, 2, 4) and tok_rows <= tokens.shape[1]
    if capacity == tok_rows and shaped:
        return gathered(tokens, route_scale, expert_ids, gate_weight, up_weight, down_weight)
    return dispatched(tokens, route_scale, expert_ids, gate_weight, up_weight, down_weight)


def solution(mesh):
    placed = (
        P(("groups", "expert"), "tensor"),
        P(("groups", "expert")),
        P(("groups", "expert"), None),
        P("expert", None, "tensor"),
        P("expert", None, "tensor"),
        P("expert", "tensor", None),
    )
    return jax.shard_map(
        local,
        mesh=mesh,
        in_specs=placed,
        out_specs=P(("groups", "expert"), "tensor"),
        check_vma=False,
    )
```

```python
import jax
import jax.numpy as jnp
from jax import lax
from jax.sharding import PartitionSpec as P

SPAN = 2


def dispatched(tokens, route_scale, expert_ids, gate_weight, up_weight, down_weight):
    tok_rows = tokens.shape[0]
    n_devices = lax.axis_size("expert")
    experts = n_devices // SPAN
    capacity = min(tok_rows, 2 * tok_rows * SPAN // n_devices)
    routed = expert_ids[:, 0]
    one_hot = (routed[:, None] == jnp.arange(experts, dtype=jnp.int32)[None, :]).astype(jnp.int32)
    slot_rank = jnp.sum((jnp.cumsum(one_hot, axis=0) - one_hot) * one_hot, axis=1)
    flat_slot = routed * capacity + slot_rank
    placing = (
        flat_slot[None, :] == jnp.arange(experts * capacity, dtype=jnp.int32)[:, None]
    ).astype(jnp.bfloat16)
    scaled = (tokens.astype(jnp.float32) * route_scale[:, None]).astype(jnp.bfloat16)
    gate_local = gate_weight[0]
    up_local = up_weight[0]
    down_local = down_weight[0]
    full_rows = lax.all_gather(scaled, "tensor", axis=1, tiled=True)
    width = full_rows.shape[1]
    packed = jnp.dot(placing, full_rows, preferred_element_type=jnp.float32).astype(jnp.bfloat16)
    outgoing = jnp.repeat(packed.reshape(experts, capacity, width), SPAN, axis=0)
    arrived = lax.all_to_all(outgoing, "expert", split_axis=0, concat_axis=0, tiled=True)
    slot_rows = arrived.reshape(n_devices * capacity, width)
    gate_act = jnp.dot(slot_rows, gate_local, preferred_element_type=jnp.float32)
    up_act = jnp.dot(slot_rows, up_local, preferred_element_type=jnp.float32)
    hidden = (jax.nn.silu(gate_act) * up_act).astype(jnp.bfloat16)
    partial_value = jnp.dot(hidden, down_local, preferred_element_type=jnp.float32)
    width = partial_value.shape[1]
    outgoing_back = partial_value.astype(jnp.bfloat16).reshape(n_devices, capacity, width)
    returned = lax.all_to_all(outgoing_back, "expert", split_axis=0, concat_axis=0, tiled=True)
    paired = jnp.sum(returned.astype(jnp.float32).reshape(experts, SPAN, capacity, width), axis=1)
    picked = jnp.take(paired.reshape(experts * capacity, width), flat_slot, axis=0)
    summed = lax.psum_scatter(
        picked.astype(jnp.bfloat16), "tensor", scatter_dimension=1, tiled=True
    )
    return summed


def _xor_pairs(size, k):
    return [(i, i ^ k) for i in range(size)]


_ORDER = (0, 2, 1, 3)


def _slots(weight, t, width, axis, order=_ORDER):
    return jnp.concatenate(
        [lax.dynamic_slice_in_dim(weight, (t ^ k) * width, width, axis=axis) for k in order], axis=axis)


def gathered(tokens, route_scale, expert_ids, gate_weight, up_weight, down_weight):
    tok_rows, width = tokens.shape
    n_expert = lax.axis_size("expert")
    n_tensor = lax.axis_size("tensor")
    me = lax.axis_index("expert")
    t = lax.axis_index("tensor")
    scaled = (tokens.astype(jnp.float32) * route_scale[:, None]).astype(jnp.bfloat16)
    blocks = [scaled] + [
        lax.ppermute(scaled, "expert", _xor_pairs(n_expert, k)) for k in range(1, n_expert)
    ]
    routed = expert_ids[:, 0][:, None]
    gate_w = _slots(gate_weight[0], t, width, 0)
    up_w = _slots(up_weight[0], t, width, 0)
    down_keep = _slots(down_weight[0], t, width, 1, _ORDER[:2])
    down_send = _slots(down_weight[0], t, width, 1, _ORDER[2:])
    halves = 2 if tok_rows % 32 == 0 else 1
    rows_h = tok_rows // halves
    order = [0] + list(range(2, n_expert)) + [1][:n_expert - 1]
    waves = [(k, h) for k in order for h in range(halves)]
    totals = [None] * halves
    previous = None
    for k, h in waves:
        piece = blocks[k][h * rows_h:(h + 1) * rows_h]
        pair = jnp.concatenate(
            [piece, lax.ppermute(piece, "tensor", _xor_pairs(n_tensor, 2))], axis=1)
        rows = jnp.concatenate(
            [pair, lax.ppermute(pair, "tensor", _xor_pairs(n_tensor, 1))], axis=1)
        if previous is not None:
            rows, _ = lax.optimization_barrier((rows, previous))
        gate_act = jnp.dot(rows, gate_w, preferred_element_type=jnp.float32)
        up_act = jnp.dot(rows, up_w, preferred_element_type=jnp.float32)
        hidden = (jax.nn.silu(gate_act) * up_act).astype(jnp.bfloat16)
        keep = jnp.dot(hidden, down_keep, preferred_element_type=jnp.float32).astype(jnp.bfloat16)
        send = jnp.dot(hidden, down_send, preferred_element_type=jnp.float32).astype(jnp.bfloat16)
        previous = keep
        over_c = keep.astype(jnp.float32) + lax.ppermute(
            send, "tensor", _xor_pairs(n_tensor, 1)).astype(jnp.float32)
        part = over_c[:, :width] + lax.ppermute(
            over_c[:, width:].astype(jnp.bfloat16), "tensor", _xor_pairs(n_tensor, 2)).astype(jnp.float32)
        if k:
            part = lax.ppermute(
                part.astype(jnp.bfloat16), "expert", _xor_pairs(n_expert, k)).astype(jnp.float32)
        part = jnp.where(routed[h * rows_h:(h + 1) * rows_h] == (me ^ k) // SPAN, part, 0.0)
        totals[h] = part if totals[h] is None else totals[h] + part
    total = jnp.concatenate(totals, axis=0)
    return total.astype(jnp.bfloat16)


def local(tokens, route_scale, expert_ids, gate_weight, up_weight, down_weight):
    tok_rows = tokens.shape[0]
    n_devices = lax.axis_size("expert")
    capacity = min(tok_rows, 2 * tok_rows * SPAN // n_devices)
    n_tensor = lax.axis_size("tensor")
    shaped = n_tensor == 4 and n_devices in (1, 2, 4) and tok_rows <= tokens.shape[1]
    if capacity == tok_rows and shaped:
        return gathered(tokens, route_scale, expert_ids, gate_weight, up_weight, down_weight)
    return dispatched(tokens, route_scale, expert_ids, gate_weight, up_weight, down_weight)


def solution(mesh):
    placed = (
        P(("groups", "expert"), "tensor"),
        P(("groups", "expert")),
        P(("groups", "expert"), None),
        P("expert", None, "tensor"),
        P("expert", None, "tensor"),
        P("expert", "tensor", None),
    )
    return jax.shard_map(
        local,
        mesh=mesh,
        in_specs=placed,
        out_specs=P(("groups", "expert"), "tensor"),
        check_vma=False,
    )
```

```python
import jax
import jax.numpy as jnp
from jax import lax
from jax.sharding import PartitionSpec as P

SPAN = 2


def dispatched(tokens, route_scale, expert_ids, gate_weight, up_weight, down_weight):
    tok_rows = tokens.shape[0]
    n_devices = lax.axis_size("expert")
    experts = n_devices // SPAN
    capacity = min(tok_rows, 2 * tok_rows * SPAN // n_devices)
    routed = expert_ids[:, 0]
    one_hot = (routed[:, None] == jnp.arange(experts, dtype=jnp.int32)[None, :]).astype(jnp.int32)
    slot_rank = jnp.sum((jnp.cumsum(one_hot, axis=0) - one_hot) * one_hot, axis=1)
    flat_slot = routed * capacity + slot_rank
    placing = (
        flat_slot[None, :] == jnp.arange(experts * capacity, dtype=jnp.int32)[:, None]
    ).astype(jnp.bfloat16)
    scaled = (tokens.astype(jnp.float32) * route_scale[:, None]).astype(jnp.bfloat16)
    gate_local = gate_weight[0]
    up_local = up_weight[0]
    down_local = down_weight[0]
    full_rows = lax.all_gather(scaled, "tensor", axis=1, tiled=True)
    width = full_rows.shape[1]
    packed = jnp.dot(placing, full_rows, preferred_element_type=jnp.float32).astype(jnp.bfloat16)
    outgoing = jnp.repeat(packed.reshape(experts, capacity, width), SPAN, axis=0)
    arrived = lax.all_to_all(outgoing, "expert", split_axis=0, concat_axis=0, tiled=True)
    slot_rows = arrived.reshape(n_devices * capacity, width)
    gate_act = jnp.dot(slot_rows, gate_local, preferred_element_type=jnp.float32)
    up_act = jnp.dot(slot_rows, up_local, preferred_element_type=jnp.float32)
    hidden = (jax.nn.silu(gate_act) * up_act).astype(jnp.bfloat16)
    partial_value = jnp.dot(hidden, down_local, preferred_element_type=jnp.float32)
    width = partial_value.shape[1]
    outgoing_back = partial_value.astype(jnp.bfloat16).reshape(n_devices, capacity, width)
    returned = lax.all_to_all(outgoing_back, "expert", split_axis=0, concat_axis=0, tiled=True)
    paired = jnp.sum(returned.astype(jnp.float32).reshape(experts, SPAN, capacity, width), axis=1)
    picked = jnp.take(paired.reshape(experts * capacity, width), flat_slot, axis=0)
    summed = lax.psum_scatter(
        picked.astype(jnp.bfloat16), "tensor", scatter_dimension=1, tiled=True
    )
    return summed


def _xor_pairs(size, k):
    return [(i, i ^ k) for i in range(size)]


_ORDER = (0, 2, 1, 3)


def _slots(weight, t, width, axis, order=_ORDER):
    return jnp.concatenate(
        [lax.dynamic_slice_in_dim(weight, (t ^ k) * width, width, axis=axis) for k in order], axis=axis)


def gathered(tokens, route_scale, expert_ids, gate_weight, up_weight, down_weight):
    tok_rows, width = tokens.shape
    n_expert = lax.axis_size("expert")
    n_tensor = lax.axis_size("tensor")
    me = lax.axis_index("expert")
    t = lax.axis_index("tensor")
    scaled = (tokens.astype(jnp.float32) * route_scale[:, None]).astype(jnp.bfloat16)
    routed = expert_ids[:, 0][:, None]
    gate_w = _slots(gate_weight[0], t, width, 0)
    up_w = _slots(up_weight[0], t, width, 0)
    down_keep = _slots(down_weight[0], t, width, 1, _ORDER[:2])
    down_send = _slots(down_weight[0], t, width, 1, _ORDER[2:])
    waves = [[k] for k in [0] + list(range(2, n_expert)) + [1][:n_expert - 1]]
    total = None
    previous = None
    for wave in waves:
        piece = jnp.concatenate([
            lax.ppermute(scaled, "expert", _xor_pairs(n_expert, k)) if k else scaled for k in wave])
        pair = jnp.concatenate(
            [piece, lax.ppermute(piece, "tensor", _xor_pairs(n_tensor, 2))], axis=1)
        rows = jnp.concatenate(
            [pair, lax.ppermute(pair, "tensor", _xor_pairs(n_tensor, 1))], axis=1)
        if previous is not None:
            rows, _ = lax.optimization_barrier((rows, previous))
        gate_act = jnp.dot(rows, gate_w, preferred_element_type=jnp.float32)
        up_act = jnp.dot(rows, up_w, preferred_element_type=jnp.float32)
        hidden = (jax.nn.silu(gate_act) * up_act).astype(jnp.bfloat16)
        keep = jnp.dot(hidden, down_keep, preferred_element_type=jnp.float32).astype(jnp.bfloat16)
        send = jnp.dot(hidden, down_send, preferred_element_type=jnp.float32).astype(jnp.bfloat16)
        previous = keep
        over_c = keep.astype(jnp.float32) + lax.ppermute(
            send, "tensor", _xor_pairs(n_tensor, 1)).astype(jnp.float32)
        summed = over_c[:, :width] + lax.ppermute(
            over_c[:, width:].astype(jnp.bfloat16), "tensor", _xor_pairs(n_tensor, 2)).astype(jnp.float32)
        for i, k in enumerate(wave):
            part = summed[i * tok_rows:(i + 1) * tok_rows]
            if k:
                part = lax.ppermute(
                    part.astype(jnp.bfloat16), "expert", _xor_pairs(n_expert, k)).astype(jnp.float32)
            part = jnp.where(routed == (me ^ k) // SPAN, part, 0.0)
            total = part if total is None else total + part
    return total.astype(jnp.bfloat16)


def local(tokens, route_scale, expert_ids, gate_weight, up_weight, down_weight):
    tok_rows = tokens.shape[0]
    n_devices = lax.axis_size("expert")
    capacity = min(tok_rows, 2 * tok_rows * SPAN // n_devices)
    n_tensor = lax.axis_size("tensor")
    shaped = n_tensor == 4 and n_devices in (1, 2, 4) and tok_rows <= tokens.shape[1]
    if capacity == tok_rows and shaped:
        return gathered(tokens, route_scale, expert_ids, gate_weight, up_weight, down_weight)
    return dispatched(tokens, route_scale, expert_ids, gate_weight, up_weight, down_weight)


def solution(mesh):
    placed = (
        P(("groups", "expert"), "tensor"),
        P(("groups", "expert")),
        P(("groups", "expert"), None),
        P("expert", None, "tensor"),
        P("expert", None, "tensor"),
        P("expert", "tensor", None),
    )
    return jax.shard_map(
        local,
        mesh=mesh,
        in_specs=placed,
        out_specs=P(("groups", "expert"), "tensor"),
        check_vma=False,
    )
```

```python
import jax
import jax.numpy as jnp
from jax import lax
from jax.sharding import PartitionSpec as P

SPAN = 2


def dispatched(tokens, route_scale, expert_ids, gate_weight, up_weight, down_weight):
    tok_rows = tokens.shape[0]
    n_devices = lax.axis_size("expert")
    experts = n_devices // SPAN
    capacity = min(tok_rows, 2 * tok_rows * SPAN // n_devices)
    routed = expert_ids[:, 0]
    one_hot = (routed[:, None] == jnp.arange(experts, dtype=jnp.int32)[None, :]).astype(jnp.int32)
    slot_rank = jnp.sum((jnp.cumsum(one_hot, axis=0) - one_hot) * one_hot, axis=1)
    flat_slot = routed * capacity + slot_rank
    placing = (
        flat_slot[None, :] == jnp.arange(experts * capacity, dtype=jnp.int32)[:, None]
    ).astype(jnp.bfloat16)
    scaled = (tokens.astype(jnp.float32) * route_scale[:, None]).astype(jnp.bfloat16)
    gate_local = gate_weight[0]
    up_local = up_weight[0]
    down_local = down_weight[0]
    full_rows = lax.all_gather(scaled, "tensor", axis=1, tiled=True)
    width = full_rows.shape[1]
    packed = jnp.dot(placing, full_rows, preferred_element_type=jnp.float32).astype(jnp.bfloat16)
    outgoing = jnp.repeat(packed.reshape(experts, capacity, width), SPAN, axis=0)
    arrived = lax.all_to_all(outgoing, "expert", split_axis=0, concat_axis=0, tiled=True)
    slot_rows = arrived.reshape(n_devices * capacity, width)
    gate_act = jnp.dot(slot_rows, gate_local, preferred_element_type=jnp.float32)
    up_act = jnp.dot(slot_rows, up_local, preferred_element_type=jnp.float32)
    hidden = (jax.nn.silu(gate_act) * up_act).astype(jnp.bfloat16)
    partial_value = jnp.dot(hidden, down_local, preferred_element_type=jnp.float32)
    width = partial_value.shape[1]
    outgoing_back = partial_value.astype(jnp.bfloat16).reshape(n_devices, capacity, width)
    returned = lax.all_to_all(outgoing_back, "expert", split_axis=0, concat_axis=0, tiled=True)
    paired = jnp.sum(returned.astype(jnp.float32).reshape(experts, SPAN, capacity, width), axis=1)
    picked = jnp.take(paired.reshape(experts * capacity, width), flat_slot, axis=0)
    summed = lax.psum_scatter(
        picked.astype(jnp.bfloat16), "tensor", scatter_dimension=1, tiled=True
    )
    return summed


def _xor_pairs(size, k):
    return [(i, i ^ k) for i in range(size)]


_ORDER = (0, 2, 1, 3)


def _slots(weight, t, width, axis, order=_ORDER):
    return jnp.concatenate(
        [lax.dynamic_slice_in_dim(weight, (t ^ k) * width, width, axis=axis) for k in order], axis=axis)


def gathered(tokens, route_scale, expert_ids, gate_weight, up_weight, down_weight):
    tok_rows, width = tokens.shape
    n_expert = lax.axis_size("expert")
    n_tensor = lax.axis_size("tensor")
    me = lax.axis_index("expert")
    t = lax.axis_index("tensor")
    scaled = (tokens.astype(jnp.float32) * route_scale[:, None]).astype(jnp.bfloat16)
    blocks = [scaled] + [
        lax.ppermute(scaled, "expert", _xor_pairs(n_expert, k)) for k in range(1, n_expert)
    ]
    routed = expert_ids[:, 0][:, None]
    gate_w = _slots(gate_weight[0], t, width, 0)
    up_w = _slots(up_weight[0], t, width, 0)
    down_keep = _slots(down_weight[0], t, width, 1, _ORDER[:2])
    down_send = _slots(down_weight[0], t, width, 1, _ORDER[2:])
    waves = [[k] for k in [0] + list(range(2, n_expert)) + [1][:n_expert - 1]]
    total = None
    previous = None
    def full_rows(piece):
        pair = jnp.concatenate(
            [piece, lax.ppermute(piece, "tensor", _xor_pairs(n_tensor, 2))], axis=1)
        return jnp.concatenate(
            [pair, lax.ppermute(pair, "tensor", _xor_pairs(n_tensor, 1))], axis=1)

    wave_rows = [full_rows(blocks[0])]
    if len(waves) > 1:
        rest = full_rows(jnp.concatenate([blocks[wave[0]] for wave in waves[1:]]))
        wave_rows += [rest[i * tok_rows:(i + 1) * tok_rows] for i in range(len(waves) - 1)]
    for wave, rows in zip(waves, wave_rows):
        if previous is not None:
            rows, _ = lax.optimization_barrier((rows, previous))
        gate_act = jnp.dot(rows, gate_w, preferred_element_type=jnp.float32)
        up_act = jnp.dot(rows, up_w, preferred_element_type=jnp.float32)
        hidden = (jax.nn.silu(gate_act) * up_act).astype(jnp.bfloat16)
        keep = jnp.dot(hidden, down_keep, preferred_element_type=jnp.float32).astype(jnp.bfloat16)
        send = jnp.dot(hidden, down_send, preferred_element_type=jnp.float32).astype(jnp.bfloat16)
        previous = keep
        over_c = keep.astype(jnp.float32) + lax.ppermute(
            send, "tensor", _xor_pairs(n_tensor, 1)).astype(jnp.float32)
        summed = over_c[:, :width] + lax.ppermute(
            over_c[:, width:].astype(jnp.bfloat16), "tensor", _xor_pairs(n_tensor, 2)).astype(jnp.float32)
        for i, k in enumerate(wave):
            part = summed[i * tok_rows:(i + 1) * tok_rows]
            if k:
                part = lax.ppermute(
                    part.astype(jnp.bfloat16), "expert", _xor_pairs(n_expert, k)).astype(jnp.float32)
            part = jnp.where(routed == (me ^ k) // SPAN, part, 0.0)
            total = part if total is None else total + part
    return total.astype(jnp.bfloat16)


def local(tokens, route_scale, expert_ids, gate_weight, up_weight, down_weight):
    tok_rows = tokens.shape[0]
    n_devices = lax.axis_size("expert")
    capacity = min(tok_rows, 2 * tok_rows * SPAN // n_devices)
    n_tensor = lax.axis_size("tensor")
    shaped = n_tensor == 4 and n_devices in (1, 2, 4) and tok_rows <= tokens.shape[1]
    if capacity == tok_rows and shaped:
        return gathered(tokens, route_scale, expert_ids, gate_weight, up_weight, down_weight)
    return dispatched(tokens, route_scale, expert_ids, gate_weight, up_weight, down_weight)


def solution(mesh):
    placed = (
        P(("groups", "expert"), "tensor"),
        P(("groups", "expert")),
        P(("groups", "expert"), None),
        P("expert", None, "tensor"),
        P("expert", None, "tensor"),
        P("expert", "tensor", None),
    )
    return jax.shard_map(
        local,
        mesh=mesh,
        in_specs=placed,
        out_specs=P(("groups", "expert"), "tensor"),
        check_vma=False,
    )
```

```python
import jax
import jax.numpy as jnp
from jax import lax
from jax.sharding import PartitionSpec as P

SPAN = 2


def dispatched(tokens, route_scale, expert_ids, gate_weight, up_weight, down_weight):
    tok_rows = tokens.shape[0]
    n_devices = lax.axis_size("expert")
    experts = n_devices // SPAN
    capacity = min(tok_rows, 2 * tok_rows * SPAN // n_devices)
    routed = expert_ids[:, 0]
    one_hot = (routed[:, None] == jnp.arange(experts, dtype=jnp.int32)[None, :]).astype(jnp.int32)
    slot_rank = jnp.sum((jnp.cumsum(one_hot, axis=0) - one_hot) * one_hot, axis=1)
    flat_slot = routed * capacity + slot_rank
    placing = (
        flat_slot[None, :] == jnp.arange(experts * capacity, dtype=jnp.int32)[:, None]
    ).astype(jnp.bfloat16)
    scaled = (tokens.astype(jnp.float32) * route_scale[:, None]).astype(jnp.bfloat16)
    gate_local = gate_weight[0]
    up_local = up_weight[0]
    down_local = down_weight[0]
    full_rows = lax.all_gather(scaled, "tensor", axis=1, tiled=True)
    width = full_rows.shape[1]
    packed = jnp.dot(placing, full_rows, preferred_element_type=jnp.float32).astype(jnp.bfloat16)
    outgoing = jnp.repeat(packed.reshape(experts, capacity, width), SPAN, axis=0)
    arrived = lax.all_to_all(outgoing, "expert", split_axis=0, concat_axis=0, tiled=True)
    slot_rows = arrived.reshape(n_devices * capacity, width)
    gate_act = jnp.dot(slot_rows, gate_local, preferred_element_type=jnp.float32)
    up_act = jnp.dot(slot_rows, up_local, preferred_element_type=jnp.float32)
    hidden = (jax.nn.silu(gate_act) * up_act).astype(jnp.bfloat16)
    partial_value = jnp.dot(hidden, down_local, preferred_element_type=jnp.float32)
    width = partial_value.shape[1]
    outgoing_back = partial_value.astype(jnp.bfloat16).reshape(n_devices, capacity, width)
    returned = lax.all_to_all(outgoing_back, "expert", split_axis=0, concat_axis=0, tiled=True)
    paired = jnp.sum(returned.astype(jnp.float32).reshape(experts, SPAN, capacity, width), axis=1)
    picked = jnp.take(paired.reshape(experts * capacity, width), flat_slot, axis=0)
    summed = lax.psum_scatter(
        picked.astype(jnp.bfloat16), "tensor", scatter_dimension=1, tiled=True
    )
    return summed


def _xor_pairs(size, k):
    return [(i, i ^ k) for i in range(size)]


_ORDER = (0, 2, 1, 3)


def _slots(weight, t, width, axis, order=_ORDER):
    return jnp.concatenate(
        [lax.dynamic_slice_in_dim(weight, (t ^ k) * width, width, axis=axis) for k in order], axis=axis)


def gathered(tokens, route_scale, expert_ids, gate_weight, up_weight, down_weight):
    tok_rows, width = tokens.shape
    n_expert = lax.axis_size("expert")
    n_tensor = lax.axis_size("tensor")
    me = lax.axis_index("expert")
    t = lax.axis_index("tensor")
    scaled = (tokens.astype(jnp.float32) * route_scale[:, None]).astype(jnp.bfloat16)
    blocks = [scaled] + [
        lax.ppermute(scaled, "expert", _xor_pairs(n_expert, k)) for k in range(1, n_expert)
    ]
    routed = expert_ids[:, 0][:, None]
    gate_w = _slots(gate_weight[0], t, width, 0)
    up_w = _slots(up_weight[0], t, width, 0)
    down_keep = _slots(down_weight[0], t, width, 1, _ORDER[:2])
    down_send = _slots(down_weight[0], t, width, 1, _ORDER[2:])
    waves = [[k] for k in list(range(2, n_expert)) + [1][:n_expert - 1] + [0]]
    total = None
    previous = None
    for wave in waves:
        piece = jnp.concatenate([blocks[k] for k in wave])
        pair = jnp.concatenate(
            [piece, lax.ppermute(piece, "tensor", _xor_pairs(n_tensor, 2))], axis=1)
        rows = jnp.concatenate(
            [pair, lax.ppermute(pair, "tensor", _xor_pairs(n_tensor, 1))], axis=1)
        if previous is not None:
            rows, _ = lax.optimization_barrier((rows, previous))
        gate_act = jnp.dot(rows, gate_w, preferred_element_type=jnp.float32)
        up_act = jnp.dot(rows, up_w, preferred_element_type=jnp.float32)
        hidden = (jax.nn.silu(gate_act) * up_act).astype(jnp.bfloat16)
        keep = jnp.dot(hidden, down_keep, preferred_element_type=jnp.float32).astype(jnp.bfloat16)
        send = jnp.dot(hidden, down_send, preferred_element_type=jnp.float32).astype(jnp.bfloat16)
        previous = keep
        over_c = keep.astype(jnp.float32) + lax.ppermute(
            send, "tensor", _xor_pairs(n_tensor, 1)).astype(jnp.float32)
        summed = over_c[:, :width] + lax.ppermute(
            over_c[:, width:].astype(jnp.bfloat16), "tensor", _xor_pairs(n_tensor, 2)).astype(jnp.float32)
        for i, k in enumerate(wave):
            part = summed[i * tok_rows:(i + 1) * tok_rows]
            if k:
                part = lax.ppermute(
                    part.astype(jnp.bfloat16), "expert", _xor_pairs(n_expert, k)).astype(jnp.float32)
            part = jnp.where(routed == (me ^ k) // SPAN, part, 0.0)
            total = part if total is None else total + part
    return total.astype(jnp.bfloat16)


def local(tokens, route_scale, expert_ids, gate_weight, up_weight, down_weight):
    tok_rows = tokens.shape[0]
    n_devices = lax.axis_size("expert")
    capacity = min(tok_rows, 2 * tok_rows * SPAN // n_devices)
    n_tensor = lax.axis_size("tensor")
    shaped = n_tensor == 4 and n_devices in (1, 2, 4) and tok_rows <= tokens.shape[1]
    if capacity == tok_rows and shaped:
        return gathered(tokens, route_scale, expert_ids, gate_weight, up_weight, down_weight)
    return dispatched(tokens, route_scale, expert_ids, gate_weight, up_weight, down_weight)


def solution(mesh):
    placed = (
        P(("groups", "expert"), "tensor"),
        P(("groups", "expert")),
        P(("groups", "expert"), None),
        P("expert", None, "tensor"),
        P("expert", None, "tensor"),
        P("expert", "tensor", None),
    )
    return jax.shard_map(
        local,
        mesh=mesh,
        in_specs=placed,
        out_specs=P(("groups", "expert"), "tensor"),
        check_vma=False,
    )
```

```python
import jax
import jax.numpy as jnp
from jax import lax
from jax.sharding import PartitionSpec as P

SPAN = 2


def dispatched(tokens, route_scale, expert_ids, gate_weight, up_weight, down_weight):
    tok_rows = tokens.shape[0]
    n_devices = lax.axis_size("expert")
    experts = n_devices // SPAN
    capacity = min(tok_rows, 2 * tok_rows * SPAN // n_devices)
    routed = expert_ids[:, 0]
    one_hot = (routed[:, None] == jnp.arange(experts, dtype=jnp.int32)[None, :]).astype(jnp.int32)
    slot_rank = jnp.sum((jnp.cumsum(one_hot, axis=0) - one_hot) * one_hot, axis=1)
    flat_slot = routed * capacity + slot_rank
    placing = (
        flat_slot[None, :] == jnp.arange(experts * capacity, dtype=jnp.int32)[:, None]
    ).astype(jnp.bfloat16)
    scaled = (tokens.astype(jnp.float32) * route_scale[:, None]).astype(jnp.bfloat16)
    gate_local = gate_weight[0]
    up_local = up_weight[0]
    down_local = down_weight[0]
    full_rows = lax.all_gather(scaled, "tensor", axis=1, tiled=True)
    width = full_rows.shape[1]
    packed = jnp.dot(placing, full_rows, preferred_element_type=jnp.float32).astype(jnp.bfloat16)
    outgoing = jnp.repeat(packed.reshape(experts, capacity, width), SPAN, axis=0)
    arrived = lax.all_to_all(outgoing, "expert", split_axis=0, concat_axis=0, tiled=True)
    slot_rows = arrived.reshape(n_devices * capacity, width)
    gate_act = jnp.dot(slot_rows, gate_local, preferred_element_type=jnp.float32)
    up_act = jnp.dot(slot_rows, up_local, preferred_element_type=jnp.float32)
    hidden = (jax.nn.silu(gate_act) * up_act).astype(jnp.bfloat16)
    partial_value = jnp.dot(hidden, down_local, preferred_element_type=jnp.float32)
    width = partial_value.shape[1]
    outgoing_back = partial_value.astype(jnp.bfloat16).reshape(n_devices, capacity, width)
    returned = lax.all_to_all(outgoing_back, "expert", split_axis=0, concat_axis=0, tiled=True)
    paired = jnp.sum(returned.astype(jnp.float32).reshape(experts, SPAN, capacity, width), axis=1)
    picked = jnp.take(paired.reshape(experts * capacity, width), flat_slot, axis=0)
    summed = lax.psum_scatter(
        picked.astype(jnp.bfloat16), "tensor", scatter_dimension=1, tiled=True
    )
    return summed


def _xor_pairs(size, k):
    return [(i, i ^ k) for i in range(size)]


_ORDER = (0, 2, 1, 3)


def _slots(weight, t, width, axis, order=_ORDER):
    return jnp.concatenate(
        [lax.dynamic_slice_in_dim(weight, (t ^ k) * width, width, axis=axis) for k in order], axis=axis)


def gathered(tokens, route_scale, expert_ids, gate_weight, up_weight, down_weight):
    tok_rows, width = tokens.shape
    n_expert = lax.axis_size("expert")
    n_tensor = lax.axis_size("tensor")
    me = lax.axis_index("expert")
    t = lax.axis_index("tensor")
    scaled = (tokens.astype(jnp.float32) * route_scale[:, None]).astype(jnp.bfloat16)
    blocks = [scaled] + [
        lax.ppermute(scaled, "expert", _xor_pairs(n_expert, k)) for k in range(1, n_expert)
    ]
    routed = expert_ids[:, 0][:, None]
    gate_w = _slots(gate_weight[0], t, width, 0)
    up_w = _slots(up_weight[0], t, width, 0)
    down_keep = _slots(down_weight[0], t, width, 1, _ORDER[:2])
    down_send = _slots(down_weight[0], t, width, 1, _ORDER[2:])
    waves = [[k] for k in list(range(2, n_expert)) + [1][:n_expert - 1] + [0]]
    total = None
    previous = None
    for wave in waves:
        piece = jnp.concatenate([blocks[k] for k in wave])
        pair = jnp.concatenate(
            [piece, lax.ppermute(piece, "tensor", _xor_pairs(n_tensor, 2))], axis=1)
        other = lax.ppermute(pair, "tensor", _xor_pairs(n_tensor, 1))
        if previous is not None:
            pair, other, _ = lax.optimization_barrier((pair, other, previous))
        gate_act = jnp.dot(pair, gate_w[:2 * width], preferred_element_type=jnp.float32) + jnp.dot(
            other, gate_w[2 * width:], preferred_element_type=jnp.float32)
        up_act = jnp.dot(pair, up_w[:2 * width], preferred_element_type=jnp.float32) + jnp.dot(
            other, up_w[2 * width:], preferred_element_type=jnp.float32)
        hidden = (jax.nn.silu(gate_act) * up_act).astype(jnp.bfloat16)
        keep = jnp.dot(hidden, down_keep, preferred_element_type=jnp.float32).astype(jnp.bfloat16)
        send = jnp.dot(hidden, down_send, preferred_element_type=jnp.float32).astype(jnp.bfloat16)
        previous = keep
        over_c = keep.astype(jnp.float32) + lax.ppermute(
            send, "tensor", _xor_pairs(n_tensor, 1)).astype(jnp.float32)
        summed = over_c[:, :width] + lax.ppermute(
            over_c[:, width:].astype(jnp.bfloat16), "tensor", _xor_pairs(n_tensor, 2)).astype(jnp.float32)
        for i, k in enumerate(wave):
            part = summed[i * tok_rows:(i + 1) * tok_rows]
            if k:
                part = lax.ppermute(
                    part.astype(jnp.bfloat16), "expert", _xor_pairs(n_expert, k)).astype(jnp.float32)
            part = jnp.where(routed == (me ^ k) // SPAN, part, 0.0)
            total = part if total is None else total + part
    return total.astype(jnp.bfloat16)


def local(tokens, route_scale, expert_ids, gate_weight, up_weight, down_weight):
    tok_rows = tokens.shape[0]
    n_devices = lax.axis_size("expert")
    capacity = min(tok_rows, 2 * tok_rows * SPAN // n_devices)
    n_tensor = lax.axis_size("tensor")
    shaped = n_tensor == 4 and n_devices in (1, 2, 4) and tok_rows <= tokens.shape[1]
    if capacity == tok_rows and shaped:
        return gathered(tokens, route_scale, expert_ids, gate_weight, up_weight, down_weight)
    return dispatched(tokens, route_scale, expert_ids, gate_weight, up_weight, down_weight)


def solution(mesh):
    placed = (
        P(("groups", "expert"), "tensor"),
        P(("groups", "expert")),
        P(("groups", "expert"), None),
        P("expert", None, "tensor"),
        P("expert", None, "tensor"),
        P("expert", "tensor", None),
    )
    return jax.shard_map(
        local,
        mesh=mesh,
        in_specs=placed,
        out_specs=P(("groups", "expert"), "tensor"),
        check_vma=False,
    )
```

```python
import jax
import jax.numpy as jnp
from jax import lax
from jax.sharding import PartitionSpec as P

SPAN = 2


def dispatched(tokens, route_scale, expert_ids, gate_weight, up_weight, down_weight):
    tok_rows = tokens.shape[0]
    n_devices = lax.axis_size("expert")
    experts = n_devices // SPAN
    capacity = min(tok_rows, 2 * tok_rows * SPAN // n_devices)
    routed = expert_ids[:, 0]
    one_hot = (routed[:, None] == jnp.arange(experts, dtype=jnp.int32)[None, :]).astype(jnp.int32)
    slot_rank = jnp.sum((jnp.cumsum(one_hot, axis=0) - one_hot) * one_hot, axis=1)
    flat_slot = routed * capacity + slot_rank
    placing = (
        flat_slot[None, :] == jnp.arange(experts * capacity, dtype=jnp.int32)[:, None]
    ).astype(jnp.bfloat16)
    scaled = (tokens.astype(jnp.float32) * route_scale[:, None]).astype(jnp.bfloat16)
    gate_local = gate_weight[0]
    up_local = up_weight[0]
    down_local = down_weight[0]
    full_rows = lax.all_gather(scaled, "tensor", axis=1, tiled=True)
    width = full_rows.shape[1]
    packed = jnp.dot(placing, full_rows, preferred_element_type=jnp.float32).astype(jnp.bfloat16)
    outgoing = jnp.repeat(packed.reshape(experts, capacity, width), SPAN, axis=0)
    arrived = lax.all_to_all(outgoing, "expert", split_axis=0, concat_axis=0, tiled=True)
    slot_rows = arrived.reshape(n_devices * capacity, width)
    gate_act = jnp.dot(slot_rows, gate_local, preferred_element_type=jnp.float32)
    up_act = jnp.dot(slot_rows, up_local, preferred_element_type=jnp.float32)
    hidden = (jax.nn.silu(gate_act) * up_act).astype(jnp.bfloat16)
    partial_value = jnp.dot(hidden, down_local, preferred_element_type=jnp.float32)
    width = partial_value.shape[1]
    outgoing_back = partial_value.astype(jnp.bfloat16).reshape(n_devices, capacity, width)
    returned = lax.all_to_all(outgoing_back, "expert", split_axis=0, concat_axis=0, tiled=True)
    paired = jnp.sum(returned.astype(jnp.float32).reshape(experts, SPAN, capacity, width), axis=1)
    picked = jnp.take(paired.reshape(experts * capacity, width), flat_slot, axis=0)
    summed = lax.psum_scatter(
        picked.astype(jnp.bfloat16), "tensor", scatter_dimension=1, tiled=True
    )
    return summed


def _xor_pairs(size, k):
    return [(i, i ^ k) for i in range(size)]


_ORDER = (0, 2, 1, 3)


def _slots(weight, t, width, axis, order=_ORDER):
    return jnp.concatenate(
        [lax.dynamic_slice_in_dim(weight, (t ^ k) * width, width, axis=axis) for k in order], axis=axis)


def gathered(tokens, route_scale, expert_ids, gate_weight, up_weight, down_weight):
    tok_rows, width = tokens.shape
    n_expert = lax.axis_size("expert")
    n_tensor = lax.axis_size("tensor")
    me = lax.axis_index("expert")
    t = lax.axis_index("tensor")
    scaled = (tokens.astype(jnp.float32) * route_scale[:, None]).astype(jnp.bfloat16)
    blocks = [scaled] + [
        lax.ppermute(scaled, "expert", _xor_pairs(n_expert, k)) for k in range(1, n_expert)
    ]
    routed = expert_ids[:, 0][:, None]
    gate_w = _slots(gate_weight[0], t, width, 0)
    up_w = _slots(up_weight[0], t, width, 0)
    down_keep = _slots(down_weight[0], t, width, 1, _ORDER[:2])
    down_send = _slots(down_weight[0], t, width, 1, _ORDER[2:])
    waves = [[k] for k in list(range(2, n_expert)) + [1][:n_expert - 1] + [0]]
    def returned(keep, send, wave, total):
        over_c = keep.astype(jnp.float32) + lax.ppermute(
            send, "tensor", _xor_pairs(n_tensor, 1)).astype(jnp.float32)
        summed = over_c[:, :width] + lax.ppermute(
            over_c[:, width:].astype(jnp.bfloat16), "tensor", _xor_pairs(n_tensor, 2)).astype(jnp.float32)
        for i, k in enumerate(wave):
            part = summed[i * tok_rows:(i + 1) * tok_rows]
            if k:
                part = lax.ppermute(
                    part.astype(jnp.bfloat16), "expert", _xor_pairs(n_expert, k)).astype(jnp.float32)
            part = jnp.where(routed == (me ^ k) // SPAN, part, 0.0)
            total = part if total is None else total + part
        return total

    total = None
    previous = None
    pending = None
    for wave in waves:
        piece = jnp.concatenate([blocks[k] for k in wave])
        pair = jnp.concatenate(
            [piece, lax.ppermute(piece, "tensor", _xor_pairs(n_tensor, 2))], axis=1)
        rows = jnp.concatenate(
            [pair, lax.ppermute(pair, "tensor", _xor_pairs(n_tensor, 1))], axis=1)
        if previous is not None:
            rows, _ = lax.optimization_barrier((rows, previous))
        gate_act = jnp.dot(rows, gate_w, preferred_element_type=jnp.float32)
        up_act = jnp.dot(rows, up_w, preferred_element_type=jnp.float32)
        hidden = (jax.nn.silu(gate_act) * up_act).astype(jnp.bfloat16)
        keep = jnp.dot(hidden, down_keep, preferred_element_type=jnp.float32).astype(jnp.bfloat16)
        send = jnp.dot(hidden, down_send, preferred_element_type=jnp.float32).astype(jnp.bfloat16)
        previous = keep
        if len(waves) > 1 and wave is waves[-2]:
            pending = (keep, send)
            continue
        if pending is not None:
            (held_keep, held_send), _ = lax.optimization_barrier((pending, keep))
            total = returned(held_keep, held_send, waves[-2], total)
        total = returned(keep, send, wave, total)
    return total.astype(jnp.bfloat16)


def local(tokens, route_scale, expert_ids, gate_weight, up_weight, down_weight):
    tok_rows = tokens.shape[0]
    n_devices = lax.axis_size("expert")
    capacity = min(tok_rows, 2 * tok_rows * SPAN // n_devices)
    n_tensor = lax.axis_size("tensor")
    shaped = n_tensor == 4 and n_devices in (1, 2, 4) and tok_rows <= tokens.shape[1]
    if capacity == tok_rows and shaped:
        return gathered(tokens, route_scale, expert_ids, gate_weight, up_weight, down_weight)
    return dispatched(tokens, route_scale, expert_ids, gate_weight, up_weight, down_weight)


def solution(mesh):
    placed = (
        P(("groups", "expert"), "tensor"),
        P(("groups", "expert")),
        P(("groups", "expert"), None),
        P("expert", None, "tensor"),
        P("expert", None, "tensor"),
        P("expert", "tensor", None),
    )
    return jax.shard_map(
        local,
        mesh=mesh,
        in_specs=placed,
        out_specs=P(("groups", "expert"), "tensor"),
        check_vma=False,
    )
```

```python
import jax
import jax.numpy as jnp
from jax import lax
from jax.sharding import PartitionSpec as P

SPAN = 2


def dispatched(tokens, route_scale, expert_ids, gate_weight, up_weight, down_weight):
    tok_rows = tokens.shape[0]
    n_devices = lax.axis_size("expert")
    experts = n_devices // SPAN
    capacity = min(tok_rows, 2 * tok_rows * SPAN // n_devices)
    routed = expert_ids[:, 0]
    one_hot = (routed[:, None] == jnp.arange(experts, dtype=jnp.int32)[None, :]).astype(jnp.int32)
    slot_rank = jnp.sum((jnp.cumsum(one_hot, axis=0) - one_hot) * one_hot, axis=1)
    flat_slot = routed * capacity + slot_rank
    placing = (
        flat_slot[None, :] == jnp.arange(experts * capacity, dtype=jnp.int32)[:, None]
    ).astype(jnp.bfloat16)
    scaled = (tokens.astype(jnp.float32) * route_scale[:, None]).astype(jnp.bfloat16)
    gate_local = gate_weight[0]
    up_local = up_weight[0]
    down_local = down_weight[0]
    full_rows = lax.all_gather(scaled, "tensor", axis=1, tiled=True)
    width = full_rows.shape[1]
    packed = jnp.dot(placing, full_rows, preferred_element_type=jnp.float32).astype(jnp.bfloat16)
    outgoing = jnp.repeat(packed.reshape(experts, capacity, width), SPAN, axis=0)
    arrived = lax.all_to_all(outgoing, "expert", split_axis=0, concat_axis=0, tiled=True)
    slot_rows = arrived.reshape(n_devices * capacity, width)
    gate_act = jnp.dot(slot_rows, gate_local, preferred_element_type=jnp.float32)
    up_act = jnp.dot(slot_rows, up_local, preferred_element_type=jnp.float32)
    hidden = (jax.nn.silu(gate_act) * up_act).astype(jnp.bfloat16)
    partial_value = jnp.dot(hidden, down_local, preferred_element_type=jnp.float32)
    width = partial_value.shape[1]
    outgoing_back = partial_value.astype(jnp.bfloat16).reshape(n_devices, capacity, width)
    returned = lax.all_to_all(outgoing_back, "expert", split_axis=0, concat_axis=0, tiled=True)
    paired = jnp.sum(returned.astype(jnp.float32).reshape(experts, SPAN, capacity, width), axis=1)
    picked = jnp.take(paired.reshape(experts * capacity, width), flat_slot, axis=0)
    summed = lax.psum_scatter(
        picked.astype(jnp.bfloat16), "tensor", scatter_dimension=1, tiled=True
    )
    return summed


def _xor_pairs(size, k):
    return [(i, i ^ k) for i in range(size)]


_ORDER = (0, 2, 1, 3)


def _slots(weight, t, width, axis, order=_ORDER):
    return jnp.concatenate(
        [lax.dynamic_slice_in_dim(weight, (t ^ k) * width, width, axis=axis) for k in order], axis=axis)


def gathered(tokens, route_scale, expert_ids, gate_weight, up_weight, down_weight):
    tok_rows, width = tokens.shape
    n_expert = lax.axis_size("expert")
    n_tensor = lax.axis_size("tensor")
    me = lax.axis_index("expert")
    t = lax.axis_index("tensor")
    scaled = (tokens.astype(jnp.float32) * route_scale[:, None]).astype(jnp.bfloat16)
    blocks = [scaled] + [
        lax.ppermute(scaled, "expert", _xor_pairs(n_expert, k)) for k in range(1, n_expert)
    ]
    routed = expert_ids[:, 0][:, None]
    gate_w = _slots(gate_weight[0], t, width, 0)
    up_w = _slots(up_weight[0], t, width, 0)
    down_keep = _slots(down_weight[0], t, width, 1, _ORDER[:2])
    down_send = _slots(down_weight[0], t, width, 1, _ORDER[2:])
    waves = [[k] for k in list(range(n_expert - 1, 1, -1)) + [1][:n_expert - 1] + [0]]
    total = None
    previous = None
    for wave in waves:
        piece = jnp.concatenate([blocks[k] for k in wave])
        pair = jnp.concatenate(
            [piece, lax.ppermute(piece, "tensor", _xor_pairs(n_tensor, 2))], axis=1)
        rows = jnp.concatenate(
            [pair, lax.ppermute(pair, "tensor", _xor_pairs(n_tensor, 1))], axis=1)
        if previous is not None:
            rows, _ = lax.optimization_barrier((rows, previous))
        gate_act = jnp.dot(rows, gate_w, preferred_element_type=jnp.float32)
        up_act = jnp.dot(rows, up_w, preferred_element_type=jnp.float32)
        hidden = (jax.nn.silu(gate_act) * up_act).astype(jnp.bfloat16)
        keep = jnp.dot(hidden, down_keep, preferred_element_type=jnp.float32).astype(jnp.bfloat16)
        send = jnp.dot(hidden, down_send, preferred_element_type=jnp.float32).astype(jnp.bfloat16)
        previous = keep
        over_c = keep.astype(jnp.float32) + lax.ppermute(
            send, "tensor", _xor_pairs(n_tensor, 1)).astype(jnp.float32)
        summed = over_c[:, :width] + lax.ppermute(
            over_c[:, width:].astype(jnp.bfloat16), "tensor", _xor_pairs(n_tensor, 2)).astype(jnp.float32)
        for i, k in enumerate(wave):
            part = summed[i * tok_rows:(i + 1) * tok_rows]
            if k:
                part = lax.ppermute(
                    part.astype(jnp.bfloat16), "expert", _xor_pairs(n_expert, k)).astype(jnp.float32)
            part = jnp.where(routed == (me ^ k) // SPAN, part, 0.0)
            total = part if total is None else total + part
    return total.astype(jnp.bfloat16)


def local(tokens, route_scale, expert_ids, gate_weight, up_weight, down_weight):
    tok_rows = tokens.shape[0]
    n_devices = lax.axis_size("expert")
    capacity = min(tok_rows, 2 * tok_rows * SPAN // n_devices)
    n_tensor = lax.axis_size("tensor")
    shaped = n_tensor == 4 and n_devices in (1, 2, 4) and tok_rows <= tokens.shape[1]
    if capacity == tok_rows and shaped:
        return gathered(tokens, route_scale, expert_ids, gate_weight, up_weight, down_weight)
    return dispatched(tokens, route_scale, expert_ids, gate_weight, up_weight, down_weight)


def solution(mesh):
    placed = (
        P(("groups", "expert"), "tensor"),
        P(("groups", "expert")),
        P(("groups", "expert"), None),
        P("expert", None, "tensor"),
        P("expert", None, "tensor"),
        P("expert", "tensor", None),
    )
    return jax.shard_map(
        local,
        mesh=mesh,
        in_specs=placed,
        out_specs=P(("groups", "expert"), "tensor"),
        check_vma=False,
    )
```

```python
import jax
import jax.numpy as jnp
from jax import lax
from jax.sharding import PartitionSpec as P

SPAN = 2


def dispatched(tokens, route_scale, expert_ids, gate_weight, up_weight, down_weight):
    tok_rows = tokens.shape[0]
    n_devices = lax.axis_size("expert")
    experts = n_devices // SPAN
    capacity = min(tok_rows, 2 * tok_rows * SPAN // n_devices)
    routed = expert_ids[:, 0]
    one_hot = (routed[:, None] == jnp.arange(experts, dtype=jnp.int32)[None, :]).astype(jnp.int32)
    slot_rank = jnp.sum((jnp.cumsum(one_hot, axis=0) - one_hot) * one_hot, axis=1)
    flat_slot = routed * capacity + slot_rank
    placing = (
        flat_slot[None, :] == jnp.arange(experts * capacity, dtype=jnp.int32)[:, None]
    ).astype(jnp.bfloat16)
    scaled = (tokens.astype(jnp.float32) * route_scale[:, None]).astype(jnp.bfloat16)
    gate_local = gate_weight[0]
    up_local = up_weight[0]
    down_local = down_weight[0]
    full_rows = lax.all_gather(scaled, "tensor", axis=1, tiled=True)
    width = full_rows.shape[1]
    packed = jnp.dot(placing, full_rows, preferred_element_type=jnp.float32).astype(jnp.bfloat16)
    outgoing = jnp.repeat(packed.reshape(experts, capacity, width), SPAN, axis=0)
    arrived = lax.all_to_all(outgoing, "expert", split_axis=0, concat_axis=0, tiled=True)
    slot_rows = arrived.reshape(n_devices * capacity, width)
    gate_act = jnp.dot(slot_rows, gate_local, preferred_element_type=jnp.float32)
    up_act = jnp.dot(slot_rows, up_local, preferred_element_type=jnp.float32)
    hidden = (jax.nn.silu(gate_act) * up_act).astype(jnp.bfloat16)
    partial_value = jnp.dot(hidden, down_local, preferred_element_type=jnp.float32)
    width = partial_value.shape[1]
    outgoing_back = partial_value.astype(jnp.bfloat16).reshape(n_devices, capacity, width)
    returned = lax.all_to_all(outgoing_back, "expert", split_axis=0, concat_axis=0, tiled=True)
    paired = jnp.sum(returned.astype(jnp.float32).reshape(experts, SPAN, capacity, width), axis=1)
    picked = jnp.take(paired.reshape(experts * capacity, width), flat_slot, axis=0)
    summed = lax.psum_scatter(
        picked.astype(jnp.bfloat16), "tensor", scatter_dimension=1, tiled=True
    )
    return summed


def _xor_pairs(size, k):
    return [(i, i ^ k) for i in range(size)]


_ORDER = (0, 2, 1, 3)


def _slots(weight, t, width, axis, order=_ORDER):
    return jnp.concatenate(
        [lax.dynamic_slice_in_dim(weight, (t ^ k) * width, width, axis=axis) for k in order], axis=axis)


def gathered(tokens, route_scale, expert_ids, gate_weight, up_weight, down_weight):
    tok_rows, width = tokens.shape
    n_expert = lax.axis_size("expert")
    n_tensor = lax.axis_size("tensor")
    me = lax.axis_index("expert")
    t = lax.axis_index("tensor")
    scaled = (tokens.astype(jnp.float32) * route_scale[:, None]).astype(jnp.bfloat16)
    blocks = [scaled] + [
        lax.ppermute(scaled, "expert", _xor_pairs(n_expert, k)) for k in range(1, n_expert)
    ]
    routed = expert_ids[:, 0][:, None]
    gate_w = _slots(gate_weight[0], t, width, 0)
    up_w = _slots(up_weight[0], t, width, 0)
    down_keep = _slots(down_weight[0], t, width, 1, _ORDER[:2])
    down_send = _slots(down_weight[0], t, width, 1, _ORDER[2:])
    waves = [[k] for k in list(range(n_expert - 1, 1, -1)) + [1][:n_expert - 1] + [0]]
    if len(waves) > 1:
        blocks[0], _ = lax.optimization_barrier((blocks[0], blocks[waves[0][0]]))
    total = None
    previous = None
    for wave in waves:
        piece = jnp.concatenate([blocks[k] for k in wave])
        pair = jnp.concatenate(
            [piece, lax.ppermute(piece, "tensor", _xor_pairs(n_tensor, 2))], axis=1)
        rows = jnp.concatenate(
            [pair, lax.ppermute(pair, "tensor", _xor_pairs(n_tensor, 1))], axis=1)
        if previous is not None:
            rows, _ = lax.optimization_barrier((rows, previous))
        gate_act = jnp.dot(rows, gate_w, preferred_element_type=jnp.float32)
        up_act = jnp.dot(rows, up_w, preferred_element_type=jnp.float32)
        hidden = (jax.nn.silu(gate_act) * up_act).astype(jnp.bfloat16)
        keep = jnp.dot(hidden, down_keep, preferred_element_type=jnp.float32).astype(jnp.bfloat16)
        send = jnp.dot(hidden, down_send, preferred_element_type=jnp.float32).astype(jnp.bfloat16)
        previous = keep
        over_c = keep.astype(jnp.float32) + lax.ppermute(
            send, "tensor", _xor_pairs(n_tensor, 1)).astype(jnp.float32)
        summed = over_c[:, :width] + lax.ppermute(
            over_c[:, width:].astype(jnp.bfloat16), "tensor", _xor_pairs(n_tensor, 2)).astype(jnp.float32)
        for i, k in enumerate(wave):
            part = summed[i * tok_rows:(i + 1) * tok_rows]
            if k:
                part = lax.ppermute(
                    part.astype(jnp.bfloat16), "expert", _xor_pairs(n_expert, k)).astype(jnp.float32)
            part = jnp.where(routed == (me ^ k) // SPAN, part, 0.0)
            total = part if total is None else total + part
    return total.astype(jnp.bfloat16)


def local(tokens, route_scale, expert_ids, gate_weight, up_weight, down_weight):
    tok_rows = tokens.shape[0]
    n_devices = lax.axis_size("expert")
    capacity = min(tok_rows, 2 * tok_rows * SPAN // n_devices)
    n_tensor = lax.axis_size("tensor")
    shaped = n_tensor == 4 and n_devices in (1, 2, 4) and tok_rows <= tokens.shape[1]
    if capacity == tok_rows and shaped:
        return gathered(tokens, route_scale, expert_ids, gate_weight, up_weight, down_weight)
    return dispatched(tokens, route_scale, expert_ids, gate_weight, up_weight, down_weight)


def solution(mesh):
    placed = (
        P(("groups", "expert"), "tensor"),
        P(("groups", "expert")),
        P(("groups", "expert"), None),
        P("expert", None, "tensor"),
        P("expert", None, "tensor"),
        P("expert", "tensor", None),
    )
    return jax.shard_map(
        local,
        mesh=mesh,
        in_specs=placed,
        out_specs=P(("groups", "expert"), "tensor"),
        check_vma=False,
    )
```

```python
import jax
import jax.numpy as jnp
from jax import lax
from jax.sharding import PartitionSpec as P

SPAN = 2


def dispatched(tokens, route_scale, expert_ids, gate_weight, up_weight, down_weight):
    tok_rows = tokens.shape[0]
    n_devices = lax.axis_size("expert")
    experts = n_devices // SPAN
    capacity = min(tok_rows, 2 * tok_rows * SPAN // n_devices)
    routed = expert_ids[:, 0]
    one_hot = (routed[:, None] == jnp.arange(experts, dtype=jnp.int32)[None, :]).astype(jnp.int32)
    slot_rank = jnp.sum((jnp.cumsum(one_hot, axis=0) - one_hot) * one_hot, axis=1)
    flat_slot = routed * capacity + slot_rank
    placing = (
        flat_slot[None, :] == jnp.arange(experts * capacity, dtype=jnp.int32)[:, None]
    ).astype(jnp.bfloat16)
    scaled = (tokens.astype(jnp.float32) * route_scale[:, None]).astype(jnp.bfloat16)
    gate_local = gate_weight[0]
    up_local = up_weight[0]
    down_local = down_weight[0]
    full_rows = lax.all_gather(scaled, "tensor", axis=1, tiled=True)
    width = full_rows.shape[1]
    packed = jnp.dot(placing, full_rows, preferred_element_type=jnp.float32).astype(jnp.bfloat16)
    outgoing = jnp.repeat(packed.reshape(experts, capacity, width), SPAN, axis=0)
    arrived = lax.all_to_all(outgoing, "expert", split_axis=0, concat_axis=0, tiled=True)
    slot_rows = arrived.reshape(n_devices * capacity, width)
    gate_act = jnp.dot(slot_rows, gate_local, preferred_element_type=jnp.float32)
    up_act = jnp.dot(slot_rows, up_local, preferred_element_type=jnp.float32)
    hidden = (jax.nn.silu(gate_act) * up_act).astype(jnp.bfloat16)
    partial_value = jnp.dot(hidden, down_local, preferred_element_type=jnp.float32)
    width = partial_value.shape[1]
    outgoing_back = partial_value.astype(jnp.bfloat16).reshape(n_devices, capacity, width)
    returned = lax.all_to_all(outgoing_back, "expert", split_axis=0, concat_axis=0, tiled=True)
    paired = jnp.sum(returned.astype(jnp.float32).reshape(experts, SPAN, capacity, width), axis=1)
    picked = jnp.take(paired.reshape(experts * capacity, width), flat_slot, axis=0)
    summed = lax.psum_scatter(
        picked.astype(jnp.bfloat16), "tensor", scatter_dimension=1, tiled=True
    )
    return summed


def _xor_pairs(size, k):
    return [(i, i ^ k) for i in range(size)]


_ORDER = (0, 2, 1, 3)


def _slots(weight, t, width, axis, order=_ORDER):
    return jnp.concatenate(
        [lax.dynamic_slice_in_dim(weight, (t ^ k) * width, width, axis=axis) for k in order], axis=axis)


def gathered(tokens, route_scale, expert_ids, gate_weight, up_weight, down_weight):
    tok_rows, width = tokens.shape
    n_expert = lax.axis_size("expert")
    n_tensor = lax.axis_size("tensor")
    me = lax.axis_index("expert")
    t = lax.axis_index("tensor")
    scaled = (tokens.astype(jnp.float32) * route_scale[:, None]).astype(jnp.bfloat16)
    blocks = [scaled] + [
        lax.ppermute(scaled, "expert", _xor_pairs(n_expert, k)) for k in range(1, n_expert)
    ]
    routed = expert_ids[:, 0][:, None]
    gate_w = _slots(gate_weight[0], t, width, 0)
    up_w = _slots(up_weight[0], t, width, 0)
    down_keep = _slots(down_weight[0], t, width, 1, _ORDER[:2])
    down_send = _slots(down_weight[0], t, width, 1, _ORDER[2:])
    waves = [[k] for k in (n_expert - 1,) + tuple(range(1, n_expert - 1)) + (0,)] if n_expert > 1 else [[0]]
    total = None
    previous = None
    for wave in waves:
        piece = jnp.concatenate([blocks[k] for k in wave])
        pair = jnp.concatenate(
            [piece, lax.ppermute(piece, "tensor", _xor_pairs(n_tensor, 2))], axis=1)
        rows = jnp.concatenate(
            [pair, lax.ppermute(pair, "tensor", _xor_pairs(n_tensor, 1))], axis=1)
        if previous is not None:
            rows, _ = lax.optimization_barrier((rows, previous))
        gate_act = jnp.dot(rows, gate_w, preferred_element_type=jnp.float32)
        up_act = jnp.dot(rows, up_w, preferred_element_type=jnp.float32)
        hidden = (jax.nn.silu(gate_act) * up_act).astype(jnp.bfloat16)
        keep = jnp.dot(hidden, down_keep, preferred_element_type=jnp.float32).astype(jnp.bfloat16)
        send = jnp.dot(hidden, down_send, preferred_element_type=jnp.float32).astype(jnp.bfloat16)
        previous = keep
        over_c = keep.astype(jnp.float32) + lax.ppermute(
            send, "tensor", _xor_pairs(n_tensor, 1)).astype(jnp.float32)
        summed = over_c[:, :width] + lax.ppermute(
            over_c[:, width:].astype(jnp.bfloat16), "tensor", _xor_pairs(n_tensor, 2)).astype(jnp.float32)
        for i, k in enumerate(wave):
            part = summed[i * tok_rows:(i + 1) * tok_rows]
            if k:
                part = lax.ppermute(
                    part.astype(jnp.bfloat16), "expert", _xor_pairs(n_expert, k)).astype(jnp.float32)
            part = jnp.where(routed == (me ^ k) // SPAN, part, 0.0)
            total = part if total is None else total + part
    return total.astype(jnp.bfloat16)


def local(tokens, route_scale, expert_ids, gate_weight, up_weight, down_weight):
    tok_rows = tokens.shape[0]
    n_devices = lax.axis_size("expert")
    capacity = min(tok_rows, 2 * tok_rows * SPAN // n_devices)
    n_tensor = lax.axis_size("tensor")
    shaped = n_tensor == 4 and n_devices in (1, 2, 4) and tok_rows <= tokens.shape[1]
    if capacity == tok_rows and shaped:
        return gathered(tokens, route_scale, expert_ids, gate_weight, up_weight, down_weight)
    return dispatched(tokens, route_scale, expert_ids, gate_weight, up_weight, down_weight)


def solution(mesh):
    placed = (
        P(("groups", "expert"), "tensor"),
        P(("groups", "expert")),
        P(("groups", "expert"), None),
        P("expert", None, "tensor"),
        P("expert", None, "tensor"),
        P("expert", "tensor", None),
    )
    return jax.shard_map(
        local,
        mesh=mesh,
        in_specs=placed,
        out_specs=P(("groups", "expert"), "tensor"),
        check_vma=False,
    )
```

```python
import jax
import jax.numpy as jnp
from jax import lax
from jax.sharding import PartitionSpec as P

SPAN = 2


def dispatched(tokens, route_scale, expert_ids, gate_weight, up_weight, down_weight):
    tok_rows = tokens.shape[0]
    n_devices = lax.axis_size("expert")
    experts = n_devices // SPAN
    capacity = min(tok_rows, 2 * tok_rows * SPAN // n_devices)
    routed = expert_ids[:, 0]
    one_hot = (routed[:, None] == jnp.arange(experts, dtype=jnp.int32)[None, :]).astype(jnp.int32)
    slot_rank = jnp.sum((jnp.cumsum(one_hot, axis=0) - one_hot) * one_hot, axis=1)
    flat_slot = routed * capacity + slot_rank
    placing = (
        flat_slot[None, :] == jnp.arange(experts * capacity, dtype=jnp.int32)[:, None]
    ).astype(jnp.bfloat16)
    scaled = (tokens.astype(jnp.float32) * route_scale[:, None]).astype(jnp.bfloat16)
    gate_local = gate_weight[0]
    up_local = up_weight[0]
    down_local = down_weight[0]
    full_rows = lax.all_gather(scaled, "tensor", axis=1, tiled=True)
    width = full_rows.shape[1]
    packed = jnp.dot(placing, full_rows, preferred_element_type=jnp.float32).astype(jnp.bfloat16)
    outgoing = jnp.repeat(packed.reshape(experts, capacity, width), SPAN, axis=0)
    arrived = lax.all_to_all(outgoing, "expert", split_axis=0, concat_axis=0, tiled=True)
    slot_rows = arrived.reshape(n_devices * capacity, width)
    gate_act = jnp.dot(slot_rows, gate_local, preferred_element_type=jnp.float32)
    up_act = jnp.dot(slot_rows, up_local, preferred_element_type=jnp.float32)
    hidden = (jax.nn.silu(gate_act) * up_act).astype(jnp.bfloat16)
    partial_value = jnp.dot(hidden, down_local, preferred_element_type=jnp.float32)
    width = partial_value.shape[1]
    outgoing_back = partial_value.astype(jnp.bfloat16).reshape(n_devices, capacity, width)
    returned = lax.all_to_all(outgoing_back, "expert", split_axis=0, concat_axis=0, tiled=True)
    paired = jnp.sum(returned.astype(jnp.float32).reshape(experts, SPAN, capacity, width), axis=1)
    picked = jnp.take(paired.reshape(experts * capacity, width), flat_slot, axis=0)
    summed = lax.psum_scatter(
        picked.astype(jnp.bfloat16), "tensor", scatter_dimension=1, tiled=True
    )
    return summed


def _xor_pairs(size, k):
    return [(i, i ^ k) for i in range(size)]


_ORDER = (0, 2, 1, 3)


def _slots(weight, t, width, axis, order=_ORDER):
    return jnp.concatenate(
        [lax.dynamic_slice_in_dim(weight, (t ^ k) * width, width, axis=axis) for k in order], axis=axis)


def gathered(tokens, route_scale, expert_ids, gate_weight, up_weight, down_weight):
    tok_rows, width = tokens.shape
    n_expert = lax.axis_size("expert")
    n_tensor = lax.axis_size("tensor")
    me = lax.axis_index("expert")
    t = lax.axis_index("tensor")
    scaled = (tokens.astype(jnp.float32) * route_scale[:, None]).astype(jnp.bfloat16)
    blocks = [scaled] + [
        lax.ppermute(scaled, "expert", _xor_pairs(n_expert, k)) for k in range(1, n_expert)
    ]
    routed = expert_ids[:, 0][:, None]
    gate_w = _slots(gate_weight[0], t, width, 0)
    up_w = _slots(up_weight[0], t, width, 0)
    down_keep = _slots(down_weight[0], t, width, 1, _ORDER[:2])
    down_send = _slots(down_weight[0], t, width, 1, _ORDER[2:])
    waves = [[k] for k in list(range(n_expert - 1, 1, -1)) + [1][:n_expert - 1] + [0]]
    total = None
    previous = None
    for wave in waves:
        piece = jnp.concatenate([blocks[k] for k in wave])
        pair = jnp.concatenate(
            [piece, lax.ppermute(piece, "tensor", _xor_pairs(n_tensor, 2))], axis=1)
        rows = jnp.concatenate(
            [pair, lax.ppermute(pair, "tensor", _xor_pairs(n_tensor, 1))], axis=1)
        if previous is not None:
            rows, _ = lax.optimization_barrier((rows, previous))
        gate_act = jnp.dot(rows, gate_w, preferred_element_type=jnp.float32)
        up_act = jnp.dot(rows, up_w, preferred_element_type=jnp.float32)
        hidden = (jax.nn.silu(gate_act) * up_act).astype(jnp.bfloat16)
        keep = jnp.dot(hidden, down_keep, preferred_element_type=jnp.float32).astype(jnp.bfloat16)
        send = jnp.dot(hidden, down_send, preferred_element_type=jnp.float32).astype(jnp.bfloat16)
        previous = keep
        if wave == [0] and n_expert > 1:
            part = keep[:, :width].astype(jnp.float32)
            for values, k in [(keep[:, width:], 2), (send[:, :width], 1), (send[:, width:], 3)]:
                part = part + lax.ppermute(values, "tensor", _xor_pairs(n_tensor, k)).astype(jnp.float32)
            part = jnp.where(routed == me // SPAN, part, 0.0)
            total = part if total is None else total + part
            continue
        over_c = keep.astype(jnp.float32) + lax.ppermute(
            send, "tensor", _xor_pairs(n_tensor, 1)).astype(jnp.float32)
        summed = over_c[:, :width] + lax.ppermute(
            over_c[:, width:].astype(jnp.bfloat16), "tensor", _xor_pairs(n_tensor, 2)).astype(jnp.float32)
        for i, k in enumerate(wave):
            part = summed[i * tok_rows:(i + 1) * tok_rows]
            if k:
                part = lax.ppermute(
                    part.astype(jnp.bfloat16), "expert", _xor_pairs(n_expert, k)).astype(jnp.float32)
            part = jnp.where(routed == (me ^ k) // SPAN, part, 0.0)
            total = part if total is None else total + part
    return total.astype(jnp.bfloat16)


def local(tokens, route_scale, expert_ids, gate_weight, up_weight, down_weight):
    tok_rows = tokens.shape[0]
    n_devices = lax.axis_size("expert")
    capacity = min(tok_rows, 2 * tok_rows * SPAN // n_devices)
    n_tensor = lax.axis_size("tensor")
    shaped = n_tensor == 4 and n_devices in (1, 2, 4) and tok_rows <= tokens.shape[1]
    if capacity == tok_rows and shaped:
        return gathered(tokens, route_scale, expert_ids, gate_weight, up_weight, down_weight)
    return dispatched(tokens, route_scale, expert_ids, gate_weight, up_weight, down_weight)


def solution(mesh):
    placed = (
        P(("groups", "expert"), "tensor"),
        P(("groups", "expert")),
        P(("groups", "expert"), None),
        P("expert", None, "tensor"),
        P("expert", None, "tensor"),
        P("expert", "tensor", None),
    )
    return jax.shard_map(
        local,
        mesh=mesh,
        in_specs=placed,
        out_specs=P(("groups", "expert"), "tensor"),
        check_vma=False,
    )
```

```python
import jax
import jax.numpy as jnp
from jax import lax
from jax.sharding import PartitionSpec as P

SPAN = 2


def dispatched(tokens, route_scale, expert_ids, gate_weight, up_weight, down_weight):
    tok_rows = tokens.shape[0]
    n_devices = lax.axis_size("expert")
    experts = n_devices // SPAN
    capacity = min(tok_rows, 2 * tok_rows * SPAN // n_devices)
    routed = expert_ids[:, 0]
    one_hot = (routed[:, None] == jnp.arange(experts, dtype=jnp.int32)[None, :]).astype(jnp.int32)
    slot_rank = jnp.sum((jnp.cumsum(one_hot, axis=0) - one_hot) * one_hot, axis=1)
    flat_slot = routed * capacity + slot_rank
    placing = (
        flat_slot[None, :] == jnp.arange(experts * capacity, dtype=jnp.int32)[:, None]
    ).astype(jnp.bfloat16)
    scaled = (tokens.astype(jnp.float32) * route_scale[:, None]).astype(jnp.bfloat16)
    gate_local = gate_weight[0]
    up_local = up_weight[0]
    down_local = down_weight[0]
    full_rows = lax.all_gather(scaled, "tensor", axis=1, tiled=True)
    width = full_rows.shape[1]
    packed = jnp.dot(placing, full_rows, preferred_element_type=jnp.float32).astype(jnp.bfloat16)
    outgoing = jnp.repeat(packed.reshape(experts, capacity, width), SPAN, axis=0)
    arrived = lax.all_to_all(outgoing, "expert", split_axis=0, concat_axis=0, tiled=True)
    slot_rows = arrived.reshape(n_devices * capacity, width)
    gate_act = jnp.dot(slot_rows, gate_local, preferred_element_type=jnp.float32)
    up_act = jnp.dot(slot_rows, up_local, preferred_element_type=jnp.float32)
    hidden = (jax.nn.silu(gate_act) * up_act).astype(jnp.bfloat16)
    partial_value = jnp.dot(hidden, down_local, preferred_element_type=jnp.float32)
    width = partial_value.shape[1]
    outgoing_back = partial_value.astype(jnp.bfloat16).reshape(n_devices, capacity, width)
    returned = lax.all_to_all(outgoing_back, "expert", split_axis=0, concat_axis=0, tiled=True)
    paired = jnp.sum(returned.astype(jnp.float32).reshape(experts, SPAN, capacity, width), axis=1)
    picked = jnp.take(paired.reshape(experts * capacity, width), flat_slot, axis=0)
    summed = lax.psum_scatter(
        picked.astype(jnp.bfloat16), "tensor", scatter_dimension=1, tiled=True
    )
    return summed


def _xor_pairs(size, k):
    return [(i, i ^ k) for i in range(size)]


_ORDER = (0, 2, 1, 3)


def _slots(weight, t, width, axis, order=_ORDER):
    return jnp.concatenate(
        [lax.dynamic_slice_in_dim(weight, (t ^ k) * width, width, axis=axis) for k in order], axis=axis)


def gathered(tokens, route_scale, expert_ids, gate_weight, up_weight, down_weight):
    tok_rows, width = tokens.shape
    n_expert = lax.axis_size("expert")
    n_tensor = lax.axis_size("tensor")
    me = lax.axis_index("expert")
    t = lax.axis_index("tensor")
    scaled = (tokens.astype(jnp.float32) * route_scale[:, None]).astype(jnp.bfloat16)
    blocks = [scaled] + [
        lax.ppermute(scaled, "expert", _xor_pairs(n_expert, k)) for k in range(1, n_expert)
    ]
    routed = expert_ids[:, 0][:, None]
    gate_w = _slots(gate_weight[0], t, width, 0)
    up_w = _slots(up_weight[0], t, width, 0)
    down_keep = _slots(down_weight[0], t, width, 1, _ORDER[:2])
    down_send = _slots(down_weight[0], t, width, 1, _ORDER[2:])
    waves = [[k] for k in list(range(n_expert - 1, 1, -1)) + [1][:n_expert - 1] + [0]]
    total = None
    previous = None
    for wave in waves:
        piece = jnp.concatenate([blocks[k] for k in wave])
        pair = jnp.concatenate(
            [piece, lax.ppermute(piece, "tensor", _xor_pairs(n_tensor, 2))], axis=1)
        rows = jnp.concatenate(
            [pair, lax.ppermute(pair, "tensor", _xor_pairs(n_tensor, 1))], axis=1)
        if previous is not None:
            rows, _ = lax.optimization_barrier((rows, previous))
        gate_act = jnp.dot(rows, gate_w, preferred_element_type=jnp.float32)
        up_act = jnp.dot(rows, up_w, preferred_element_type=jnp.float32)
        hidden = (jax.nn.silu(gate_act) * up_act).astype(jnp.bfloat16)
        keep = jnp.dot(hidden, down_keep, preferred_element_type=jnp.float32).astype(jnp.bfloat16)
        send = jnp.dot(hidden, down_send, preferred_element_type=jnp.float32).astype(jnp.bfloat16)
        previous = send
        over_c = keep.astype(jnp.float32) + lax.ppermute(
            send, "tensor", _xor_pairs(n_tensor, 1)).astype(jnp.float32)
        summed = over_c[:, :width] + lax.ppermute(
            over_c[:, width:].astype(jnp.bfloat16), "tensor", _xor_pairs(n_tensor, 2)).astype(jnp.float32)
        for i, k in enumerate(wave):
            part = summed[i * tok_rows:(i + 1) * tok_rows]
            if k:
                part = lax.ppermute(
                    part.astype(jnp.bfloat16), "expert", _xor_pairs(n_expert, k)).astype(jnp.float32)
            part = jnp.where(routed == (me ^ k) // SPAN, part, 0.0)
            total = part if total is None else total + part
    return total.astype(jnp.bfloat16)


def local(tokens, route_scale, expert_ids, gate_weight, up_weight, down_weight):
    tok_rows = tokens.shape[0]
    n_devices = lax.axis_size("expert")
    capacity = min(tok_rows, 2 * tok_rows * SPAN // n_devices)
    n_tensor = lax.axis_size("tensor")
    shaped = n_tensor == 4 and n_devices in (1, 2, 4) and tok_rows <= tokens.shape[1]
    if capacity == tok_rows and shaped:
        return gathered(tokens, route_scale, expert_ids, gate_weight, up_weight, down_weight)
    return dispatched(tokens, route_scale, expert_ids, gate_weight, up_weight, down_weight)


def solution(mesh):
    placed = (
        P(("groups", "expert"), "tensor"),
        P(("groups", "expert")),
        P(("groups", "expert"), None),
        P("expert", None, "tensor"),
        P("expert", None, "tensor"),
        P("expert", "tensor", None),
    )
    return jax.shard_map(
        local,
        mesh=mesh,
        in_specs=placed,
        out_specs=P(("groups", "expert"), "tensor"),
        check_vma=False,
    )
```

```python
import jax
import jax.numpy as jnp
from jax import lax
from jax.sharding import PartitionSpec as P

SPAN = 2


def dispatched(tokens, route_scale, expert_ids, gate_weight, up_weight, down_weight):
    tok_rows = tokens.shape[0]
    n_devices = lax.axis_size("expert")
    experts = n_devices // SPAN
    capacity = min(tok_rows, 2 * tok_rows * SPAN // n_devices)
    routed = expert_ids[:, 0]
    one_hot = (routed[:, None] == jnp.arange(experts, dtype=jnp.int32)[None, :]).astype(jnp.int32)
    slot_rank = jnp.sum((jnp.cumsum(one_hot, axis=0) - one_hot) * one_hot, axis=1)
    flat_slot = routed * capacity + slot_rank
    placing = (
        flat_slot[None, :] == jnp.arange(experts * capacity, dtype=jnp.int32)[:, None]
    ).astype(jnp.bfloat16)
    scaled = (tokens.astype(jnp.float32) * route_scale[:, None]).astype(jnp.bfloat16)
    gate_local = gate_weight[0]
    up_local = up_weight[0]
    down_local = down_weight[0]
    full_rows = lax.all_gather(scaled, "tensor", axis=1, tiled=True)
    width = full_rows.shape[1]
    packed = jnp.dot(placing, full_rows, preferred_element_type=jnp.float32).astype(jnp.bfloat16)
    outgoing = jnp.repeat(packed.reshape(experts, capacity, width), SPAN, axis=0)
    arrived = lax.all_to_all(outgoing, "expert", split_axis=0, concat_axis=0, tiled=True)
    slot_rows = arrived.reshape(n_devices * capacity, width)
    gate_act = jnp.dot(slot_rows, gate_local, preferred_element_type=jnp.float32)
    up_act = jnp.dot(slot_rows, up_local, preferred_element_type=jnp.float32)
    hidden = (jax.nn.silu(gate_act) * up_act).astype(jnp.bfloat16)
    partial_value = jnp.dot(hidden, down_local, preferred_element_type=jnp.float32)
    width = partial_value.shape[1]
    outgoing_back = partial_value.astype(jnp.bfloat16).reshape(n_devices, capacity, width)
    returned = lax.all_to_all(outgoing_back, "expert", split_axis=0, concat_axis=0, tiled=True)
    paired = jnp.sum(returned.astype(jnp.float32).reshape(experts, SPAN, capacity, width), axis=1)
    picked = jnp.take(paired.reshape(experts * capacity, width), flat_slot, axis=0)
    summed = lax.psum_scatter(
        picked.astype(jnp.bfloat16), "tensor", scatter_dimension=1, tiled=True
    )
    return summed


def _xor_pairs(size, k):
    return [(i, i ^ k) for i in range(size)]


_ORDER = (0, 2, 1, 3)


def _slots(weight, t, width, axis, order=_ORDER):
    return jnp.concatenate(
        [lax.dynamic_slice_in_dim(weight, (t ^ k) * width, width, axis=axis) for k in order], axis=axis)


def gathered(tokens, route_scale, expert_ids, gate_weight, up_weight, down_weight):
    tok_rows, width = tokens.shape
    n_expert = lax.axis_size("expert")
    n_tensor = lax.axis_size("tensor")
    me = lax.axis_index("expert")
    t = lax.axis_index("tensor")
    scaled = (tokens.astype(jnp.float32) * route_scale[:, None]).astype(jnp.bfloat16)
    blocks = [scaled] + [
        lax.ppermute(scaled, "expert", _xor_pairs(n_expert, k)) for k in range(1, n_expert)
    ]
    routed = expert_ids[:, 0][:, None]
    gate_w = _slots(gate_weight[0], t, width, 0)
    up_w = _slots(up_weight[0], t, width, 0)
    down_keep = _slots(down_weight[0], t, width, 1, _ORDER[:2])
    down_send = _slots(down_weight[0], t, width, 1, _ORDER[2:])
    waves = [[k] for k in list(range(n_expert - 1, 1, -1)) + [1][:n_expert - 1] + [0]]
    total = None
    previous = None
    own_other = lax.ppermute(tokens, "tensor", _xor_pairs(n_tensor, 2))
    own_other = (own_other.astype(jnp.float32) * route_scale[:, None]).astype(jnp.bfloat16)
    for wave in waves:
        piece = jnp.concatenate([blocks[k] for k in wave])
        if wave == [0]:
            other = own_other
        else:
            other = lax.ppermute(piece, "tensor", _xor_pairs(n_tensor, 2))
        pair = jnp.concatenate([piece, other], axis=1)
        rows = jnp.concatenate(
            [pair, lax.ppermute(pair, "tensor", _xor_pairs(n_tensor, 1))], axis=1)
        if previous is not None:
            rows, _ = lax.optimization_barrier((rows, previous))
        gate_act = jnp.dot(rows, gate_w, preferred_element_type=jnp.float32)
        up_act = jnp.dot(rows, up_w, preferred_element_type=jnp.float32)
        hidden = (jax.nn.silu(gate_act) * up_act).astype(jnp.bfloat16)
        keep = jnp.dot(hidden, down_keep, preferred_element_type=jnp.float32).astype(jnp.bfloat16)
        send = jnp.dot(hidden, down_send, preferred_element_type=jnp.float32).astype(jnp.bfloat16)
        previous = keep
        over_c = keep.astype(jnp.float32) + lax.ppermute(
            send, "tensor", _xor_pairs(n_tensor, 1)).astype(jnp.float32)
        summed = over_c[:, :width] + lax.ppermute(
            over_c[:, width:].astype(jnp.bfloat16), "tensor", _xor_pairs(n_tensor, 2)).astype(jnp.float32)
        for i, k in enumerate(wave):
            part = summed[i * tok_rows:(i + 1) * tok_rows]
            if k:
                part = lax.ppermute(
                    part.astype(jnp.bfloat16), "expert", _xor_pairs(n_expert, k)).astype(jnp.float32)
            part = jnp.where(routed == (me ^ k) // SPAN, part, 0.0)
            total = part if total is None else total + part
    return total.astype(jnp.bfloat16)


def local(tokens, route_scale, expert_ids, gate_weight, up_weight, down_weight):
    tok_rows = tokens.shape[0]
    n_devices = lax.axis_size("expert")
    capacity = min(tok_rows, 2 * tok_rows * SPAN // n_devices)
    n_tensor = lax.axis_size("tensor")
    shaped = n_tensor == 4 and n_devices in (1, 2, 4) and tok_rows <= tokens.shape[1]
    if capacity == tok_rows and shaped:
        return gathered(tokens, route_scale, expert_ids, gate_weight, up_weight, down_weight)
    return dispatched(tokens, route_scale, expert_ids, gate_weight, up_weight, down_weight)


def solution(mesh):
    placed = (
        P(("groups", "expert"), "tensor"),
        P(("groups", "expert")),
        P(("groups", "expert"), None),
        P("expert", None, "tensor"),
        P("expert", None, "tensor"),
        P("expert", "tensor", None),
    )
    return jax.shard_map(
        local,
        mesh=mesh,
        in_specs=placed,
        out_specs=P(("groups", "expert"), "tensor"),
        check_vma=False,
    )
```

```python
import jax
import jax.numpy as jnp
from jax import lax
from jax.sharding import PartitionSpec as P

SPAN = 2


def dispatched(tokens, route_scale, expert_ids, gate_weight, up_weight, down_weight):
    tok_rows = tokens.shape[0]
    n_devices = lax.axis_size("expert")
    experts = n_devices // SPAN
    capacity = min(tok_rows, 2 * tok_rows * SPAN // n_devices)
    routed = expert_ids[:, 0]
    one_hot = (routed[:, None] == jnp.arange(experts, dtype=jnp.int32)[None, :]).astype(jnp.int32)
    slot_rank = jnp.sum((jnp.cumsum(one_hot, axis=0) - one_hot) * one_hot, axis=1)
    flat_slot = routed * capacity + slot_rank
    placing = (
        flat_slot[None, :] == jnp.arange(experts * capacity, dtype=jnp.int32)[:, None]
    ).astype(jnp.bfloat16)
    scaled = (tokens.astype(jnp.float32) * route_scale[:, None]).astype(jnp.bfloat16)
    gate_local = gate_weight[0]
    up_local = up_weight[0]
    down_local = down_weight[0]
    full_rows = lax.all_gather(scaled, "tensor", axis=1, tiled=True)
    width = full_rows.shape[1]
    packed = jnp.dot(placing, full_rows, preferred_element_type=jnp.float32).astype(jnp.bfloat16)
    outgoing = jnp.repeat(packed.reshape(experts, capacity, width), SPAN, axis=0)
    arrived = lax.all_to_all(outgoing, "expert", split_axis=0, concat_axis=0, tiled=True)
    slot_rows = arrived.reshape(n_devices * capacity, width)
    gate_act = jnp.dot(slot_rows, gate_local, preferred_element_type=jnp.float32)
    up_act = jnp.dot(slot_rows, up_local, preferred_element_type=jnp.float32)
    hidden = (jax.nn.silu(gate_act) * up_act).astype(jnp.bfloat16)
    partial_value = jnp.dot(hidden, down_local, preferred_element_type=jnp.float32)
    width = partial_value.shape[1]
    outgoing_back = partial_value.astype(jnp.bfloat16).reshape(n_devices, capacity, width)
    returned = lax.all_to_all(outgoing_back, "expert", split_axis=0, concat_axis=0, tiled=True)
    paired = jnp.sum(returned.astype(jnp.float32).reshape(experts, SPAN, capacity, width), axis=1)
    picked = jnp.take(paired.reshape(experts * capacity, width), flat_slot, axis=0)
    summed = lax.psum_scatter(
        picked.astype(jnp.bfloat16), "tensor", scatter_dimension=1, tiled=True
    )
    return summed


def _xor_pairs(size, k):
    return [(i, i ^ k) for i in range(size)]


_ORDER = (0, 2, 1, 3)


def _slots(weight, t, width, axis, order=_ORDER):
    return jnp.concatenate(
        [lax.dynamic_slice_in_dim(weight, (t ^ k) * width, width, axis=axis) for k in order], axis=axis)


def gathered(tokens, route_scale, expert_ids, gate_weight, up_weight, down_weight):
    tok_rows, width = tokens.shape
    n_expert = lax.axis_size("expert")
    n_tensor = lax.axis_size("tensor")
    me = lax.axis_index("expert")
    t = lax.axis_index("tensor")
    scaled = (tokens.astype(jnp.float32) * route_scale[:, None]).astype(jnp.bfloat16)
    blocks = [scaled] + [
        lax.ppermute(scaled, "expert", _xor_pairs(n_expert, k)) for k in range(1, n_expert)
    ]
    routed = expert_ids[:, 0][:, None]
    gate_w = _slots(gate_weight[0], t, width, 0)
    up_w = _slots(up_weight[0], t, width, 0)
    down_keep = _slots(down_weight[0], t, width, 1, _ORDER[:2])
    down_send = _slots(down_weight[0], t, width, 1, _ORDER[2:])
    waves = [[k] for k in list(range(n_expert - 1, 1, -1)) + [1][:n_expert - 1] + [0]]
    total = None
    previous = None
    for wave in waves:
        piece = jnp.concatenate([blocks[k] for k in wave])
        pair = jnp.concatenate(
            [piece, lax.ppermute(piece, "tensor", _xor_pairs(n_tensor, 2))], axis=1)
        rows = jnp.concatenate(
            [pair, lax.ppermute(pair, "tensor", _xor_pairs(n_tensor, 1))], axis=1)
        if previous is not None:
            rows, _ = lax.optimization_barrier((rows, previous))
        gate_act = jnp.dot(rows, gate_w, preferred_element_type=jnp.float32)
        up_act = jnp.dot(rows, up_w, preferred_element_type=jnp.float32)
        hidden = (jax.nn.silu(gate_act) * up_act).astype(jnp.bfloat16)
        keep = jnp.dot(hidden, down_keep, preferred_element_type=jnp.float32).astype(jnp.bfloat16)
        send = jnp.dot(hidden, down_send, preferred_element_type=jnp.float32).astype(jnp.bfloat16)
        previous = keep
        over_c = keep.astype(jnp.float32) + lax.ppermute(
            send, "tensor", _xor_pairs(n_tensor, 1)).astype(jnp.float32)
        k = wave[0]
        if k:
            over_c = lax.ppermute(
                over_c.astype(jnp.bfloat16), "expert", _xor_pairs(n_expert, k)).astype(jnp.float32)
        over_c = jnp.where(routed == (me ^ k) // SPAN, over_c, 0.0)
        total = over_c if total is None else total + over_c
    total = total[:, :width] + lax.ppermute(
        total[:, width:].astype(jnp.bfloat16), "tensor", _xor_pairs(n_tensor, 2)).astype(jnp.float32)
    return total.astype(jnp.bfloat16)


def local(tokens, route_scale, expert_ids, gate_weight, up_weight, down_weight):
    tok_rows = tokens.shape[0]
    n_devices = lax.axis_size("expert")
    capacity = min(tok_rows, 2 * tok_rows * SPAN // n_devices)
    n_tensor = lax.axis_size("tensor")
    shaped = n_tensor == 4 and n_devices in (1, 2, 4) and tok_rows <= tokens.shape[1]
    if capacity == tok_rows and shaped:
        return gathered(tokens, route_scale, expert_ids, gate_weight, up_weight, down_weight)
    return dispatched(tokens, route_scale, expert_ids, gate_weight, up_weight, down_weight)


def solution(mesh):
    placed = (
        P(("groups", "expert"), "tensor"),
        P(("groups", "expert")),
        P(("groups", "expert"), None),
        P("expert", None, "tensor"),
        P("expert", None, "tensor"),
        P("expert", "tensor", None),
    )
    return jax.shard_map(
        local,
        mesh=mesh,
        in_specs=placed,
        out_specs=P(("groups", "expert"), "tensor"),
        check_vma=False,
    )
```

```python
import jax
import jax.numpy as jnp
from jax import lax
from jax.sharding import PartitionSpec as P

SPAN = 2


def dispatched(tokens, route_scale, expert_ids, gate_weight, up_weight, down_weight):
    tok_rows = tokens.shape[0]
    n_devices = lax.axis_size("expert")
    experts = n_devices // SPAN
    capacity = min(tok_rows, 2 * tok_rows * SPAN // n_devices)
    routed = expert_ids[:, 0]
    one_hot = (routed[:, None] == jnp.arange(experts, dtype=jnp.int32)[None, :]).astype(jnp.int32)
    slot_rank = jnp.sum((jnp.cumsum(one_hot, axis=0) - one_hot) * one_hot, axis=1)
    flat_slot = routed * capacity + slot_rank
    placing = (
        flat_slot[None, :] == jnp.arange(experts * capacity, dtype=jnp.int32)[:, None]
    ).astype(jnp.bfloat16)
    scaled = (tokens.astype(jnp.float32) * route_scale[:, None]).astype(jnp.bfloat16)
    gate_local = gate_weight[0]
    up_local = up_weight[0]
    down_local = down_weight[0]
    full_rows = lax.all_gather(scaled, "tensor", axis=1, tiled=True)
    width = full_rows.shape[1]
    packed = jnp.dot(placing, full_rows, preferred_element_type=jnp.float32).astype(jnp.bfloat16)
    outgoing = jnp.repeat(packed.reshape(experts, capacity, width), SPAN, axis=0)
    arrived = lax.all_to_all(outgoing, "expert", split_axis=0, concat_axis=0, tiled=True)
    slot_rows = arrived.reshape(n_devices * capacity, width)
    gate_act = jnp.dot(slot_rows, gate_local, preferred_element_type=jnp.float32)
    up_act = jnp.dot(slot_rows, up_local, preferred_element_type=jnp.float32)
    hidden = (jax.nn.silu(gate_act) * up_act).astype(jnp.bfloat16)
    partial_value = jnp.dot(hidden, down_local, preferred_element_type=jnp.float32)
    width = partial_value.shape[1]
    outgoing_back = partial_value.astype(jnp.bfloat16).reshape(n_devices, capacity, width)
    returned = lax.all_to_all(outgoing_back, "expert", split_axis=0, concat_axis=0, tiled=True)
    paired = jnp.sum(returned.astype(jnp.float32).reshape(experts, SPAN, capacity, width), axis=1)
    picked = jnp.take(paired.reshape(experts * capacity, width), flat_slot, axis=0)
    summed = lax.psum_scatter(
        picked.astype(jnp.bfloat16), "tensor", scatter_dimension=1, tiled=True
    )
    return summed


def _xor_pairs(size, k):
    return [(i, i ^ k) for i in range(size)]


_ORDER = (0, 2, 1, 3)


def _slots(weight, t, width, axis, order=_ORDER):
    return jnp.concatenate(
        [lax.dynamic_slice_in_dim(weight, (t ^ k) * width, width, axis=axis) for k in order], axis=axis)


def gathered(tokens, route_scale, expert_ids, gate_weight, up_weight, down_weight):
    tok_rows, width = tokens.shape
    n_expert = lax.axis_size("expert")
    n_tensor = lax.axis_size("tensor")
    me = lax.axis_index("expert")
    t = lax.axis_index("tensor")
    scaled = (tokens.astype(jnp.float32) * route_scale[:, None]).astype(jnp.bfloat16)
    blocks = [scaled] + [
        lax.ppermute(scaled, "expert", _xor_pairs(n_expert, k)) for k in range(1, n_expert)
    ]
    routed = expert_ids[:, 0][:, None]
    gate_w = _slots(gate_weight[0], t, width, 0)
    up_w = _slots(up_weight[0], t, width, 0)
    down_keep = _slots(down_weight[0], t, width, 1, _ORDER[:2])
    down_send = _slots(down_weight[0], t, width, 1, _ORDER[2:])
    waves = [[k] for k in [1][:n_expert - 1] + list(range(n_expert - 1, 1, -1)) + [0]]
    total = None
    previous = None
    for wave in waves:
        piece = jnp.concatenate([blocks[k] for k in wave])
        pair = jnp.concatenate(
            [piece, lax.ppermute(piece, "tensor", _xor_pairs(n_tensor, 2))], axis=1)
        rows = jnp.concatenate(
            [pair, lax.ppermute(pair, "tensor", _xor_pairs(n_tensor, 1))], axis=1)
        if previous is not None:
            rows, _ = lax.optimization_barrier((rows, previous))
        gate_act = jnp.dot(rows, gate_w, preferred_element_type=jnp.float32)
        up_act = jnp.dot(rows, up_w, preferred_element_type=jnp.float32)
        hidden = (jax.nn.silu(gate_act) * up_act).astype(jnp.bfloat16)
        keep = jnp.dot(hidden, down_keep, preferred_element_type=jnp.float32).astype(jnp.bfloat16)
        send = jnp.dot(hidden, down_send, preferred_element_type=jnp.float32).astype(jnp.bfloat16)
        previous = keep
        over_c = keep.astype(jnp.float32) + lax.ppermute(
            send, "tensor", _xor_pairs(n_tensor, 1)).astype(jnp.float32)
        summed = over_c[:, :width] + lax.ppermute(
            over_c[:, width:].astype(jnp.bfloat16), "tensor", _xor_pairs(n_tensor, 2)).astype(jnp.float32)
        for i, k in enumerate(wave):
            part = summed[i * tok_rows:(i + 1) * tok_rows]
            if k:
                part = lax.ppermute(
                    part.astype(jnp.bfloat16), "expert", _xor_pairs(n_expert, k)).astype(jnp.float32)
            part = jnp.where(routed == (me ^ k) // SPAN, part, 0.0)
            total = part if total is None else total + part
    return total.astype(jnp.bfloat16)


def local(tokens, route_scale, expert_ids, gate_weight, up_weight, down_weight):
    tok_rows = tokens.shape[0]
    n_devices = lax.axis_size("expert")
    capacity = min(tok_rows, 2 * tok_rows * SPAN // n_devices)
    n_tensor = lax.axis_size("tensor")
    shaped = n_tensor == 4 and n_devices in (1, 2, 4) and tok_rows <= tokens.shape[1]
    if capacity == tok_rows and shaped:
        return gathered(tokens, route_scale, expert_ids, gate_weight, up_weight, down_weight)
    return dispatched(tokens, route_scale, expert_ids, gate_weight, up_weight, down_weight)


def solution(mesh):
    placed = (
        P(("groups", "expert"), "tensor"),
        P(("groups", "expert")),
        P(("groups", "expert"), None),
        P("expert", None, "tensor"),
        P("expert", None, "tensor"),
        P("expert", "tensor", None),
    )
    return jax.shard_map(
        local,
        mesh=mesh,
        in_specs=placed,
        out_specs=P(("groups", "expert"), "tensor"),
        check_vma=False,
    )
```

```python
import jax
import jax.numpy as jnp
from jax import lax
from jax.sharding import PartitionSpec as P

SPAN = 2


def dispatched(tokens, route_scale, expert_ids, gate_weight, up_weight, down_weight):
    tok_rows = tokens.shape[0]
    n_devices = lax.axis_size("expert")
    experts = n_devices // SPAN
    capacity = min(tok_rows, 2 * tok_rows * SPAN // n_devices)
    routed = expert_ids[:, 0]
    one_hot = (routed[:, None] == jnp.arange(experts, dtype=jnp.int32)[None, :]).astype(jnp.int32)
    slot_rank = jnp.sum((jnp.cumsum(one_hot, axis=0) - one_hot) * one_hot, axis=1)
    flat_slot = routed * capacity + slot_rank
    placing = (
        flat_slot[None, :] == jnp.arange(experts * capacity, dtype=jnp.int32)[:, None]
    ).astype(jnp.bfloat16)
    scaled = (tokens.astype(jnp.float32) * route_scale[:, None]).astype(jnp.bfloat16)
    gate_local = gate_weight[0]
    up_local = up_weight[0]
    down_local = down_weight[0]
    full_rows = lax.all_gather(scaled, "tensor", axis=1, tiled=True)
    width = full_rows.shape[1]
    packed = jnp.dot(placing, full_rows, preferred_element_type=jnp.float32).astype(jnp.bfloat16)
    outgoing = jnp.repeat(packed.reshape(experts, capacity, width), SPAN, axis=0)
    arrived = lax.all_to_all(outgoing, "expert", split_axis=0, concat_axis=0, tiled=True)
    slot_rows = arrived.reshape(n_devices * capacity, width)
    gate_act = jnp.dot(slot_rows, gate_local, preferred_element_type=jnp.float32)
    up_act = jnp.dot(slot_rows, up_local, preferred_element_type=jnp.float32)
    hidden = (jax.nn.silu(gate_act) * up_act).astype(jnp.bfloat16)
    partial_value = jnp.dot(hidden, down_local, preferred_element_type=jnp.float32)
    width = partial_value.shape[1]
    outgoing_back = partial_value.astype(jnp.bfloat16).reshape(n_devices, capacity, width)
    returned = lax.all_to_all(outgoing_back, "expert", split_axis=0, concat_axis=0, tiled=True)
    paired = jnp.sum(returned.astype(jnp.float32).reshape(experts, SPAN, capacity, width), axis=1)
    picked = jnp.take(paired.reshape(experts * capacity, width), flat_slot, axis=0)
    summed = lax.psum_scatter(
        picked.astype(jnp.bfloat16), "tensor", scatter_dimension=1, tiled=True
    )
    return summed


def _xor_pairs(size, k):
    return [(i, i ^ k) for i in range(size)]


_ORDER = (0, 2, 1, 3)


def _slots(weight, t, width, axis, order=_ORDER):
    return jnp.concatenate(
        [lax.dynamic_slice_in_dim(weight, (t ^ k) * width, width, axis=axis) for k in order], axis=axis)


def gathered(tokens, route_scale, expert_ids, gate_weight, up_weight, down_weight):
    tok_rows, width = tokens.shape
    n_expert = lax.axis_size("expert")
    n_tensor = lax.axis_size("tensor")
    me = lax.axis_index("expert")
    t = lax.axis_index("tensor")
    scaled = (tokens.astype(jnp.float32) * route_scale[:, None]).astype(jnp.bfloat16)
    blocks = [scaled] + [
        lax.ppermute(scaled, "expert", _xor_pairs(n_expert, k)) for k in range(1, n_expert)
    ]
    routed = expert_ids[:, 0][:, None]
    gate_w = _slots(gate_weight[0], t, width, 0)
    up_w = _slots(up_weight[0], t, width, 0)
    down_keep = _slots(down_weight[0], t, width, 1, _ORDER[:2])
    down_send = _slots(down_weight[0], t, width, 1, _ORDER[2:])
    half = tok_rows // 2 if tok_rows % 32 == 0 else tok_rows
    waves = [(k, 0, tok_rows) for k in list(range(n_expert - 1, 1, -1)) + [1][:n_expert - 1]]
    waves += [(0, lo, min(lo + half, tok_rows)) for lo in range(0, tok_rows, half)]
    total = None
    previous = None
    parts = [None] * len(waves)
    for index, (k, lo, hi) in enumerate(waves):
        piece = blocks[k][lo:hi]
        pair = jnp.concatenate(
            [piece, lax.ppermute(piece, "tensor", _xor_pairs(n_tensor, 2))], axis=1)
        rows = jnp.concatenate(
            [pair, lax.ppermute(pair, "tensor", _xor_pairs(n_tensor, 1))], axis=1)
        if previous is not None:
            rows, _ = lax.optimization_barrier((rows, previous))
        gate_act = jnp.dot(rows, gate_w, preferred_element_type=jnp.float32)
        up_act = jnp.dot(rows, up_w, preferred_element_type=jnp.float32)
        hidden = (jax.nn.silu(gate_act) * up_act).astype(jnp.bfloat16)
        keep = jnp.dot(hidden, down_keep, preferred_element_type=jnp.float32).astype(jnp.bfloat16)
        send = jnp.dot(hidden, down_send, preferred_element_type=jnp.float32).astype(jnp.bfloat16)
        previous = keep
        over_c = keep.astype(jnp.float32) + lax.ppermute(
            send, "tensor", _xor_pairs(n_tensor, 1)).astype(jnp.float32)
        summed = over_c[:, :width] + lax.ppermute(
            over_c[:, width:].astype(jnp.bfloat16), "tensor", _xor_pairs(n_tensor, 2)).astype(jnp.float32)
        if k:
            summed = lax.ppermute(
                summed.astype(jnp.bfloat16), "expert", _xor_pairs(n_expert, k)).astype(jnp.float32)
        summed = jnp.where(routed[lo:hi] == (me ^ k) // SPAN, summed, 0.0)
        parts[index] = summed
    full = [p for (k, lo, hi), p in zip(waves, parts) if hi - lo == tok_rows]
    own = jnp.concatenate([p for (k, lo, hi), p in zip(waves, parts) if hi - lo < tok_rows] or [0.0 * full[0]])
    total = own
    for p in full:
        total = total + p
    return total.astype(jnp.bfloat16)


def local(tokens, route_scale, expert_ids, gate_weight, up_weight, down_weight):
    tok_rows = tokens.shape[0]
    n_devices = lax.axis_size("expert")
    capacity = min(tok_rows, 2 * tok_rows * SPAN // n_devices)
    n_tensor = lax.axis_size("tensor")
    shaped = n_tensor == 4 and n_devices in (1, 2, 4) and tok_rows <= tokens.shape[1]
    if capacity == tok_rows and shaped:
        return gathered(tokens, route_scale, expert_ids, gate_weight, up_weight, down_weight)
    return dispatched(tokens, route_scale, expert_ids, gate_weight, up_weight, down_weight)


def solution(mesh):
    placed = (
        P(("groups", "expert"), "tensor"),
        P(("groups", "expert")),
        P(("groups", "expert"), None),
        P("expert", None, "tensor"),
        P("expert", None, "tensor"),
        P("expert", "tensor", None),
    )
    return jax.shard_map(
        local,
        mesh=mesh,
        in_specs=placed,
        out_specs=P(("groups", "expert"), "tensor"),
        check_vma=False,
    )
```

```python
import jax
import jax.numpy as jnp
from jax import lax
from jax.sharding import PartitionSpec as P

SPAN = 2


def dispatched(tokens, route_scale, expert_ids, gate_weight, up_weight, down_weight):
    tok_rows = tokens.shape[0]
    n_devices = lax.axis_size("expert")
    experts = n_devices // SPAN
    capacity = min(tok_rows, 2 * tok_rows * SPAN // n_devices)
    routed = expert_ids[:, 0]
    one_hot = (routed[:, None] == jnp.arange(experts, dtype=jnp.int32)[None, :]).astype(jnp.int32)
    slot_rank = jnp.sum((jnp.cumsum(one_hot, axis=0) - one_hot) * one_hot, axis=1)
    flat_slot = routed * capacity + slot_rank
    placing = (
        flat_slot[None, :] == jnp.arange(experts * capacity, dtype=jnp.int32)[:, None]
    ).astype(jnp.bfloat16)
    scaled = (tokens.astype(jnp.float32) * route_scale[:, None]).astype(jnp.bfloat16)
    gate_local = gate_weight[0]
    up_local = up_weight[0]
    down_local = down_weight[0]
    full_rows = lax.all_gather(scaled, "tensor", axis=1, tiled=True)
    width = full_rows.shape[1]
    packed = jnp.dot(placing, full_rows, preferred_element_type=jnp.float32).astype(jnp.bfloat16)
    outgoing = jnp.repeat(packed.reshape(experts, capacity, width), SPAN, axis=0)
    arrived = lax.all_to_all(outgoing, "expert", split_axis=0, concat_axis=0, tiled=True)
    slot_rows = arrived.reshape(n_devices * capacity, width)
    gate_act = jnp.dot(slot_rows, gate_local, preferred_element_type=jnp.float32)
    up_act = jnp.dot(slot_rows, up_local, preferred_element_type=jnp.float32)
    hidden = (jax.nn.silu(gate_act) * up_act).astype(jnp.bfloat16)
    partial_value = jnp.dot(hidden, down_local, preferred_element_type=jnp.float32)
    width = partial_value.shape[1]
    outgoing_back = partial_value.astype(jnp.bfloat16).reshape(n_devices, capacity, width)
    returned = lax.all_to_all(outgoing_back, "expert", split_axis=0, concat_axis=0, tiled=True)
    paired = jnp.sum(returned.astype(jnp.float32).reshape(experts, SPAN, capacity, width), axis=1)
    picked = jnp.take(paired.reshape(experts * capacity, width), flat_slot, axis=0)
    summed = lax.psum_scatter(
        picked.astype(jnp.bfloat16), "tensor", scatter_dimension=1, tiled=True
    )
    return summed


def _xor_pairs(size, k):
    return [(i, i ^ k) for i in range(size)]


_ORDER = (0, 2, 1, 3)


def _slots(weight, t, width, axis, order=_ORDER):
    return jnp.concatenate(
        [lax.dynamic_slice_in_dim(weight, (t ^ k) * width, width, axis=axis) for k in order], axis=axis)


def gathered(tokens, route_scale, expert_ids, gate_weight, up_weight, down_weight):
    tok_rows, width = tokens.shape
    n_expert = lax.axis_size("expert")
    n_tensor = lax.axis_size("tensor")
    me = lax.axis_index("expert")
    t = lax.axis_index("tensor")
    scaled = (tokens.astype(jnp.float32) * route_scale[:, None]).astype(jnp.bfloat16)
    blocks = [scaled] + [
        lax.ppermute(scaled, "expert", _xor_pairs(n_expert, k)) for k in range(1, n_expert)
    ]
    routed = expert_ids[:, 0][:, None]
    gate_w = _slots(gate_weight[0], t, width, 0)
    up_w = _slots(up_weight[0], t, width, 0)
    down_keep = _slots(down_weight[0], t, width, 1, _ORDER[:2])
    down_send = _slots(down_weight[0], t, width, 1, _ORDER[2:])
    waves = [[k] for k in list(range(n_expert - 1, 1, -1)) + [1][:n_expert - 1] + [0]]
    total = None
    previous = None
    for wave in waves:
        piece = jnp.concatenate([blocks[k] for k in wave])
        pair = jnp.concatenate(
            [piece, lax.ppermute(piece, "tensor", _xor_pairs(n_tensor, 2))], axis=1)
        rows = jnp.concatenate(
            [pair, lax.ppermute(pair, "tensor", _xor_pairs(n_tensor, 1))], axis=1)
        if previous is not None:
            rows, _ = lax.optimization_barrier((rows, previous))
        gate_act = jnp.dot(rows, gate_w, preferred_element_type=jnp.float32)
        up_act = jnp.dot(rows, up_w, preferred_element_type=jnp.float32)
        hidden = (jax.nn.silu(gate_act) * up_act).astype(jnp.bfloat16)
        keep = jnp.dot(hidden, down_keep, preferred_element_type=jnp.float32).astype(jnp.bfloat16)
        send = jnp.dot(hidden, down_send, preferred_element_type=jnp.float32).astype(jnp.bfloat16)
        previous = hidden
        over_c = keep.astype(jnp.float32) + lax.ppermute(
            send, "tensor", _xor_pairs(n_tensor, 1)).astype(jnp.float32)
        summed = over_c[:, :width] + lax.ppermute(
            over_c[:, width:].astype(jnp.bfloat16), "tensor", _xor_pairs(n_tensor, 2)).astype(jnp.float32)
        for i, k in enumerate(wave):
            part = summed[i * tok_rows:(i + 1) * tok_rows]
            if k:
                part = lax.ppermute(
                    part.astype(jnp.bfloat16), "expert", _xor_pairs(n_expert, k)).astype(jnp.float32)
            part = jnp.where(routed == (me ^ k) // SPAN, part, 0.0)
            total = part if total is None else total + part
    return total.astype(jnp.bfloat16)


def local(tokens, route_scale, expert_ids, gate_weight, up_weight, down_weight):
    tok_rows = tokens.shape[0]
    n_devices = lax.axis_size("expert")
    capacity = min(tok_rows, 2 * tok_rows * SPAN // n_devices)
    n_tensor = lax.axis_size("tensor")
    shaped = n_tensor == 4 and n_devices in (1, 2, 4) and tok_rows <= tokens.shape[1]
    if capacity == tok_rows and shaped:
        return gathered(tokens, route_scale, expert_ids, gate_weight, up_weight, down_weight)
    return dispatched(tokens, route_scale, expert_ids, gate_weight, up_weight, down_weight)


def solution(mesh):
    placed = (
        P(("groups", "expert"), "tensor"),
        P(("groups", "expert")),
        P(("groups", "expert"), None),
        P("expert", None, "tensor"),
        P("expert", None, "tensor"),
        P("expert", "tensor", None),
    )
    return jax.shard_map(
        local,
        mesh=mesh,
        in_specs=placed,
        out_specs=P(("groups", "expert"), "tensor"),
        check_vma=False,
    )
```

```python
import jax
import jax.numpy as jnp
from jax import lax
from jax.sharding import PartitionSpec as P

SPAN = 2


def dispatched(tokens, route_scale, expert_ids, gate_weight, up_weight, down_weight):
    tok_rows = tokens.shape[0]
    n_devices = lax.axis_size("expert")
    experts = n_devices // SPAN
    capacity = min(tok_rows, 2 * tok_rows * SPAN // n_devices)
    routed = expert_ids[:, 0]
    one_hot = (routed[:, None] == jnp.arange(experts, dtype=jnp.int32)[None, :]).astype(jnp.int32)
    slot_rank = jnp.sum((jnp.cumsum(one_hot, axis=0) - one_hot) * one_hot, axis=1)
    flat_slot = routed * capacity + slot_rank
    placing = (
        flat_slot[None, :] == jnp.arange(experts * capacity, dtype=jnp.int32)[:, None]
    ).astype(jnp.bfloat16)
    scaled = (tokens.astype(jnp.float32) * route_scale[:, None]).astype(jnp.bfloat16)
    gate_local = gate_weight[0]
    up_local = up_weight[0]
    down_local = down_weight[0]
    full_rows = lax.all_gather(scaled, "tensor", axis=1, tiled=True)
    width = full_rows.shape[1]
    packed = jnp.dot(placing, full_rows, preferred_element_type=jnp.float32).astype(jnp.bfloat16)
    outgoing = jnp.repeat(packed.reshape(experts, capacity, width), SPAN, axis=0)
    arrived = lax.all_to_all(outgoing, "expert", split_axis=0, concat_axis=0, tiled=True)
    slot_rows = arrived.reshape(n_devices * capacity, width)
    gate_act = jnp.dot(slot_rows, gate_local, preferred_element_type=jnp.float32)
    up_act = jnp.dot(slot_rows, up_local, preferred_element_type=jnp.float32)
    hidden = (jax.nn.silu(gate_act) * up_act).astype(jnp.bfloat16)
    partial_value = jnp.dot(hidden, down_local, preferred_element_type=jnp.float32)
    width = partial_value.shape[1]
    outgoing_back = partial_value.astype(jnp.bfloat16).reshape(n_devices, capacity, width)
    returned = lax.all_to_all(outgoing_back, "expert", split_axis=0, concat_axis=0, tiled=True)
    paired = jnp.sum(returned.astype(jnp.float32).reshape(experts, SPAN, capacity, width), axis=1)
    picked = jnp.take(paired.reshape(experts * capacity, width), flat_slot, axis=0)
    summed = lax.psum_scatter(
        picked.astype(jnp.bfloat16), "tensor", scatter_dimension=1, tiled=True
    )
    return summed


def _xor_pairs(size, k):
    return [(i, i ^ k) for i in range(size)]


_ORDER = (0, 2, 1, 3)


def _slots(weight, t, width, axis, order=_ORDER):
    return jnp.concatenate(
        [lax.dynamic_slice_in_dim(weight, (t ^ k) * width, width, axis=axis) for k in order], axis=axis)


def gathered(tokens, route_scale, expert_ids, gate_weight, up_weight, down_weight):
    tok_rows, width = tokens.shape
    n_expert = lax.axis_size("expert")
    n_tensor = lax.axis_size("tensor")
    me = lax.axis_index("expert")
    t = lax.axis_index("tensor")
    scaled = (tokens.astype(jnp.float32) * route_scale[:, None]).astype(jnp.bfloat16)
    blocks = [scaled] + [
        lax.ppermute(scaled, "expert", _xor_pairs(n_expert, k)) for k in range(1, n_expert)
    ]
    routed = expert_ids[:, 0][:, None]
    gate_w = _slots(gate_weight[0], t, width, 0)
    up_w = _slots(up_weight[0], t, width, 0)
    down_keep = _slots(down_weight[0], t, width, 1, _ORDER[:2])
    down_send = _slots(down_weight[0], t, width, 1, _ORDER[2:])
    waves = [[k] for k in ([2, 1, 3] if n_expert == 4 else list(range(n_expert - 1, 0, -1))) + [0]]
    total = None
    previous = None
    for wave in waves:
        piece = jnp.concatenate([blocks[k] for k in wave])
        pair = jnp.concatenate(
            [piece, lax.ppermute(piece, "tensor", _xor_pairs(n_tensor, 2))], axis=1)
        rows = jnp.concatenate(
            [pair, lax.ppermute(pair, "tensor", _xor_pairs(n_tensor, 1))], axis=1)
        if previous is not None:
            rows, _ = lax.optimization_barrier((rows, previous))
        gate_act = jnp.dot(rows, gate_w, preferred_element_type=jnp.float32)
        up_act = jnp.dot(rows, up_w, preferred_element_type=jnp.float32)
        hidden = (jax.nn.silu(gate_act) * up_act).astype(jnp.bfloat16)
        keep = jnp.dot(hidden, down_keep, preferred_element_type=jnp.float32).astype(jnp.bfloat16)
        send = jnp.dot(hidden, down_send, preferred_element_type=jnp.float32).astype(jnp.bfloat16)
        previous = keep
        over_c = keep.astype(jnp.float32) + lax.ppermute(
            send, "tensor", _xor_pairs(n_tensor, 1)).astype(jnp.float32)
        summed = over_c[:, :width] + lax.ppermute(
            over_c[:, width:].astype(jnp.bfloat16), "tensor", _xor_pairs(n_tensor, 2)).astype(jnp.float32)
        for i, k in enumerate(wave):
            part = summed[i * tok_rows:(i + 1) * tok_rows]
            if k:
                part = lax.ppermute(
                    part.astype(jnp.bfloat16), "expert", _xor_pairs(n_expert, k)).astype(jnp.float32)
            part = jnp.where(routed == (me ^ k) // SPAN, part, 0.0)
            total = part if total is None else total + part
    return total.astype(jnp.bfloat16)


def local(tokens, route_scale, expert_ids, gate_weight, up_weight, down_weight):
    tok_rows = tokens.shape[0]
    n_devices = lax.axis_size("expert")
    capacity = min(tok_rows, 2 * tok_rows * SPAN // n_devices)
    n_tensor = lax.axis_size("tensor")
    shaped = n_tensor == 4 and n_devices in (1, 2, 4) and tok_rows <= tokens.shape[1]
    if capacity == tok_rows and shaped:
        return gathered(tokens, route_scale, expert_ids, gate_weight, up_weight, down_weight)
    return dispatched(tokens, route_scale, expert_ids, gate_weight, up_weight, down_weight)


def solution(mesh):
    placed = (
        P(("groups", "expert"), "tensor"),
        P(("groups", "expert")),
        P(("groups", "expert"), None),
        P("expert", None, "tensor"),
        P("expert", None, "tensor"),
        P("expert", "tensor", None),
    )
    return jax.shard_map(
        local,
        mesh=mesh,
        in_specs=placed,
        out_specs=P(("groups", "expert"), "tensor"),
        check_vma=False,
    )
```
